32 devices in a mesh: exp: 4 (over z), row: 4 (over y, core), col: 2 (over x).
Axes of the slice: x: 2, y: 2, z: 4, core: 2. Of those that a mesh axis runs over, the one named last changes fastest.
Arguments:
- exposures: float32 [64, 128, 1024], P('exp', 'row', 'col'), may hold values from -6 to 6
- bad_pixels: int32 [64, 128, 1024], P('exp', 'row', 'col'), may hold values 0 or 1
- offsets: int32 [64, 2], P('exp'), may hold values from -8 to 8, as said below
- warp_index: int32 [64, 2], P('exp'), may hold values from 0 to 15
- blur_index: int32 [64], P('exp'), may hold values from 0 to 7
Outputs:
- residual: float32 [64, 128, 1024], P('exp', 'row', 'col')
- median_sky: float32 [128, 1024], P('row', 'col')
The draws below stay inside these ranges and needn't reach their ends.
Inputs may be any that keep to these rules, and one draw needn't show every extreme that they name: `offsets`: in each component some exposure has the offset -8 and some has 8.
All inputs are finite; a program needn't handle non-finite values. No bound on the sum of `bad_pixels` on one device may be relied on, other than what follows from the above.
Results may differ from the reference program's by a relative error of at most 0.0003.
Values sent between devices are 32-bit elements; how exact they have to be, the bound alone decides.
No kernel may reach another device: no remote copies, remote signals or barrier semaphores. Data moves between devices by JAX's collectives and lax.ppermute only.
A program may use at most 64 MiB of HBM per device.

```python
import jax
import jax.numpy as jnp
from jax import lax

SHIFT_MAX = 8
NFRAC = 16
NPSF = 8
PSF_RADIUS = 4
PASSES = 16
HALO = 11
EXPOSURES = 64
NY = 128
NX = 1024


def shifts_for(key):
    shift_key, shuffle_key = jax.random.split(jax.random.fold_in(key, 7))
    drawn = jax.random.randint(shift_key, (EXPOSURES, 2), -SHIFT_MAX, SHIFT_MAX + 1)
    shuffle = jax.random.permutation(shuffle_key, EXPOSURES)
    drawn = drawn.at[shuffle[0]].set(jnp.array([SHIFT_MAX, -SHIFT_MAX], dtype=jnp.int32))
    drawn = drawn.at[shuffle[1]].set(jnp.array([-SHIFT_MAX, SHIFT_MAX], dtype=jnp.int32))
    return drawn.astype(jnp.int32)


def draw_offsets(key, part):
    return shifts_for(key)


def draw_exposures(key, part):
    shifts = shifts_for(key)
    sky_key, noise_key = jax.random.split(jax.random.fold_in(key, 23))
    backdrop = jnp.clip(jax.random.normal(sky_key, (NY + 2 * SHIFT_MAX, NX + 2 * SHIFT_MAX), jnp.float32), -4.0, 4.0)
    jitter = 0.5 * jnp.clip(jax.random.normal(noise_key, (EXPOSURES, NY, NX), jnp.float32), -4.0, 4.0)

    def place(shift_pair):
        return lax.dynamic_slice(backdrop, ((SHIFT_MAX - shift_pair[0]).astype(jnp.int32), (SHIFT_MAX - shift_pair[1]).astype(jnp.int32)), (NY, NX))
    aligned = jax.vmap(place)(shifts)
    return (aligned + jitter).astype(jnp.float32)


def place_ends(values, key, least, largest):
    longest = values.shape.index(max(values.shape))
    spots = []
    for shift in (0, 1):
        where = [jax.random.randint(jax.random.fold_in(key, axis), (), 0, length) for axis, length in enumerate(values.shape)]
        where[longest] = (where[longest] + shift) % values.shape[longest]
        spots.append(tuple(where))
    return values.at[spots[0]].set(least).at[spots[1]].set(largest)


def setup_inputs(seed: int = 0) -> dict:
    splits = jax.random.split(jax.random.key(seed), 6)
    exposures = draw_exposures(jax.random.fold_in(splits[5], 71), 0)
    bad_pixels = place_ends((jax.random.randint(splits[1], (EXPOSURES, NY, NX), 0, 10) < 1).astype(jnp.int32), jax.random.fold_in(splits[1], 1), 0, 1)
    offsets = draw_offsets(jax.random.fold_in(splits[5], 71), 0)
    warp_index = place_ends(jax.random.randint(splits[3], (EXPOSURES, 2), 0, NFRAC), jax.random.fold_in(splits[3], 1), 0, NFRAC - 1).astype(jnp.int32)
    blur_index = place_ends(jax.random.randint(splits[4], (EXPOSURES,), 0, NPSF), jax.random.fold_in(splits[4], 1), 0, NPSF - 1).astype(jnp.int32)
    return dict(exposures=exposures, bad_pixels=bad_pixels, offsets=offsets, warp_index=warp_index, blur_index=blur_index)


sentinel = 1.0e6
half_sentinel = 5.0e5
pivot_span = 16.0


def lanczos_table():
    fraction = jnp.arange(NFRAC, dtype=jnp.float32) / NFRAC
    offset_grid = jnp.arange(-2, 4, dtype=jnp.float32)
    spread = offset_grid[None, :] - fraction[:, None]
    kernel = jnp.sinc(spread) * jnp.sinc(spread / 3.0)
    return kernel / jnp.sum(kernel, axis=1, keepdims=True)


def blur_table():
    offset_grid = jnp.arange(-PSF_RADIUS, PSF_RADIUS + 1, dtype=jnp.float32)
    widths = 0.7 + 0.2 * jnp.arange(NPSF, dtype=jnp.float32)
    kernel = jnp.exp(-0.5 * (offset_grid[None, :] / widths[:, None]) ** 2)
    return kernel / jnp.sum(kernel, axis=1, keepdims=True)


def warp_single(inputs):
    picture, shifts, kernel_pair = inputs
    padded = jnp.pad(picture, HALO)
    anchor_zero = jnp.zeros((), jnp.int32)
    across = jnp.zeros((NY, NX + 2 * HALO), jnp.float32)
    for tap_no in range(6):
        anchor = (HALO + shifts[0] + tap_no - 2).astype(jnp.int32)
        across = across + kernel_pair[0, tap_no] * lax.dynamic_slice(padded, (anchor, anchor_zero), (NY, NX + 2 * HALO))
    warped = jnp.zeros((NY, NX), jnp.float32)
    for tap_no in range(6):
        anchor = (HALO + shifts[1] + tap_no - 2).astype(jnp.int32)
        warped = warped + kernel_pair[1, tap_no] * lax.dynamic_slice(across, (anchor_zero, anchor), (NY, NX))
    return warped


def reference(exposures, bad_pixels, offsets, warp_index, blur_index):
    kernels = lanczos_table()[warp_index]
    warped = lax.map(warp_single, (exposures, offsets, kernels))
    flagged = jnp.where(bad_pixels == 1, sentinel, warped)
    valid_count = jnp.sum(flagged < half_sentinel, axis=0, dtype=jnp.float32)

    def one_pass(sweep_no, bounds):
        lower_edge, upper_edge = bounds
        middle = 0.5 * (lower_edge + upper_edge)
        counted = jnp.sum(flagged <= middle[None], axis=0, dtype=jnp.float32)
        enough = 2.0 * counted >= valid_count
        return (jnp.where(enough, lower_edge, middle), jnp.where(enough, middle, upper_edge))

    initial = (jnp.full((NY, NX), -pivot_span, jnp.float32), jnp.full((NY, NX), pivot_span, jnp.float32))
    lower_edge = lax.fori_loop(0, PASSES, one_pass, initial)[0]
    median_sky = jnp.min(jnp.where(flagged > lower_edge[None], flagged, sentinel), axis=0)

    bordered = jnp.pad(median_sky, PSF_RADIUS)
    blur = blur_table()

    def smooth_kernel(weights):
        across = jnp.zeros((NY, NX + 2 * PSF_RADIUS), jnp.float32)
        for tap_no in range(2 * PSF_RADIUS + 1):
            across = across + weights[tap_no] * bordered[tap_no:tap_no + NY, :]
        result = jnp.zeros((NY, NX), jnp.float32)
        for tap_no in range(2 * PSF_RADIUS + 1):
            result = result + weights[tap_no] * across[:, tap_no:tap_no + NX]
        return result

    smoothed = lax.map(smooth_kernel, blur)
    sky_model = smoothed[blur_index]
    residual = jnp.where(bad_pixels == 1, 0.0, warped - sky_model)
    return residual, median_sky
```

```python
import jax
import jax.numpy as jnp
from jax import lax
from jax.sharding import PartitionSpec as P

NFRAC = 16
NPSF = 8
PSF_RADIUS = 4
PASSES = 16
HALO = 11


sentinel = 1000000.0
half_sentinel = 500000.0
pivot_span = 16.0


def _grid_pairs(nrow, ncol, dr, dc, flat):
    pairs = []
    for r in range(nrow):
        for c in range(ncol):
            tr, tc = r - dr, c - dc
            if 0 <= tr < nrow and 0 <= tc < ncol:
                pairs.append((flat(r, c), flat(tr, tc)))
    return pairs


def extended(block, row_dim, col_dim, width):
    nrow = lax.axis_size("row")
    ncol = lax.axis_size("col")
    rows = block.shape[row_dim]
    cols = block.shape[col_dim]

    def piece(dr, dc):
        part = block
        if dr == -1:
            part = lax.slice_in_dim(part, rows - width, rows, axis=row_dim)
        elif dr == 1:
            part = lax.slice_in_dim(part, 0, width, axis=row_dim)
        if dc == -1:
            part = lax.slice_in_dim(part, cols - width, cols, axis=col_dim)
        elif dc == 1:
            part = lax.slice_in_dim(part, 0, width, axis=col_dim)
        if dr == 0:
            pairs = _grid_pairs(1, ncol, 0, dc, lambda r, c: c)
            return lax.ppermute(part, "col", pairs)
        if dc == 0:
            pairs = _grid_pairs(nrow, 1, dr, 0, lambda r, c: r)
            return lax.ppermute(part, "row", pairs)
        pairs = _grid_pairs(nrow, ncol, dr, dc, lambda r, c: r * ncol + c)
        return lax.ppermute(part, ("row", "col"), pairs)

    bands = []
    for dr in (-1, 0, 1):
        line = [block if (dr, dc) == (0, 0) else piece(dr, dc) for dc in (-1, 0, 1)]
        bands.append(jnp.concatenate(line, axis=col_dim))
    return jnp.concatenate(bands, axis=row_dim)


def lanczos_table():
    fraction = jnp.arange(NFRAC, dtype=jnp.float32) / NFRAC
    offset_grid = jnp.arange(-2, 4, dtype=jnp.float32)
    spread = offset_grid[None, :] - fraction[:, None]
    kernel = jnp.sinc(spread) * jnp.sinc(spread / 3.0)
    return kernel / jnp.sum(kernel, axis=1, keepdims=True)


def blur_table():
    offset_grid = jnp.arange(-PSF_RADIUS, PSF_RADIUS + 1, dtype=jnp.float32)
    widths = 0.7 + 0.2 * jnp.arange(NPSF, dtype=jnp.float32)
    kernel = jnp.exp(-0.5 * (offset_grid[None, :] / widths[:, None]) ** 2)
    return kernel / jnp.sum(kernel, axis=1, keepdims=True)


def lookup(indices, entries, kernel_table):
    chooser = (indices[:, None] == lax.broadcasted_iota(jnp.int32, (1, entries), 1)).astype(
        jnp.float32
    )
    return jnp.dot(chooser, kernel_table, precision=lax.Precision.HIGHEST)


def placed_taps(weights, shifts):
    reach = 2 * HALO + 1
    positions = lax.broadcasted_iota(jnp.int32, (1, 1, reach), 2)
    tap_slot = HALO + shifts[:, None, None] + lax.broadcasted_iota(jnp.int32, (1, 6, 1), 1) - 2
    spread = (tap_slot == positions).astype(jnp.float32)
    return jnp.sum(weights[:, :, None] * spread, axis=1)


def resample_axis(stack, coefficients, out_len, which_axis):
    out_shape = list(stack.shape)
    out_shape[which_axis] = out_len
    total = jnp.zeros(tuple(out_shape), jnp.float32)
    for position in range(2 * HALO + 1):
        window = lax.slice_in_dim(stack, position, position + out_len, 1, which_axis)
        total = total + coefficients[:, position, None, None] * window
    return total


def bisect_lower(valid_count, count_below):

    def one_pass(sweep_no, bounds):
        lower_edge, upper_edge = bounds
        middle = 0.5 * (lower_edge + upper_edge)
        enough = 2.0 * count_below(middle) >= valid_count
        return (jnp.where(enough, lower_edge, middle), jnp.where(enough, middle, upper_edge))

    initial = (
        jnp.full(valid_count.shape, -pivot_span, jnp.float32),
        jnp.full(valid_count.shape, pivot_span, jnp.float32),
    )
    return lax.fori_loop(0, PASSES, one_pass, initial)[0]


def stack_median(pixel_stack):
    valid_count = jnp.sum(pixel_stack < half_sentinel, axis=0, dtype=jnp.float32)

    def count_below(middle):
        return jnp.sum(pixel_stack <= middle[None], axis=0, dtype=jnp.float32)

    lower_edge = bisect_lower(valid_count, count_below)
    return jnp.min(jnp.where(pixel_stack > lower_edge[None], pixel_stack, sentinel), axis=0)


def body(exposures, bad_pixels, offsets, warp_index, blur_index):
    group_size, row_count, col_count = exposures.shape
    kernel_table = lanczos_table()
    coef_down = placed_taps(lookup(warp_index[:, 0], NFRAC, kernel_table), offsets[:, 0])
    coef_across = placed_taps(lookup(warp_index[:, 1], NFRAC, kernel_table), offsets[:, 1])
    padded = extended(exposures, 1, 2, HALO)
    across = resample_axis(padded, coef_down, row_count, 1)
    warped = resample_axis(across, coef_across, col_count, 2)
    flagged = jnp.where(bad_pixels == 1, sentinel, warped)
    band = stack_median(lax.all_to_all(flagged, "exp", split_axis=1, concat_axis=0, tiled=True))
    groups = lax.axis_size("exp")
    median_sky = lax.all_to_all(
        jnp.tile(band, (groups, 1)), "exp", split_axis=0, concat_axis=0, tiled=True
    )
    bordered = extended(median_sky, 0, 1, PSF_RADIUS)
    blur = blur_table()
    taps = 2 * PSF_RADIUS + 1
    blurred_rows = jnp.zeros((NPSF, row_count, col_count + 2 * PSF_RADIUS), jnp.float32)
    for tap_no in range(taps):
        blurred_rows = (
            blurred_rows
            + blur[:, tap_no, None, None] * bordered[None, tap_no : tap_no + row_count, :]
        )
    smoothed = jnp.zeros((NPSF, row_count, col_count), jnp.float32)
    for tap_no in range(taps):
        smoothed = (
            smoothed + blur[:, tap_no, None, None] * blurred_rows[:, :, tap_no : tap_no + col_count]
        )
    chooser = (blur_index[:, None] == lax.broadcasted_iota(jnp.int32, (1, NPSF), 1)).astype(
        jnp.float32
    )
    sky_model = jnp.zeros((group_size, row_count, col_count), jnp.float32)
    for kernel_no in range(NPSF):
        sky_model = sky_model + chooser[:, kernel_no, None, None] * smoothed[kernel_no][None]
    residual = jnp.where(bad_pixels == 1, 0.0, warped - sky_model)
    return (residual, median_sky)


def solution(mesh):
    return jax.shard_map(
        body,
        mesh=mesh,
        in_specs=(
            P("exp", "row", "col"),
            P("exp", "row", "col"),
            P("exp", None),
            P("exp", None),
            P("exp"),
        ),
        out_specs=(P("exp", "row", "col"), P("row", "col")),
        check_vma=False,
    )
```

```python
import jax
import jax.numpy as jnp
from jax import lax
from jax.sharding import PartitionSpec as P

NFRAC = 16
NPSF = 8
PSF_RADIUS = 4
PASSES = 16
HALO = 11


sentinel = 1000000.0
half_sentinel = 500000.0
pivot_span = 16.0


def _row_halo(block, dim, width):
    count = lax.axis_size("row")
    forward = [(i, i + 1) for i in range(count - 1)]
    backward = [(target, source) for source, target in forward]
    size = block.shape[dim]
    low = lax.ppermute(lax.slice_in_dim(block, size - width, None, axis=dim), "row", forward)
    high = lax.ppermute(lax.slice_in_dim(block, 0, width, axis=dim), "row", backward)
    return jnp.concatenate([low, block, high], axis=dim)


def _col_halo(block, dim, width):
    count = lax.axis_size("col")
    size = block.shape[dim]
    right_edge = lax.slice_in_dim(block, size - width, None, axis=dim)
    left_edge = lax.slice_in_dim(block, 0, width, axis=dim)
    if count != 2:
        forward = [(i, i + 1) for i in range(count - 1)]
        backward = [(target, source) for source, target in forward]
        low = lax.ppermute(right_edge, "col", forward)
        high = lax.ppermute(left_edge, "col", backward)
        return jnp.concatenate([low, block, high], axis=dim)
    first = lax.axis_index("col") == 0
    outgoing = jnp.moveaxis(jnp.where(first, right_edge, left_edge), dim, 0)
    packed_shape = outgoing.shape
    packed = outgoing.reshape(width, -1)
    arrived = lax.ppermute(packed, "col", [(0, 1), (1, 0)])
    arrived = jnp.moveaxis(arrived.reshape(packed_shape), 0, dim)
    zeros = jnp.zeros_like(arrived)
    low = jnp.where(first, zeros, arrived)
    high = jnp.where(first, arrived, zeros)
    return jnp.concatenate([low, block, high], axis=dim)


def extended(block, row_dim, col_dim, width):
    return _col_halo(_row_halo(block, row_dim, width), col_dim, width)


def lanczos_table():
    fraction = jnp.arange(NFRAC, dtype=jnp.float32) / NFRAC
    offset_grid = jnp.arange(-2, 4, dtype=jnp.float32)
    spread = offset_grid[None, :] - fraction[:, None]
    kernel = jnp.sinc(spread) * jnp.sinc(spread / 3.0)
    return kernel / jnp.sum(kernel, axis=1, keepdims=True)


def blur_table():
    offset_grid = jnp.arange(-PSF_RADIUS, PSF_RADIUS + 1, dtype=jnp.float32)
    widths = 0.7 + 0.2 * jnp.arange(NPSF, dtype=jnp.float32)
    kernel = jnp.exp(-0.5 * (offset_grid[None, :] / widths[:, None]) ** 2)
    return kernel / jnp.sum(kernel, axis=1, keepdims=True)


def lookup(indices, entries, kernel_table):
    chooser = (indices[:, None] == lax.broadcasted_iota(jnp.int32, (1, entries), 1)).astype(
        jnp.float32
    )
    return jnp.dot(chooser, kernel_table, precision=lax.Precision.HIGHEST)


def placed_taps(weights, shifts):
    reach = 2 * HALO + 1
    positions = lax.broadcasted_iota(jnp.int32, (1, 1, reach), 2)
    tap_slot = HALO + shifts[:, None, None] + lax.broadcasted_iota(jnp.int32, (1, 6, 1), 1) - 2
    spread = (tap_slot == positions).astype(jnp.float32)
    return jnp.sum(weights[:, :, None] * spread, axis=1)


def resample_axis(stack, coefficients, out_len, which_axis):
    out_shape = list(stack.shape)
    out_shape[which_axis] = out_len
    total = jnp.zeros(tuple(out_shape), jnp.float32)
    for position in range(2 * HALO + 1):
        window = lax.slice_in_dim(stack, position, position + out_len, 1, which_axis)
        total = total + coefficients[:, position, None, None] * window
    return total


def bisect_lower(valid_count, count_below):

    def one_pass(sweep_no, bounds):
        lower_edge, upper_edge = bounds
        middle = 0.5 * (lower_edge + upper_edge)
        enough = 2.0 * count_below(middle) >= valid_count
        return (jnp.where(enough, lower_edge, middle), jnp.where(enough, middle, upper_edge))

    initial = (
        jnp.full(valid_count.shape, -pivot_span, jnp.float32),
        jnp.full(valid_count.shape, pivot_span, jnp.float32),
    )
    return lax.fori_loop(0, PASSES, one_pass, initial)[0]


def stack_median(pixel_stack):
    valid_count = jnp.sum(pixel_stack < half_sentinel, axis=0, dtype=jnp.float32)

    def count_below(middle):
        return jnp.sum(pixel_stack <= middle[None], axis=0, dtype=jnp.float32)

    lower_edge = bisect_lower(valid_count, count_below)
    return jnp.min(jnp.where(pixel_stack > lower_edge[None], pixel_stack, sentinel), axis=0)


def body(exposures, bad_pixels, offsets, warp_index, blur_index):
    group_size, row_count, col_count = exposures.shape
    kernel_table = lanczos_table()
    coef_down = placed_taps(lookup(warp_index[:, 0], NFRAC, kernel_table), offsets[:, 0])
    coef_across = placed_taps(lookup(warp_index[:, 1], NFRAC, kernel_table), offsets[:, 1])
    padded = extended(exposures, 1, 2, HALO)
    across = resample_axis(padded, coef_down, row_count, 1)
    warped = resample_axis(across, coef_across, col_count, 2)
    flagged = jnp.where(bad_pixels == 1, sentinel, warped)
    band = stack_median(lax.all_to_all(flagged, "exp", split_axis=1, concat_axis=0, tiled=True))
    groups = lax.axis_size("exp")
    median_sky = lax.all_to_all(
        jnp.tile(band, (groups, 1)), "exp", split_axis=0, concat_axis=0, tiled=True
    )
    bordered = extended(median_sky, 0, 1, PSF_RADIUS)
    blur = blur_table()
    taps = 2 * PSF_RADIUS + 1
    blurred_rows = jnp.zeros((NPSF, row_count, col_count + 2 * PSF_RADIUS), jnp.float32)
    for tap_no in range(taps):
        blurred_rows = (
            blurred_rows
            + blur[:, tap_no, None, None] * bordered[None, tap_no : tap_no + row_count, :]
        )
    smoothed = jnp.zeros((NPSF, row_count, col_count), jnp.float32)
    for tap_no in range(taps):
        smoothed = (
            smoothed + blur[:, tap_no, None, None] * blurred_rows[:, :, tap_no : tap_no + col_count]
        )
    chooser = (blur_index[:, None] == lax.broadcasted_iota(jnp.int32, (1, NPSF), 1)).astype(
        jnp.float32
    )
    sky_model = jnp.zeros((group_size, row_count, col_count), jnp.float32)
    for kernel_no in range(NPSF):
        sky_model = sky_model + chooser[:, kernel_no, None, None] * smoothed[kernel_no][None]
    residual = jnp.where(bad_pixels == 1, 0.0, warped - sky_model)
    return (residual, median_sky)


def solution(mesh):
    return jax.shard_map(
        body,
        mesh=mesh,
        in_specs=(
            P("exp", "row", "col"),
            P("exp", "row", "col"),
            P("exp", None),
            P("exp", None),
            P("exp"),
        ),
        out_specs=(P("exp", "row", "col"), P("row", "col")),
        check_vma=False,
    )
```

```python
import jax
import jax.numpy as jnp
from jax import lax
from jax.sharding import PartitionSpec as P
from jax.experimental import pallas as pl
from jax.experimental.pallas import tpu as pltpu

NFRAC = 16
NPSF = 8
PSF_RADIUS = 4
PASSES = 16
HALO = 11


sentinel = 1000000.0
half_sentinel = 500000.0
pivot_span = 16.0


def _row_halo(block, dim, width):
    count = lax.axis_size("row")
    forward = [(i, i + 1) for i in range(count - 1)]
    backward = [(target, source) for source, target in forward]
    size = block.shape[dim]
    low = lax.ppermute(lax.slice_in_dim(block, size - width, None, axis=dim), "row", forward)
    high = lax.ppermute(lax.slice_in_dim(block, 0, width, axis=dim), "row", backward)
    return jnp.concatenate([low, block, high], axis=dim)


def _col_halo(block, dim, width):
    count = lax.axis_size("col")
    size = block.shape[dim]
    right_edge = lax.slice_in_dim(block, size - width, None, axis=dim)
    left_edge = lax.slice_in_dim(block, 0, width, axis=dim)
    if count != 2:
        forward = [(i, i + 1) for i in range(count - 1)]
        backward = [(target, source) for source, target in forward]
        low = lax.ppermute(right_edge, "col", forward)
        high = lax.ppermute(left_edge, "col", backward)
        return jnp.concatenate([low, block, high], axis=dim)
    first = lax.axis_index("col") == 0
    outgoing = jnp.moveaxis(jnp.where(first, right_edge, left_edge), dim, 0)
    packed_shape = outgoing.shape
    packed = outgoing.reshape(width, -1)
    arrived = lax.ppermute(packed, "col", [(0, 1), (1, 0)])
    arrived = jnp.moveaxis(arrived.reshape(packed_shape), 0, dim)
    zeros = jnp.zeros_like(arrived)
    low = jnp.where(first, zeros, arrived)
    high = jnp.where(first, arrived, zeros)
    return jnp.concatenate([low, block, high], axis=dim)


def extended(block, row_dim, col_dim, width):
    return _col_halo(_row_halo(block, row_dim, width), col_dim, width)


def lanczos_table():
    fraction = jnp.arange(NFRAC, dtype=jnp.float32) / NFRAC
    offset_grid = jnp.arange(-2, 4, dtype=jnp.float32)
    spread = offset_grid[None, :] - fraction[:, None]
    kernel = jnp.sinc(spread) * jnp.sinc(spread / 3.0)
    return kernel / jnp.sum(kernel, axis=1, keepdims=True)


def blur_table():
    offset_grid = jnp.arange(-PSF_RADIUS, PSF_RADIUS + 1, dtype=jnp.float32)
    widths = 0.7 + 0.2 * jnp.arange(NPSF, dtype=jnp.float32)
    kernel = jnp.exp(-0.5 * (offset_grid[None, :] / widths[:, None]) ** 2)
    return kernel / jnp.sum(kernel, axis=1, keepdims=True)


def lookup(indices, entries, kernel_table):
    chooser = (indices[:, None] == lax.broadcasted_iota(jnp.int32, (1, entries), 1)).astype(
        jnp.float32
    )
    return jnp.dot(chooser, kernel_table, precision=lax.Precision.HIGHEST)


def placed_taps(weights, shifts):
    reach = 2 * HALO + 1
    positions = lax.broadcasted_iota(jnp.int32, (1, 1, reach), 2)
    tap_slot = HALO + shifts[:, None, None] + lax.broadcasted_iota(jnp.int32, (1, 6, 1), 1) - 2
    spread = (tap_slot == positions).astype(jnp.float32)
    return jnp.sum(weights[:, :, None] * spread, axis=1)


def resample_axis(stack, coefficients, out_len, which_axis):
    out_shape = list(stack.shape)
    out_shape[which_axis] = out_len
    total = jnp.zeros(tuple(out_shape), jnp.float32)
    for position in range(2 * HALO + 1):
        window = lax.slice_in_dim(stack, position, position + out_len, 1, which_axis)
        total = total + coefficients[:, position, None, None] * window
    return total


def bisect_lower(valid_count, count_below):

    def one_pass(sweep_no, bounds):
        lower_edge, upper_edge = bounds
        middle = 0.5 * (lower_edge + upper_edge)
        enough = 2.0 * count_below(middle) >= valid_count
        return (jnp.where(enough, lower_edge, middle), jnp.where(enough, middle, upper_edge))

    initial = (
        jnp.full(valid_count.shape, -pivot_span, jnp.float32),
        jnp.full(valid_count.shape, pivot_span, jnp.float32),
    )
    return lax.fori_loop(0, PASSES, one_pass, initial)[0]


def stack_median(pixel_stack):
    valid_count = jnp.sum(pixel_stack < half_sentinel, axis=0, dtype=jnp.float32)

    def count_below(middle):
        return jnp.sum(pixel_stack <= middle[None], axis=0, dtype=jnp.float32)

    lower_edge = bisect_lower(valid_count, count_below)
    return jnp.min(jnp.where(pixel_stack > lower_edge[None], pixel_stack, sentinel), axis=0)


TAPS = 6


def _warp_kernel(
    row_shift, col_shift, row_weight, col_weight, padded, bad, warped_out, flagged_out
):
    group_size, row_count, col_count = warped_out.shape
    width = padded.shape[2]

    height = padded.shape[1]

    def one_exposure(e, carry):
        block = pltpu.roll(padded[e], height - row_shift[e], 0)
        across = None
        for tap in range(TAPS):
            term = row_weight[e * TAPS + tap] * block[tap : tap + row_count, :]
            across = term if across is None else across + term
        across = pltpu.roll(across, width - col_shift[e], 1)
        total = None
        for tap in range(TAPS):
            term = col_weight[e * TAPS + tap] * across[:, tap : tap + col_count]
            total = term if total is None else total + term
        warped_out[e] = total
        flagged_out[e] = jnp.where(bad[e] == 1, sentinel, total)
        return carry

    lax.fori_loop(0, group_size, one_exposure, 0)


def warp_and_flag(padded, bad_pixels, offsets, warp_index):
    group_size, row_count, col_count = bad_pixels.shape
    kernel_table = lanczos_table()
    row_weight = lookup(warp_index[:, 0], NFRAC, kernel_table).reshape(-1)
    col_weight = lookup(warp_index[:, 1], NFRAC, kernel_table).reshape(-1)
    row_shift = offsets[:, 0] + (HALO - 2)
    col_shift = offsets[:, 1] + (HALO - 2)
    lanes = -(-padded.shape[2] // 128) * 128
    rows = -(-padded.shape[1] // 8) * 8
    padded = jnp.pad(
        padded, ((0, 0), (0, rows - padded.shape[1]), (0, lanes - padded.shape[2]))
    )
    smem = pl.BlockSpec(memory_space=pltpu.SMEM)
    vmem = pl.BlockSpec(memory_space=pltpu.VMEM)
    shape = jax.ShapeDtypeStruct((group_size, row_count, col_count), jnp.float32)
    return pl.pallas_call(
        _warp_kernel,
        out_shape=(shape, shape),
        in_specs=[smem, smem, smem, smem, vmem, vmem],
        out_specs=(vmem, vmem),
    )(row_shift, col_shift, row_weight, col_weight, padded, bad_pixels)


def body(exposures, bad_pixels, offsets, warp_index, blur_index):
    group_size, row_count, col_count = exposures.shape
    padded = extended(exposures, 1, 2, HALO)
    warped, flagged = warp_and_flag(padded, bad_pixels, offsets, warp_index)
    band = stack_median(lax.all_to_all(flagged, "exp", split_axis=1, concat_axis=0, tiled=True))
    groups = lax.axis_size("exp")
    median_sky = lax.all_to_all(
        jnp.tile(band, (groups, 1)), "exp", split_axis=0, concat_axis=0, tiled=True
    )
    bordered = extended(median_sky, 0, 1, PSF_RADIUS)
    blur = blur_table()
    taps = 2 * PSF_RADIUS + 1
    blurred_rows = jnp.zeros((NPSF, row_count, col_count + 2 * PSF_RADIUS), jnp.float32)
    for tap_no in range(taps):
        blurred_rows = (
            blurred_rows
            + blur[:, tap_no, None, None] * bordered[None, tap_no : tap_no + row_count, :]
        )
    smoothed = jnp.zeros((NPSF, row_count, col_count), jnp.float32)
    for tap_no in range(taps):
        smoothed = (
            smoothed + blur[:, tap_no, None, None] * blurred_rows[:, :, tap_no : tap_no + col_count]
        )
    chooser = (blur_index[:, None] == lax.broadcasted_iota(jnp.int32, (1, NPSF), 1)).astype(
        jnp.float32
    )
    sky_model = jnp.zeros((group_size, row_count, col_count), jnp.float32)
    for kernel_no in range(NPSF):
        sky_model = sky_model + chooser[:, kernel_no, None, None] * smoothed[kernel_no][None]
    residual = jnp.where(bad_pixels == 1, 0.0, warped - sky_model)
    return (residual, median_sky)


def solution(mesh):
    return jax.shard_map(
        body,
        mesh=mesh,
        in_specs=(
            P("exp", "row", "col"),
            P("exp", "row", "col"),
            P("exp", None),
            P("exp", None),
            P("exp"),
        ),
        out_specs=(P("exp", "row", "col"), P("row", "col")),
        check_vma=False,
    )
```

```python
import jax
import jax.numpy as jnp
from jax import lax
from jax.sharding import PartitionSpec as P
from jax.experimental import pallas as pl
from jax.experimental.pallas import tpu as pltpu

NFRAC = 16
NPSF = 8
PSF_RADIUS = 4
PASSES = 16
HALO = 11


sentinel = 1000000.0
half_sentinel = 500000.0
pivot_span = 16.0


def _row_halo(block, dim, width):
    count = lax.axis_size("row")
    forward = [(i, i + 1) for i in range(count - 1)]
    backward = [(target, source) for source, target in forward]
    size = block.shape[dim]
    low = lax.ppermute(lax.slice_in_dim(block, size - width, None, axis=dim), "row", forward)
    high = lax.ppermute(lax.slice_in_dim(block, 0, width, axis=dim), "row", backward)
    return jnp.concatenate([low, block, high], axis=dim)


def _col_halo(block, dim, width):
    count = lax.axis_size("col")
    size = block.shape[dim]
    right_edge = lax.slice_in_dim(block, size - width, None, axis=dim)
    left_edge = lax.slice_in_dim(block, 0, width, axis=dim)
    if count != 2:
        forward = [(i, i + 1) for i in range(count - 1)]
        backward = [(target, source) for source, target in forward]
        low = lax.ppermute(right_edge, "col", forward)
        high = lax.ppermute(left_edge, "col", backward)
        return jnp.concatenate([low, block, high], axis=dim)
    first = lax.axis_index("col") == 0
    outgoing = jnp.moveaxis(jnp.where(first, right_edge, left_edge), dim, 0)
    packed_shape = outgoing.shape
    packed = outgoing.reshape(width, -1)
    arrived = lax.ppermute(packed, "col", [(0, 1), (1, 0)])
    arrived = jnp.moveaxis(arrived.reshape(packed_shape), 0, dim)
    zeros = jnp.zeros_like(arrived)
    low = jnp.where(first, zeros, arrived)
    high = jnp.where(first, arrived, zeros)
    return jnp.concatenate([low, block, high], axis=dim)


def extended(block, row_dim, col_dim, width):
    return _col_halo(_row_halo(block, row_dim, width), col_dim, width)


def lanczos_table():
    fraction = jnp.arange(NFRAC, dtype=jnp.float32) / NFRAC
    offset_grid = jnp.arange(-2, 4, dtype=jnp.float32)
    spread = offset_grid[None, :] - fraction[:, None]
    kernel = jnp.sinc(spread) * jnp.sinc(spread / 3.0)
    return kernel / jnp.sum(kernel, axis=1, keepdims=True)


def blur_table():
    offset_grid = jnp.arange(-PSF_RADIUS, PSF_RADIUS + 1, dtype=jnp.float32)
    widths = 0.7 + 0.2 * jnp.arange(NPSF, dtype=jnp.float32)
    kernel = jnp.exp(-0.5 * (offset_grid[None, :] / widths[:, None]) ** 2)
    return kernel / jnp.sum(kernel, axis=1, keepdims=True)


def lookup(indices, entries, kernel_table):
    chooser = (indices[:, None] == lax.broadcasted_iota(jnp.int32, (1, entries), 1)).astype(
        jnp.float32
    )
    return jnp.dot(chooser, kernel_table, precision=lax.Precision.HIGHEST)


def placed_taps(weights, shifts):
    reach = 2 * HALO + 1
    positions = lax.broadcasted_iota(jnp.int32, (1, 1, reach), 2)
    tap_slot = HALO + shifts[:, None, None] + lax.broadcasted_iota(jnp.int32, (1, 6, 1), 1) - 2
    spread = (tap_slot == positions).astype(jnp.float32)
    return jnp.sum(weights[:, :, None] * spread, axis=1)


def resample_axis(stack, coefficients, out_len, which_axis):
    out_shape = list(stack.shape)
    out_shape[which_axis] = out_len
    total = jnp.zeros(tuple(out_shape), jnp.float32)
    for position in range(2 * HALO + 1):
        window = lax.slice_in_dim(stack, position, position + out_len, 1, which_axis)
        total = total + coefficients[:, position, None, None] * window
    return total


def bisect_lower(valid_count, count_below):

    def one_pass(sweep_no, bounds):
        lower_edge, upper_edge = bounds
        middle = 0.5 * (lower_edge + upper_edge)
        enough = 2.0 * count_below(middle) >= valid_count
        return (jnp.where(enough, lower_edge, middle), jnp.where(enough, middle, upper_edge))

    initial = (
        jnp.full(valid_count.shape, -pivot_span, jnp.float32),
        jnp.full(valid_count.shape, pivot_span, jnp.float32),
    )
    return lax.fori_loop(0, PASSES, one_pass, initial)[0]


def stack_median(pixel_stack):
    valid_count = jnp.sum(pixel_stack < half_sentinel, axis=0, dtype=jnp.float32)

    def count_below(middle):
        return jnp.sum(pixel_stack <= middle[None], axis=0, dtype=jnp.float32)

    lower_edge = bisect_lower(valid_count, count_below)
    return jnp.min(jnp.where(pixel_stack > lower_edge[None], pixel_stack, sentinel), axis=0)


TAPS = 6


def _banded(shape, shift, weight, base, first):
    down = lax.broadcasted_iota(jnp.int32, shape, 0)
    across = lax.broadcasted_iota(jnp.int32, shape, 1)
    gap = (across - down if first else down - across) + (base - shift)
    matrix = jnp.zeros(shape, jnp.float32)
    for tap in range(TAPS):
        matrix = jnp.where(gap == tap, weight[tap], matrix)
    return matrix


def _warp_kernel(
    row_shift, col_shift, row_weight, col_weight, padded, bad, warped_out, flagged_out
):
    group_size, row_count, col_count = warped_out.shape
    height = padded.shape[1]
    bands, _, band_rows, _ = flagged_out.shape
    lane = 128
    exact = lax.Precision.HIGHEST

    def one_exposure(e, carry):
        rw = [row_weight[e * TAPS + tap] for tap in range(TAPS)]
        cw = [col_weight[e * TAPS + tap] for tap in range(TAPS)]
        down = _banded((row_count, height), row_shift[e], rw, 0, True)
        across = jnp.dot(down, padded[e], precision=exact, preferred_element_type=jnp.float32)
        same = _banded((lane, lane), col_shift[e], cw, 0, False)
        after = _banded((lane, lane), col_shift[e], cw, lane, False)
        pieces = []
        for block in range(col_count // lane):
            here = across[:, block * lane : (block + 1) * lane]
            ahead = across[:, (block + 1) * lane : (block + 2) * lane]
            pieces.append(
                jnp.dot(here, same, precision=exact, preferred_element_type=jnp.float32)
                + jnp.dot(ahead, after, precision=exact, preferred_element_type=jnp.float32)
            )
        total = jnp.concatenate(pieces, axis=1)
        warped_out[e] = total
        flagged = jnp.where(bad[e] == 1, sentinel, total)
        for band in range(bands):
            flagged_out[band, e] = flagged[band * band_rows : (band + 1) * band_rows]
        return carry

    lax.fori_loop(0, group_size, one_exposure, 0)


def warp_and_flag(padded, bad_pixels, offsets, warp_index):
    group_size, row_count, col_count = bad_pixels.shape
    kernel_table = lanczos_table()
    row_weight = lookup(warp_index[:, 0], NFRAC, kernel_table).reshape(-1)
    col_weight = lookup(warp_index[:, 1], NFRAC, kernel_table).reshape(-1)
    row_shift = offsets[:, 0] + (HALO - 2)
    col_shift = offsets[:, 1] + (HALO - 2)
    lanes = -(-padded.shape[2] // 128) * 128
    rows = -(-padded.shape[1] // 8) * 8
    padded = jnp.pad(
        padded, ((0, 0), (0, rows - padded.shape[1]), (0, lanes - padded.shape[2]))
    )
    smem = pl.BlockSpec(memory_space=pltpu.SMEM)
    vmem = pl.BlockSpec(memory_space=pltpu.VMEM)
    shape = jax.ShapeDtypeStruct((group_size, row_count, col_count), jnp.float32)
    bands = lax.axis_size("exp")
    banded = jax.ShapeDtypeStruct(
        (bands, group_size, row_count // bands, col_count), jnp.float32
    )
    return pl.pallas_call(
        _warp_kernel,
        out_shape=(shape, banded),
        in_specs=[smem, smem, smem, smem, vmem, vmem],
        out_specs=(vmem, vmem),
    )(row_shift, col_shift, row_weight, col_weight, padded, bad_pixels)


def body(exposures, bad_pixels, offsets, warp_index, blur_index):
    group_size, row_count, col_count = exposures.shape
    padded = extended(exposures, 1, 2, HALO)
    warped, flagged = warp_and_flag(padded, bad_pixels, offsets, warp_index)
    gathered = lax.all_to_all(flagged, "exp", split_axis=0, concat_axis=0, tiled=True)
    band = stack_median(gathered.reshape((-1,) + gathered.shape[2:]))
    groups = lax.axis_size("exp")
    median_sky = lax.all_to_all(
        jnp.tile(band, (groups, 1)), "exp", split_axis=0, concat_axis=0, tiled=True
    )
    bordered = extended(median_sky, 0, 1, PSF_RADIUS)
    blur = blur_table()
    taps = 2 * PSF_RADIUS + 1
    blurred_rows = jnp.zeros((NPSF, row_count, col_count + 2 * PSF_RADIUS), jnp.float32)
    for tap_no in range(taps):
        blurred_rows = (
            blurred_rows
            + blur[:, tap_no, None, None] * bordered[None, tap_no : tap_no + row_count, :]
        )
    smoothed = jnp.zeros((NPSF, row_count, col_count), jnp.float32)
    for tap_no in range(taps):
        smoothed = (
            smoothed + blur[:, tap_no, None, None] * blurred_rows[:, :, tap_no : tap_no + col_count]
        )
    chooser = (blur_index[:, None] == lax.broadcasted_iota(jnp.int32, (1, NPSF), 1)).astype(
        jnp.float32
    )
    sky_model = jnp.zeros((group_size, row_count, col_count), jnp.float32)
    for kernel_no in range(NPSF):
        sky_model = sky_model + chooser[:, kernel_no, None, None] * smoothed[kernel_no][None]
    residual = jnp.where(bad_pixels == 1, 0.0, warped - sky_model)
    return (residual, median_sky)


def solution(mesh):
    return jax.shard_map(
        body,
        mesh=mesh,
        in_specs=(
            P("exp", "row", "col"),
            P("exp", "row", "col"),
            P("exp", None),
            P("exp", None),
            P("exp"),
        ),
        out_specs=(P("exp", "row", "col"), P("row", "col")),
        check_vma=False,
    )
```

```python
import jax
import jax.numpy as jnp
from jax import lax
from jax.sharding import PartitionSpec as P
from jax.experimental import pallas as pl
from jax.experimental.pallas import tpu as pltpu

NFRAC = 16
NPSF = 8
PSF_RADIUS = 4
PASSES = 16
HALO = 11


sentinel = 1000000.0
half_sentinel = 500000.0
pivot_span = 16.0


def _row_halo(block, dim, width):
    count = lax.axis_size("row")
    forward = [(i, i + 1) for i in range(count - 1)]
    backward = [(target, source) for source, target in forward]
    size = block.shape[dim]
    low = lax.ppermute(lax.slice_in_dim(block, size - width, None, axis=dim), "row", forward)
    high = lax.ppermute(lax.slice_in_dim(block, 0, width, axis=dim), "row", backward)
    return jnp.concatenate([low, block, high], axis=dim)


def _col_halo(block, dim, width):
    count = lax.axis_size("col")
    size = block.shape[dim]
    right_edge = lax.slice_in_dim(block, size - width, None, axis=dim)
    left_edge = lax.slice_in_dim(block, 0, width, axis=dim)
    if count != 2:
        forward = [(i, i + 1) for i in range(count - 1)]
        backward = [(target, source) for source, target in forward]
        low = lax.ppermute(right_edge, "col", forward)
        high = lax.ppermute(left_edge, "col", backward)
        return jnp.concatenate([low, block, high], axis=dim)
    first = lax.axis_index("col") == 0
    outgoing = jnp.moveaxis(jnp.where(first, right_edge, left_edge), dim, 0)
    packed_shape = outgoing.shape
    packed = outgoing.reshape(width, -1)
    arrived = lax.ppermute(packed, "col", [(0, 1), (1, 0)])
    arrived = jnp.moveaxis(arrived.reshape(packed_shape), 0, dim)
    zeros = jnp.zeros_like(arrived)
    low = jnp.where(first, zeros, arrived)
    high = jnp.where(first, arrived, zeros)
    return jnp.concatenate([low, block, high], axis=dim)


def extended(block, row_dim, col_dim, width):
    return _col_halo(_row_halo(block, row_dim, width), col_dim, width)


def lanczos_table():
    fraction = jnp.arange(NFRAC, dtype=jnp.float32) / NFRAC
    offset_grid = jnp.arange(-2, 4, dtype=jnp.float32)
    spread = offset_grid[None, :] - fraction[:, None]
    kernel = jnp.sinc(spread) * jnp.sinc(spread / 3.0)
    return kernel / jnp.sum(kernel, axis=1, keepdims=True)


def blur_table():
    offset_grid = jnp.arange(-PSF_RADIUS, PSF_RADIUS + 1, dtype=jnp.float32)
    widths = 0.7 + 0.2 * jnp.arange(NPSF, dtype=jnp.float32)
    kernel = jnp.exp(-0.5 * (offset_grid[None, :] / widths[:, None]) ** 2)
    return kernel / jnp.sum(kernel, axis=1, keepdims=True)


def lookup(indices, entries, kernel_table):
    chooser = (indices[:, None] == lax.broadcasted_iota(jnp.int32, (1, entries), 1)).astype(
        jnp.float32
    )
    return jnp.dot(chooser, kernel_table, precision=lax.Precision.HIGHEST)


def placed_taps(weights, shifts):
    reach = 2 * HALO + 1
    positions = lax.broadcasted_iota(jnp.int32, (1, 1, reach), 2)
    tap_slot = HALO + shifts[:, None, None] + lax.broadcasted_iota(jnp.int32, (1, 6, 1), 1) - 2
    spread = (tap_slot == positions).astype(jnp.float32)
    return jnp.sum(weights[:, :, None] * spread, axis=1)


def resample_axis(stack, coefficients, out_len, which_axis):
    out_shape = list(stack.shape)
    out_shape[which_axis] = out_len
    total = jnp.zeros(tuple(out_shape), jnp.float32)
    for position in range(2 * HALO + 1):
        window = lax.slice_in_dim(stack, position, position + out_len, 1, which_axis)
        total = total + coefficients[:, position, None, None] * window
    return total


def bisect_lower(valid_count, count_below):

    def one_pass(sweep_no, bounds):
        lower_edge, upper_edge = bounds
        middle = 0.5 * (lower_edge + upper_edge)
        enough = 2.0 * count_below(middle) >= valid_count
        return (jnp.where(enough, lower_edge, middle), jnp.where(enough, middle, upper_edge))

    initial = (
        jnp.full(valid_count.shape, -pivot_span, jnp.float32),
        jnp.full(valid_count.shape, pivot_span, jnp.float32),
    )
    return lax.fori_loop(0, PASSES, one_pass, initial)[0]


def stack_median(pixel_stack):
    valid_count = jnp.sum(pixel_stack < half_sentinel, axis=0, dtype=jnp.float32)

    def count_below(middle):
        return jnp.sum(pixel_stack <= middle[None], axis=0, dtype=jnp.float32)

    lower_edge = bisect_lower(valid_count, count_below)
    return jnp.min(jnp.where(pixel_stack > lower_edge[None], pixel_stack, sentinel), axis=0)


TAPS = 6


def _warp_kernel(
    row_shift, col_shift, row_weight, col_weight, padded, bad, warped_out, flagged_out
):
    group_size, row_count, col_count = warped_out.shape
    bands, _, band_rows, _ = flagged_out.shape
    width = padded.shape[2]

    height = padded.shape[1]

    def one_exposure(e, carry):
        block = pltpu.roll(padded[e], height - row_shift[e], 0)
        across = None
        for tap in range(TAPS):
            term = row_weight[e * TAPS + tap] * block[tap : tap + row_count, :]
            across = term if across is None else across + term
        across = pltpu.roll(across, width - col_shift[e], 1)
        total = None
        for tap in range(TAPS):
            term = col_weight[e * TAPS + tap] * across[:, tap : tap + col_count]
            total = term if total is None else total + term
        warped_out[e] = total
        flagged = jnp.where(bad[e] == 1, sentinel, total)
        for band in range(bands):
            flagged_out[band, e] = flagged[band * band_rows : (band + 1) * band_rows]
        return carry

    lax.fori_loop(0, group_size, one_exposure, 0, unroll=True)


def warp_and_flag(padded, bad_pixels, offsets, warp_index):
    group_size, row_count, col_count = bad_pixels.shape
    kernel_table = lanczos_table()
    row_weight = lookup(warp_index[:, 0], NFRAC, kernel_table).reshape(-1)
    col_weight = lookup(warp_index[:, 1], NFRAC, kernel_table).reshape(-1)
    row_shift = offsets[:, 0] + (HALO - 2)
    col_shift = offsets[:, 1] + (HALO - 2)
    lanes = -(-padded.shape[2] // 128) * 128
    rows = -(-padded.shape[1] // 8) * 8
    padded = jnp.pad(
        padded, ((0, 0), (0, rows - padded.shape[1]), (0, lanes - padded.shape[2]))
    )
    smem = pl.BlockSpec(memory_space=pltpu.SMEM)
    vmem = pl.BlockSpec(memory_space=pltpu.VMEM)
    shape = jax.ShapeDtypeStruct((group_size, row_count, col_count), jnp.float32)
    bands = lax.axis_size("exp")
    banded = jax.ShapeDtypeStruct(
        (bands, group_size, row_count // bands, col_count), jnp.float32
    )
    return pl.pallas_call(
        _warp_kernel,
        out_shape=(shape, banded),
        in_specs=[smem, smem, smem, smem, vmem, vmem],
        out_specs=(vmem, vmem),
    )(row_shift, col_shift, row_weight, col_weight, padded, bad_pixels)


def body(exposures, bad_pixels, offsets, warp_index, blur_index):
    group_size, row_count, col_count = exposures.shape
    padded = extended(exposures, 1, 2, HALO)
    warped, flagged = warp_and_flag(padded, bad_pixels, offsets, warp_index)
    gathered = lax.all_to_all(flagged, "exp", split_axis=0, concat_axis=0, tiled=True)
    band = stack_median(gathered.reshape((-1,) + gathered.shape[2:]))
    groups = lax.axis_size("exp")
    median_sky = lax.all_to_all(
        jnp.tile(band, (groups, 1)), "exp", split_axis=0, concat_axis=0, tiled=True
    )
    bordered = extended(median_sky, 0, 1, PSF_RADIUS)
    blur = blur_table()
    taps = 2 * PSF_RADIUS + 1
    blurred_rows = jnp.zeros((NPSF, row_count, col_count + 2 * PSF_RADIUS), jnp.float32)
    for tap_no in range(taps):
        blurred_rows = (
            blurred_rows
            + blur[:, tap_no, None, None] * bordered[None, tap_no : tap_no + row_count, :]
        )
    smoothed = jnp.zeros((NPSF, row_count, col_count), jnp.float32)
    for tap_no in range(taps):
        smoothed = (
            smoothed + blur[:, tap_no, None, None] * blurred_rows[:, :, tap_no : tap_no + col_count]
        )
    chooser = (blur_index[:, None] == lax.broadcasted_iota(jnp.int32, (1, NPSF), 1)).astype(
        jnp.float32
    )
    sky_model = jnp.zeros((group_size, row_count, col_count), jnp.float32)
    for kernel_no in range(NPSF):
        sky_model = sky_model + chooser[:, kernel_no, None, None] * smoothed[kernel_no][None]
    residual = jnp.where(bad_pixels == 1, 0.0, warped - sky_model)
    return (residual, median_sky)


def solution(mesh):
    return jax.shard_map(
        body,
        mesh=mesh,
        in_specs=(
            P("exp", "row", "col"),
            P("exp", "row", "col"),
            P("exp", None),
            P("exp", None),
            P("exp"),
        ),
        out_specs=(P("exp", "row", "col"), P("row", "col")),
        check_vma=False,
    )
```

```python
import jax
import jax.numpy as jnp
from jax import lax
from jax.sharding import PartitionSpec as P
from jax.experimental import pallas as pl
from jax.experimental.pallas import tpu as pltpu

NFRAC = 16
NPSF = 8
PSF_RADIUS = 4
PASSES = 16
HALO = 11


sentinel = 1000000.0
half_sentinel = 500000.0
pivot_span = 16.0


def _row_halo(block, dim, width):
    count = lax.axis_size("row")
    forward = [(i, i + 1) for i in range(count - 1)]
    backward = [(target, source) for source, target in forward]
    size = block.shape[dim]
    low = lax.ppermute(lax.slice_in_dim(block, size - width, None, axis=dim), "row", forward)
    high = lax.ppermute(lax.slice_in_dim(block, 0, width, axis=dim), "row", backward)
    return jnp.concatenate([low, block, high], axis=dim)


def _col_halo(block, dim, width):
    count = lax.axis_size("col")
    size = block.shape[dim]
    right_edge = lax.slice_in_dim(block, size - width, None, axis=dim)
    left_edge = lax.slice_in_dim(block, 0, width, axis=dim)
    if count != 2:
        forward = [(i, i + 1) for i in range(count - 1)]
        backward = [(target, source) for source, target in forward]
        low = lax.ppermute(right_edge, "col", forward)
        high = lax.ppermute(left_edge, "col", backward)
        return jnp.concatenate([low, block, high], axis=dim)
    first = lax.axis_index("col") == 0
    outgoing = jnp.moveaxis(jnp.where(first, right_edge, left_edge), dim, 0)
    packed_shape = outgoing.shape
    packed = outgoing.reshape(width, -1)
    arrived = lax.ppermute(packed, "col", [(0, 1), (1, 0)])
    arrived = jnp.moveaxis(arrived.reshape(packed_shape), 0, dim)
    zeros = jnp.zeros_like(arrived)
    low = jnp.where(first, zeros, arrived)
    high = jnp.where(first, arrived, zeros)
    return jnp.concatenate([low, block, high], axis=dim)


def extended(block, row_dim, col_dim, width):
    return _col_halo(_row_halo(block, row_dim, width), col_dim, width)


def lanczos_table():
    fraction = jnp.arange(NFRAC, dtype=jnp.float32) / NFRAC
    offset_grid = jnp.arange(-2, 4, dtype=jnp.float32)
    spread = offset_grid[None, :] - fraction[:, None]
    kernel = jnp.sinc(spread) * jnp.sinc(spread / 3.0)
    return kernel / jnp.sum(kernel, axis=1, keepdims=True)


def blur_table():
    offset_grid = jnp.arange(-PSF_RADIUS, PSF_RADIUS + 1, dtype=jnp.float32)
    widths = 0.7 + 0.2 * jnp.arange(NPSF, dtype=jnp.float32)
    kernel = jnp.exp(-0.5 * (offset_grid[None, :] / widths[:, None]) ** 2)
    return kernel / jnp.sum(kernel, axis=1, keepdims=True)


def lookup(indices, entries, kernel_table):
    chooser = (indices[:, None] == lax.broadcasted_iota(jnp.int32, (1, entries), 1)).astype(
        jnp.float32
    )
    return jnp.dot(chooser, kernel_table, precision=lax.Precision.HIGHEST)


def placed_taps(weights, shifts):
    reach = 2 * HALO + 1
    positions = lax.broadcasted_iota(jnp.int32, (1, 1, reach), 2)
    tap_slot = HALO + shifts[:, None, None] + lax.broadcasted_iota(jnp.int32, (1, 6, 1), 1) - 2
    spread = (tap_slot == positions).astype(jnp.float32)
    return jnp.sum(weights[:, :, None] * spread, axis=1)


def resample_axis(stack, coefficients, out_len, which_axis):
    out_shape = list(stack.shape)
    out_shape[which_axis] = out_len
    total = jnp.zeros(tuple(out_shape), jnp.float32)
    for position in range(2 * HALO + 1):
        window = lax.slice_in_dim(stack, position, position + out_len, 1, which_axis)
        total = total + coefficients[:, position, None, None] * window
    return total


def bisect_lower(valid_count, count_below):

    def one_pass(sweep_no, bounds):
        lower_edge, upper_edge = bounds
        middle = 0.5 * (lower_edge + upper_edge)
        enough = 2.0 * count_below(middle) >= valid_count
        return (jnp.where(enough, lower_edge, middle), jnp.where(enough, middle, upper_edge))

    initial = (
        jnp.full(valid_count.shape, -pivot_span, jnp.float32),
        jnp.full(valid_count.shape, pivot_span, jnp.float32),
    )
    return lax.fori_loop(0, PASSES, one_pass, initial)[0]


def stack_median(pixel_stack):
    valid_count = jnp.sum(pixel_stack < half_sentinel, axis=0, dtype=jnp.float32)

    def count_below(middle):
        return jnp.sum(pixel_stack <= middle[None], axis=0, dtype=jnp.float32)

    lower_edge = bisect_lower(valid_count, count_below)
    return jnp.min(jnp.where(pixel_stack > lower_edge[None], pixel_stack, sentinel), axis=0)


TAPS = 6


def _warp_kernel(
    row_shift, col_shift, row_weight, col_weight, padded, bad, warped_out, flagged_out
):
    group_size, row_count, col_count = warped_out.shape
    bands, _, band_rows, _ = flagged_out.shape
    width = padded.shape[2]

    height = padded.shape[1]

    def one_exposure(e, carry):
        block = pltpu.roll(padded[e], height - row_shift[e], 0)
        across = None
        for tap in range(TAPS):
            term = row_weight[e * TAPS + tap] * block[tap : tap + row_count, :]
            across = term if across is None else across + term
        across = pltpu.roll(across, width - col_shift[e], 1)
        total = None
        for tap in range(TAPS):
            term = col_weight[e * TAPS + tap] * across[:, tap : tap + col_count]
            total = term if total is None else total + term
        warped_out[e] = total
        flagged = jnp.where(bad[e] == 1, sentinel, total)
        for band in range(bands):
            flagged_out[band, e] = flagged[band * band_rows : (band + 1) * band_rows]
        return carry

    lax.fori_loop(0, group_size, one_exposure, 0, unroll=True)


def warp_and_flag(padded, bad_pixels, offsets, warp_index):
    group_size, row_count, col_count = bad_pixels.shape
    kernel_table = lanczos_table()
    row_weight = lookup(warp_index[:, 0], NFRAC, kernel_table).reshape(-1)
    col_weight = lookup(warp_index[:, 1], NFRAC, kernel_table).reshape(-1)
    row_shift = offsets[:, 0] + (HALO - 2)
    col_shift = offsets[:, 1] + (HALO - 2)
    lanes = -(-padded.shape[2] // 128) * 128
    rows = -(-padded.shape[1] // 8) * 8
    padded = jnp.pad(
        padded, ((0, 0), (0, rows - padded.shape[1]), (0, lanes - padded.shape[2]))
    )
    smem = pl.BlockSpec(memory_space=pltpu.SMEM)
    vmem = pl.BlockSpec(memory_space=pltpu.VMEM)
    shape = jax.ShapeDtypeStruct((group_size, row_count, col_count), jnp.float32)
    bands = lax.axis_size("exp")
    banded = jax.ShapeDtypeStruct(
        (bands, group_size, row_count // bands, col_count), jnp.float32
    )
    return pl.pallas_call(
        _warp_kernel,
        out_shape=(shape, banded),
        in_specs=[smem, smem, smem, smem, vmem, vmem],
        out_specs=(vmem, vmem),
    )(row_shift, col_shift, row_weight, col_weight, padded, bad_pixels)


def body(exposures, bad_pixels, offsets, warp_index, blur_index):
    group_size, row_count, col_count = exposures.shape
    padded = extended(exposures, 1, 2, HALO)
    warped, flagged = warp_and_flag(padded, bad_pixels, offsets, warp_index)
    gathered = lax.all_to_all(flagged, "exp", split_axis=0, concat_axis=0, tiled=True)
    band = stack_median(gathered.reshape((-1,) + gathered.shape[2:]))
    groups = lax.axis_size("exp")
    sides = lax.axis_size("col")
    band_rows = band.shape[0]
    full = lax.all_to_all(
        jnp.tile(band, (groups * sides, 1)), ("exp", "col"), split_axis=0, concat_axis=0, tiled=True
    )
    full = full.reshape(groups, sides, band_rows, col_count)
    full = full.transpose(0, 2, 1, 3).reshape(row_count, sides * col_count)
    start = lax.axis_index("col") * col_count
    median_sky = lax.dynamic_slice_in_dim(full, start, col_count, axis=1)
    wide = jnp.pad(full, ((0, 0), (PSF_RADIUS, PSF_RADIUS)))
    wide = lax.dynamic_slice_in_dim(wide, start, col_count + 2 * PSF_RADIUS, axis=1)
    bordered = _row_halo(wide, 0, PSF_RADIUS)
    blur = blur_table()
    taps = 2 * PSF_RADIUS + 1
    blurred_rows = jnp.zeros((NPSF, row_count, col_count + 2 * PSF_RADIUS), jnp.float32)
    for tap_no in range(taps):
        blurred_rows = (
            blurred_rows
            + blur[:, tap_no, None, None] * bordered[None, tap_no : tap_no + row_count, :]
        )
    smoothed = jnp.zeros((NPSF, row_count, col_count), jnp.float32)
    for tap_no in range(taps):
        smoothed = (
            smoothed + blur[:, tap_no, None, None] * blurred_rows[:, :, tap_no : tap_no + col_count]
        )
    sky_model = jnp.take(smoothed, blur_index, axis=0)
    residual = jnp.where(bad_pixels == 1, 0.0, warped - sky_model)
    return (residual, median_sky)


def solution(mesh):
    return jax.shard_map(
        body,
        mesh=mesh,
        in_specs=(
            P("exp", "row", "col"),
            P("exp", "row", "col"),
            P("exp", None),
            P("exp", None),
            P("exp"),
        ),
        out_specs=(P("exp", "row", "col"), P("row", "col")),
        check_vma=False,
    )
```

```python
import jax
import jax.numpy as jnp
from jax import lax
from jax.sharding import PartitionSpec as P
from jax.experimental import pallas as pl
from jax.experimental.pallas import tpu as pltpu

NFRAC = 16
NPSF = 8
PSF_RADIUS = 4
PASSES = 16
HALO = 11


sentinel = 1000000.0
half_sentinel = 500000.0
pivot_span = 16.0


def _row_halo(block, dim, width):
    count = lax.axis_size("row")
    forward = [(i, i + 1) for i in range(count - 1)]
    backward = [(target, source) for source, target in forward]
    size = block.shape[dim]
    low = lax.ppermute(lax.slice_in_dim(block, size - width, None, axis=dim), "row", forward)
    high = lax.ppermute(lax.slice_in_dim(block, 0, width, axis=dim), "row", backward)
    return jnp.concatenate([low, block, high], axis=dim)


def _col_halo(block, dim, width):
    count = lax.axis_size("col")
    size = block.shape[dim]
    right_edge = lax.slice_in_dim(block, size - width, None, axis=dim)
    left_edge = lax.slice_in_dim(block, 0, width, axis=dim)
    if count != 2:
        forward = [(i, i + 1) for i in range(count - 1)]
        backward = [(target, source) for source, target in forward]
        low = lax.ppermute(right_edge, "col", forward)
        high = lax.ppermute(left_edge, "col", backward)
        return jnp.concatenate([low, block, high], axis=dim)
    first = lax.axis_index("col") == 0
    outgoing = jnp.moveaxis(jnp.where(first, right_edge, left_edge), dim, 0)
    packed_shape = outgoing.shape
    packed = outgoing.reshape(width, -1)
    arrived = lax.ppermute(packed, "col", [(0, 1), (1, 0)])
    arrived = jnp.moveaxis(arrived.reshape(packed_shape), 0, dim)
    zeros = jnp.zeros_like(arrived)
    low = jnp.where(first, zeros, arrived)
    high = jnp.where(first, arrived, zeros)
    return jnp.concatenate([low, block, high], axis=dim)


def extended(block, row_dim, col_dim, width):
    return _col_halo(_row_halo(block, row_dim, width), col_dim, width)


def lanczos_table():
    fraction = jnp.arange(NFRAC, dtype=jnp.float32) / NFRAC
    offset_grid = jnp.arange(-2, 4, dtype=jnp.float32)
    spread = offset_grid[None, :] - fraction[:, None]
    kernel = jnp.sinc(spread) * jnp.sinc(spread / 3.0)
    return kernel / jnp.sum(kernel, axis=1, keepdims=True)


def blur_table():
    offset_grid = jnp.arange(-PSF_RADIUS, PSF_RADIUS + 1, dtype=jnp.float32)
    widths = 0.7 + 0.2 * jnp.arange(NPSF, dtype=jnp.float32)
    kernel = jnp.exp(-0.5 * (offset_grid[None, :] / widths[:, None]) ** 2)
    return kernel / jnp.sum(kernel, axis=1, keepdims=True)


def lookup(indices, entries, kernel_table):
    chooser = (indices[:, None] == lax.broadcasted_iota(jnp.int32, (1, entries), 1)).astype(
        jnp.float32
    )
    return jnp.dot(chooser, kernel_table, precision=lax.Precision.HIGHEST)


def placed_taps(weights, shifts):
    reach = 2 * HALO + 1
    positions = lax.broadcasted_iota(jnp.int32, (1, 1, reach), 2)
    tap_slot = HALO + shifts[:, None, None] + lax.broadcasted_iota(jnp.int32, (1, 6, 1), 1) - 2
    spread = (tap_slot == positions).astype(jnp.float32)
    return jnp.sum(weights[:, :, None] * spread, axis=1)


def resample_axis(stack, coefficients, out_len, which_axis):
    out_shape = list(stack.shape)
    out_shape[which_axis] = out_len
    total = jnp.zeros(tuple(out_shape), jnp.float32)
    for position in range(2 * HALO + 1):
        window = lax.slice_in_dim(stack, position, position + out_len, 1, which_axis)
        total = total + coefficients[:, position, None, None] * window
    return total


def bisect_lower(valid_count, count_below):

    def one_pass(sweep_no, bounds):
        lower_edge, upper_edge = bounds
        middle = 0.5 * (lower_edge + upper_edge)
        enough = 2.0 * count_below(middle) >= valid_count
        return (jnp.where(enough, lower_edge, middle), jnp.where(enough, middle, upper_edge))

    initial = (
        jnp.full(valid_count.shape, -pivot_span, jnp.float32),
        jnp.full(valid_count.shape, pivot_span, jnp.float32),
    )
    return lax.fori_loop(0, PASSES, one_pass, initial)[0]


def stack_median(pixel_stack):
    valid_count = jnp.sum(pixel_stack < half_sentinel, axis=0, dtype=jnp.float32)

    def count_below(middle):
        return jnp.sum(pixel_stack <= middle[None], axis=0, dtype=jnp.float32)

    lower_edge = bisect_lower(valid_count, count_below)
    return jnp.min(jnp.where(pixel_stack > lower_edge[None], pixel_stack, sentinel), axis=0)


TAPS = 6


def _warp_kernel(
    row_shift, col_shift, row_weight, col_weight, padded, bad, warped_out, flagged_out
):
    group_size, row_count, col_count = warped_out.shape
    bands, _, band_rows, _ = flagged_out.shape
    width = padded.shape[2]

    height = padded.shape[1]

    def one_exposure(e, carry):
        block = pltpu.roll(padded[e], height - row_shift[e], 0)
        across = None
        for tap in range(TAPS):
            term = row_weight[e * TAPS + tap] * block[tap : tap + row_count, :]
            across = term if across is None else across + term
        across = pltpu.roll(across, width - col_shift[e], 1)
        total = None
        for tap in range(TAPS):
            term = col_weight[e * TAPS + tap] * across[:, tap : tap + col_count]
            total = term if total is None else total + term
        warped_out[e] = total
        flagged = jnp.where(bad[e] == 1, sentinel, total)
        for band in range(bands):
            flagged_out[band, e] = flagged[band * band_rows : (band + 1) * band_rows]
        return carry

    lax.fori_loop(0, group_size, one_exposure, 0, unroll=True)


def warp_and_flag(padded, bad_pixels, offsets, warp_index):
    group_size, row_count, col_count = bad_pixels.shape
    kernel_table = lanczos_table()
    row_weight = lookup(warp_index[:, 0], NFRAC, kernel_table).reshape(-1)
    col_weight = lookup(warp_index[:, 1], NFRAC, kernel_table).reshape(-1)
    row_shift = offsets[:, 0] + (HALO - 2)
    col_shift = offsets[:, 1] + (HALO - 2)
    lanes = -(-padded.shape[2] // 128) * 128
    rows = -(-padded.shape[1] // 8) * 8
    padded = jnp.pad(
        padded, ((0, 0), (0, rows - padded.shape[1]), (0, lanes - padded.shape[2]))
    )
    smem = pl.BlockSpec(memory_space=pltpu.SMEM)
    vmem = pl.BlockSpec(memory_space=pltpu.VMEM)
    shape = jax.ShapeDtypeStruct((group_size, row_count, col_count), jnp.float32)
    bands = lax.axis_size("exp")
    banded = jax.ShapeDtypeStruct(
        (bands, group_size, row_count // bands, col_count), jnp.float32
    )
    return pl.pallas_call(
        _warp_kernel,
        out_shape=(shape, banded),
        in_specs=[smem, smem, smem, smem, vmem, vmem],
        out_specs=(vmem, vmem),
    )(row_shift, col_shift, row_weight, col_weight, padded, bad_pixels)


def body(exposures, bad_pixels, offsets, warp_index, blur_index):
    group_size, row_count, col_count = exposures.shape
    padded = extended(exposures, 1, 2, HALO)
    half = group_size // 2
    parts = []
    for lo, hi in ((0, half), (half, group_size)):
        part_warped, part_flagged = warp_and_flag(
            padded[lo:hi], bad_pixels[lo:hi], offsets[lo:hi], warp_index[lo:hi]
        )
        arrived = lax.all_to_all(part_flagged, "exp", split_axis=0, concat_axis=0, tiled=True)
        parts.append((part_warped, arrived))
    warped = jnp.concatenate([w for w, _ in parts], axis=0)
    gathered = jnp.concatenate([a for _, a in parts], axis=1)
    band = stack_median(gathered.reshape((-1,) + gathered.shape[2:]))
    groups = lax.axis_size("exp")
    sides = lax.axis_size("col")
    band_rows = band.shape[0]
    full = lax.all_to_all(
        jnp.tile(band, (groups * sides, 1)), ("exp", "col"), split_axis=0, concat_axis=0, tiled=True
    )
    full = full.reshape(groups, sides, band_rows, col_count)
    full = full.transpose(0, 2, 1, 3).reshape(row_count, sides * col_count)
    start = lax.axis_index("col") * col_count
    median_sky = lax.dynamic_slice_in_dim(full, start, col_count, axis=1)
    wide = jnp.pad(full, ((0, 0), (PSF_RADIUS, PSF_RADIUS)))
    wide = lax.dynamic_slice_in_dim(wide, start, col_count + 2 * PSF_RADIUS, axis=1)
    bordered = _row_halo(wide, 0, PSF_RADIUS)
    blur = blur_table()
    taps = 2 * PSF_RADIUS + 1
    blurred_rows = jnp.zeros((NPSF, row_count, col_count + 2 * PSF_RADIUS), jnp.float32)
    for tap_no in range(taps):
        blurred_rows = (
            blurred_rows
            + blur[:, tap_no, None, None] * bordered[None, tap_no : tap_no + row_count, :]
        )
    smoothed = jnp.zeros((NPSF, row_count, col_count), jnp.float32)
    for tap_no in range(taps):
        smoothed = (
            smoothed + blur[:, tap_no, None, None] * blurred_rows[:, :, tap_no : tap_no + col_count]
        )
    chooser = (blur_index[:, None] == lax.broadcasted_iota(jnp.int32, (1, NPSF), 1)).astype(
        jnp.float32
    )
    sky_model = jnp.zeros((group_size, row_count, col_count), jnp.float32)
    for kernel_no in range(NPSF):
        sky_model = sky_model + chooser[:, kernel_no, None, None] * smoothed[kernel_no][None]
    residual = jnp.where(bad_pixels == 1, 0.0, warped - sky_model)
    return (residual, median_sky)


def solution(mesh):
    return jax.shard_map(
        body,
        mesh=mesh,
        in_specs=(
            P("exp", "row", "col"),
            P("exp", "row", "col"),
            P("exp", None),
            P("exp", None),
            P("exp"),
        ),
        out_specs=(P("exp", "row", "col"), P("row", "col")),
        check_vma=False,
    )
```

```python
import jax
import jax.numpy as jnp
from jax import lax
from jax.sharding import PartitionSpec as P
from jax.experimental import pallas as pl
from jax.experimental.pallas import tpu as pltpu

NFRAC = 16
NPSF = 8
PSF_RADIUS = 4
PASSES = 16
HALO = 11


sentinel = 1000000.0
half_sentinel = 500000.0
pivot_span = 16.0


def _row_halo(block, dim, width):
    count = lax.axis_size("row")
    forward = [(i, i + 1) for i in range(count - 1)]
    backward = [(target, source) for source, target in forward]
    size = block.shape[dim]
    low = lax.ppermute(lax.slice_in_dim(block, size - width, None, axis=dim), "row", forward)
    high = lax.ppermute(lax.slice_in_dim(block, 0, width, axis=dim), "row", backward)
    return jnp.concatenate([low, block, high], axis=dim)


def _col_halo(block, dim, width):
    count = lax.axis_size("col")
    size = block.shape[dim]
    right_edge = lax.slice_in_dim(block, size - width, None, axis=dim)
    left_edge = lax.slice_in_dim(block, 0, width, axis=dim)
    if count != 2:
        forward = [(i, i + 1) for i in range(count - 1)]
        backward = [(target, source) for source, target in forward]
        low = lax.ppermute(right_edge, "col", forward)
        high = lax.ppermute(left_edge, "col", backward)
        return jnp.concatenate([low, block, high], axis=dim)
    first = lax.axis_index("col") == 0
    outgoing = jnp.moveaxis(jnp.where(first, right_edge, left_edge), dim, 0)
    packed_shape = outgoing.shape
    packed = outgoing.reshape(width, -1)
    arrived = lax.ppermute(packed, "col", [(0, 1), (1, 0)])
    arrived = jnp.moveaxis(arrived.reshape(packed_shape), 0, dim)
    zeros = jnp.zeros_like(arrived)
    low = jnp.where(first, zeros, arrived)
    high = jnp.where(first, arrived, zeros)
    return jnp.concatenate([low, block, high], axis=dim)


def extended(block, row_dim, col_dim, width):
    return _col_halo(_row_halo(block, row_dim, width), col_dim, width)


def lanczos_table():
    fraction = jnp.arange(NFRAC, dtype=jnp.float32) / NFRAC
    offset_grid = jnp.arange(-2, 4, dtype=jnp.float32)
    spread = offset_grid[None, :] - fraction[:, None]
    kernel = jnp.sinc(spread) * jnp.sinc(spread / 3.0)
    return kernel / jnp.sum(kernel, axis=1, keepdims=True)


def blur_table():
    offset_grid = jnp.arange(-PSF_RADIUS, PSF_RADIUS + 1, dtype=jnp.float32)
    widths = 0.7 + 0.2 * jnp.arange(NPSF, dtype=jnp.float32)
    kernel = jnp.exp(-0.5 * (offset_grid[None, :] / widths[:, None]) ** 2)
    return kernel / jnp.sum(kernel, axis=1, keepdims=True)


def lookup(indices, entries, kernel_table):
    chooser = (indices[:, None] == lax.broadcasted_iota(jnp.int32, (1, entries), 1)).astype(
        jnp.float32
    )
    return jnp.dot(chooser, kernel_table, precision=lax.Precision.HIGHEST)


def placed_taps(weights, shifts):
    reach = 2 * HALO + 1
    positions = lax.broadcasted_iota(jnp.int32, (1, 1, reach), 2)
    tap_slot = HALO + shifts[:, None, None] + lax.broadcasted_iota(jnp.int32, (1, 6, 1), 1) - 2
    spread = (tap_slot == positions).astype(jnp.float32)
    return jnp.sum(weights[:, :, None] * spread, axis=1)


def resample_axis(stack, coefficients, out_len, which_axis):
    out_shape = list(stack.shape)
    out_shape[which_axis] = out_len
    total = jnp.zeros(tuple(out_shape), jnp.float32)
    for position in range(2 * HALO + 1):
        window = lax.slice_in_dim(stack, position, position + out_len, 1, which_axis)
        total = total + coefficients[:, position, None, None] * window
    return total


def bisect_lower(valid_count, count_below):

    def one_pass(sweep_no, bounds):
        lower_edge, upper_edge = bounds
        middle = 0.5 * (lower_edge + upper_edge)
        enough = 2.0 * count_below(middle) >= valid_count
        return (jnp.where(enough, lower_edge, middle), jnp.where(enough, middle, upper_edge))

    initial = (
        jnp.full(valid_count.shape, -pivot_span, jnp.float32),
        jnp.full(valid_count.shape, pivot_span, jnp.float32),
    )
    return lax.fori_loop(0, PASSES, one_pass, initial)[0]


def stack_median(pixel_stack):
    valid_count = jnp.sum(pixel_stack < half_sentinel, axis=0, dtype=jnp.float32)

    def count_below(middle):
        return jnp.sum(pixel_stack <= middle[None], axis=0, dtype=jnp.float32)

    lower_edge = bisect_lower(valid_count, count_below)
    return jnp.min(jnp.where(pixel_stack > lower_edge[None], pixel_stack, sentinel), axis=0)


TAPS = 6


def _warp_kernel(
    row_shift, col_shift, row_weight, col_weight, padded, bad, warped_out, flagged_out
):
    group_size, row_count, col_count = warped_out.shape
    bands, _, band_rows, _ = flagged_out.shape
    width = padded.shape[2]

    height = padded.shape[1]

    def one_exposure(e, carry):
        block = pltpu.roll(padded[e], height - row_shift[e], 0)
        across = None
        for tap in range(TAPS):
            term = row_weight[e * TAPS + tap] * block[tap : tap + row_count, :]
            across = term if across is None else across + term
        across = pltpu.roll(across, width - col_shift[e], 1)
        total = None
        for tap in range(TAPS):
            term = col_weight[e * TAPS + tap] * across[:, tap : tap + col_count]
            total = term if total is None else total + term
        warped_out[e] = total
        flagged = jnp.where(bad[e] == 1, sentinel, total)
        for band in range(bands):
            flagged_out[band, e] = flagged[band * band_rows : (band + 1) * band_rows]
        return carry

    lax.fori_loop(0, group_size, one_exposure, 0, unroll=True)


def warp_and_flag(padded, bad_pixels, offsets, warp_index):
    group_size, row_count, col_count = bad_pixels.shape
    kernel_table = lanczos_table()
    row_weight = lookup(warp_index[:, 0], NFRAC, kernel_table).reshape(-1)
    col_weight = lookup(warp_index[:, 1], NFRAC, kernel_table).reshape(-1)
    row_shift = offsets[:, 0] + (HALO - 2)
    col_shift = offsets[:, 1] + (HALO - 2)
    lanes = -(-padded.shape[2] // 128) * 128
    rows = -(-padded.shape[1] // 8) * 8
    padded = jnp.pad(
        padded, ((0, 0), (0, rows - padded.shape[1]), (0, lanes - padded.shape[2]))
    )
    smem = pl.BlockSpec(memory_space=pltpu.SMEM)
    vmem = pl.BlockSpec(memory_space=pltpu.VMEM)
    shape = jax.ShapeDtypeStruct((group_size, row_count, col_count), jnp.float32)
    bands = lax.axis_size("exp")
    banded = jax.ShapeDtypeStruct(
        (bands, group_size, row_count // bands, col_count), jnp.float32
    )
    return pl.pallas_call(
        _warp_kernel,
        out_shape=(shape, banded),
        in_specs=[smem, smem, smem, smem, vmem, vmem],
        out_specs=(vmem, vmem),
    )(row_shift, col_shift, row_weight, col_weight, padded, bad_pixels)


def body(exposures, bad_pixels, offsets, warp_index, blur_index):
    group_size, row_count, col_count = exposures.shape
    padded = extended(exposures, 1, 2, HALO)
    warped, flagged = warp_and_flag(padded, bad_pixels, offsets, warp_index)
    gathered = lax.all_to_all(flagged, "exp", split_axis=0, concat_axis=0, tiled=True)
    band = stack_median(gathered.reshape((-1,) + gathered.shape[2:]))
    groups = lax.axis_size("exp")
    sides = lax.axis_size("col")
    band_rows = band.shape[0]
    full = lax.all_to_all(
        jnp.tile(band, (groups * sides, 1)), ("exp", "col"), split_axis=0, concat_axis=0, tiled=True
    )
    full = full.reshape(groups, sides, band_rows, col_count)
    full = full.transpose(0, 2, 1, 3).reshape(row_count, sides * col_count)
    start = lax.axis_index("col") * col_count
    median_sky = lax.dynamic_slice_in_dim(full, start, col_count, axis=1)
    wide = jnp.pad(full, ((0, 0), (PSF_RADIUS, PSF_RADIUS)))
    wide = lax.dynamic_slice_in_dim(wide, start, col_count + 2 * PSF_RADIUS, axis=1)
    bordered = _row_halo(wide, 0, PSF_RADIUS)
    blur = blur_table()
    taps = 2 * PSF_RADIUS + 1
    blurred_rows = jnp.zeros((NPSF, row_count, col_count + 2 * PSF_RADIUS), jnp.float32)
    for tap_no in range(taps):
        blurred_rows = (
            blurred_rows
            + blur[:, tap_no, None, None] * bordered[None, tap_no : tap_no + row_count, :]
        )
    smoothed = jnp.zeros((NPSF, row_count, col_count), jnp.float32)
    for tap_no in range(taps):
        smoothed = (
            smoothed + blur[:, tap_no, None, None] * blurred_rows[:, :, tap_no : tap_no + col_count]
        )
    chooser = (blur_index[:, None] == lax.broadcasted_iota(jnp.int32, (1, NPSF), 1)).astype(
        jnp.float32
    )
    sky_model = jnp.zeros((group_size, row_count, col_count), jnp.float32)
    for kernel_no in range(NPSF):
        sky_model = sky_model + chooser[:, kernel_no, None, None] * smoothed[kernel_no][None]
    residual = jnp.where(bad_pixels == 1, 0.0, warped - sky_model)
    return (residual, median_sky)


def solution(mesh):
    return jax.shard_map(
        body,
        mesh=mesh,
        in_specs=(
            P("exp", "row", "col"),
            P("exp", "row", "col"),
            P("exp", None),
            P("exp", None),
            P("exp"),
        ),
        out_specs=(P("exp", "row", "col"), P("row", "col")),
        check_vma=False,
    )
```

```python
import jax
import jax.numpy as jnp
from jax import lax
from jax.sharding import PartitionSpec as P
from jax.experimental import pallas as pl
from jax.experimental.pallas import tpu as pltpu

NFRAC = 16
NPSF = 8
PSF_RADIUS = 4
PASSES = 16
HALO = 11


sentinel = 1000000.0
half_sentinel = 500000.0
pivot_span = 16.0


def _row_halo(block, dim, width):
    count = lax.axis_size("row")
    forward = [(i, i + 1) for i in range(count - 1)]
    backward = [(target, source) for source, target in forward]
    size = block.shape[dim]
    low = lax.ppermute(lax.slice_in_dim(block, size - width, None, axis=dim), "row", forward)
    high = lax.ppermute(lax.slice_in_dim(block, 0, width, axis=dim), "row", backward)
    return jnp.concatenate([low, block, high], axis=dim)


def _col_halo(block, dim, width):
    count = lax.axis_size("col")
    size = block.shape[dim]
    right_edge = lax.slice_in_dim(block, size - width, None, axis=dim)
    left_edge = lax.slice_in_dim(block, 0, width, axis=dim)
    if count != 2:
        forward = [(i, i + 1) for i in range(count - 1)]
        backward = [(target, source) for source, target in forward]
        low = lax.ppermute(right_edge, "col", forward)
        high = lax.ppermute(left_edge, "col", backward)
        return jnp.concatenate([low, block, high], axis=dim)
    first = lax.axis_index("col") == 0
    outgoing = jnp.moveaxis(jnp.where(first, right_edge, left_edge), dim, 0)
    packed_shape = outgoing.shape
    packed = outgoing.reshape(width, -1)
    arrived = lax.ppermute(packed, "col", [(0, 1), (1, 0)])
    arrived = jnp.moveaxis(arrived.reshape(packed_shape), 0, dim)
    zeros = jnp.zeros_like(arrived)
    low = jnp.where(first, zeros, arrived)
    high = jnp.where(first, arrived, zeros)
    return jnp.concatenate([low, block, high], axis=dim)


def extended(block, row_dim, col_dim, width):
    return _col_halo(_row_halo(block, row_dim, width), col_dim, width)


def lanczos_table():
    fraction = jnp.arange(NFRAC, dtype=jnp.float32) / NFRAC
    offset_grid = jnp.arange(-2, 4, dtype=jnp.float32)
    spread = offset_grid[None, :] - fraction[:, None]
    kernel = jnp.sinc(spread) * jnp.sinc(spread / 3.0)
    return kernel / jnp.sum(kernel, axis=1, keepdims=True)


def blur_table():
    offset_grid = jnp.arange(-PSF_RADIUS, PSF_RADIUS + 1, dtype=jnp.float32)
    widths = 0.7 + 0.2 * jnp.arange(NPSF, dtype=jnp.float32)
    kernel = jnp.exp(-0.5 * (offset_grid[None, :] / widths[:, None]) ** 2)
    return kernel / jnp.sum(kernel, axis=1, keepdims=True)


def lookup(indices, entries, kernel_table):
    chooser = (indices[:, None] == lax.broadcasted_iota(jnp.int32, (1, entries), 1)).astype(
        jnp.float32
    )
    return jnp.dot(chooser, kernel_table, precision=lax.Precision.HIGHEST)


def placed_taps(weights, shifts):
    reach = 2 * HALO + 1
    positions = lax.broadcasted_iota(jnp.int32, (1, 1, reach), 2)
    tap_slot = HALO + shifts[:, None, None] + lax.broadcasted_iota(jnp.int32, (1, 6, 1), 1) - 2
    spread = (tap_slot == positions).astype(jnp.float32)
    return jnp.sum(weights[:, :, None] * spread, axis=1)


def resample_axis(stack, coefficients, out_len, which_axis):
    out_shape = list(stack.shape)
    out_shape[which_axis] = out_len
    total = jnp.zeros(tuple(out_shape), jnp.float32)
    for position in range(2 * HALO + 1):
        window = lax.slice_in_dim(stack, position, position + out_len, 1, which_axis)
        total = total + coefficients[:, position, None, None] * window
    return total


def bisect_lower(valid_count, count_below):

    def one_pass(sweep_no, bounds):
        lower_edge, upper_edge = bounds
        middle = 0.5 * (lower_edge + upper_edge)
        enough = 2.0 * count_below(middle) >= valid_count
        return (jnp.where(enough, lower_edge, middle), jnp.where(enough, middle, upper_edge))

    initial = (
        jnp.full(valid_count.shape, -pivot_span, jnp.float32),
        jnp.full(valid_count.shape, pivot_span, jnp.float32),
    )
    return lax.fori_loop(0, PASSES, one_pass, initial)[0]


def stack_median(pixel_stack):
    valid_count = jnp.sum(pixel_stack < half_sentinel, axis=0, dtype=jnp.float32)

    def count_below(middle):
        return jnp.sum(pixel_stack <= middle[None], axis=0, dtype=jnp.float32)

    lower_edge = bisect_lower(valid_count, count_below)
    return jnp.min(jnp.where(pixel_stack > lower_edge[None], pixel_stack, sentinel), axis=0)


TAPS = 6


def _warp_kernel(
    row_shift, col_shift, row_weight, col_weight, me, padded, bad, warped_out, flagged_out
):
    group_size, row_count, col_count = warped_out.shape
    bands, _, band_rows, _ = flagged_out.shape
    width = padded.shape[2]

    height = padded.shape[1]

    def one_exposure(e, carry):
        block = pltpu.roll(padded[e], height - row_shift[e], 0)
        across = None
        for tap in range(TAPS):
            term = row_weight[e * TAPS + tap] * block[tap : tap + row_count, :]
            across = term if across is None else across + term
        across = pltpu.roll(across, width - col_shift[e], 1)
        total = None
        for tap in range(TAPS):
            term = col_weight[e * TAPS + tap] * across[:, tap : tap + col_count]
            total = term if total is None else total + term
        warped_out[e] = total
        flagged = jnp.where(bad[e] == 1, sentinel, total)
        for band in range(bands):
            slot = lax.rem(band - me[0] + bands, bands)
            flagged_out[slot, e] = flagged[band * band_rows : (band + 1) * band_rows]
        return carry

    lax.fori_loop(0, group_size, one_exposure, 0, unroll=True)


def warp_and_flag(padded, bad_pixels, offsets, warp_index):
    group_size, row_count, col_count = bad_pixels.shape
    kernel_table = lanczos_table()
    row_weight = lookup(warp_index[:, 0], NFRAC, kernel_table).reshape(-1)
    col_weight = lookup(warp_index[:, 1], NFRAC, kernel_table).reshape(-1)
    row_shift = offsets[:, 0] + (HALO - 2)
    col_shift = offsets[:, 1] + (HALO - 2)
    me = lax.axis_index("exp").astype(jnp.int32).reshape(1)
    lanes = -(-padded.shape[2] // 128) * 128
    rows = -(-padded.shape[1] // 8) * 8
    padded = jnp.pad(
        padded, ((0, 0), (0, rows - padded.shape[1]), (0, lanes - padded.shape[2]))
    )
    smem = pl.BlockSpec(memory_space=pltpu.SMEM)
    vmem = pl.BlockSpec(memory_space=pltpu.VMEM)
    shape = jax.ShapeDtypeStruct((group_size, row_count, col_count), jnp.float32)
    bands = lax.axis_size("exp")
    banded = jax.ShapeDtypeStruct(
        (bands, group_size, row_count // bands, col_count), jnp.float32
    )
    return pl.pallas_call(
        _warp_kernel,
        out_shape=(shape, banded),
        in_specs=[smem, smem, smem, smem, smem, vmem, vmem],
        out_specs=(vmem, vmem),
    )(row_shift, col_shift, row_weight, col_weight, me, padded, bad_pixels)


def body(exposures, bad_pixels, offsets, warp_index, blur_index):
    group_size, row_count, col_count = exposures.shape
    padded = extended(exposures, 1, 2, HALO)
    warped, flagged = warp_and_flag(padded, bad_pixels, offsets, warp_index)
    groups = lax.axis_size("exp")
    arrived = [flagged[0]]
    for step in range(1, groups):
        pairs = [(i, (i + step) % groups) for i in range(groups)]
        arrived.append(lax.ppermute(flagged[step], "exp", pairs))
    band = stack_median(jnp.concatenate(arrived, axis=0))
    groups = lax.axis_size("exp")
    sides = lax.axis_size("col")
    band_rows = band.shape[0]
    full = lax.all_to_all(
        jnp.tile(band, (groups * sides, 1)), ("exp", "col"), split_axis=0, concat_axis=0, tiled=True
    )
    full = full.reshape(groups, sides, band_rows, col_count)
    full = full.transpose(0, 2, 1, 3).reshape(row_count, sides * col_count)
    start = lax.axis_index("col") * col_count
    median_sky = lax.dynamic_slice_in_dim(full, start, col_count, axis=1)
    wide = jnp.pad(full, ((0, 0), (PSF_RADIUS, PSF_RADIUS)))
    wide = lax.dynamic_slice_in_dim(wide, start, col_count + 2 * PSF_RADIUS, axis=1)
    bordered = _row_halo(wide, 0, PSF_RADIUS)
    blur = blur_table()
    taps = 2 * PSF_RADIUS + 1
    blurred_rows = jnp.zeros((NPSF, row_count, col_count + 2 * PSF_RADIUS), jnp.float32)
    for tap_no in range(taps):
        blurred_rows = (
            blurred_rows
            + blur[:, tap_no, None, None] * bordered[None, tap_no : tap_no + row_count, :]
        )
    smoothed = jnp.zeros((NPSF, row_count, col_count), jnp.float32)
    for tap_no in range(taps):
        smoothed = (
            smoothed + blur[:, tap_no, None, None] * blurred_rows[:, :, tap_no : tap_no + col_count]
        )
    chooser = (blur_index[:, None] == lax.broadcasted_iota(jnp.int32, (1, NPSF), 1)).astype(
        jnp.float32
    )
    sky_model = jnp.zeros((group_size, row_count, col_count), jnp.float32)
    for kernel_no in range(NPSF):
        sky_model = sky_model + chooser[:, kernel_no, None, None] * smoothed[kernel_no][None]
    residual = jnp.where(bad_pixels == 1, 0.0, warped - sky_model)
    return (residual, median_sky)


def solution(mesh):
    return jax.shard_map(
        body,
        mesh=mesh,
        in_specs=(
            P("exp", "row", "col"),
            P("exp", "row", "col"),
            P("exp", None),
            P("exp", None),
            P("exp"),
        ),
        out_specs=(P("exp", "row", "col"), P("row", "col")),
        check_vma=False,
    )
```

```python
import functools

import jax
import jax.numpy as jnp
from jax import lax
from jax.sharding import PartitionSpec as P
from jax.experimental import pallas as pl
from jax.experimental.pallas import tpu as pltpu

NFRAC = 16
NPSF = 8
PSF_RADIUS = 4
PASSES = 16
HALO = 11


sentinel = 1000000.0
half_sentinel = 500000.0
pivot_span = 16.0


def _row_halo(block, dim, width):
    count = lax.axis_size("row")
    forward = [(i, i + 1) for i in range(count - 1)]
    backward = [(target, source) for source, target in forward]
    size = block.shape[dim]
    low = lax.ppermute(lax.slice_in_dim(block, size - width, None, axis=dim), "row", forward)
    high = lax.ppermute(lax.slice_in_dim(block, 0, width, axis=dim), "row", backward)
    return jnp.concatenate([low, block, high], axis=dim)


def _col_halo(block, dim, width):
    count = lax.axis_size("col")
    size = block.shape[dim]
    right_edge = lax.slice_in_dim(block, size - width, None, axis=dim)
    left_edge = lax.slice_in_dim(block, 0, width, axis=dim)
    if count != 2:
        forward = [(i, i + 1) for i in range(count - 1)]
        backward = [(target, source) for source, target in forward]
        low = lax.ppermute(right_edge, "col", forward)
        high = lax.ppermute(left_edge, "col", backward)
        return jnp.concatenate([low, block, high], axis=dim)
    first = lax.axis_index("col") == 0
    outgoing = jnp.moveaxis(jnp.where(first, right_edge, left_edge), dim, 0)
    packed_shape = outgoing.shape
    packed = outgoing.reshape(width, -1)
    arrived = lax.ppermute(packed, "col", [(0, 1), (1, 0)])
    arrived = jnp.moveaxis(arrived.reshape(packed_shape), 0, dim)
    zeros = jnp.zeros_like(arrived)
    low = jnp.where(first, zeros, arrived)
    high = jnp.where(first, arrived, zeros)
    return jnp.concatenate([low, block, high], axis=dim)


def extended(block, row_dim, col_dim, width):
    return _col_halo(_row_halo(block, row_dim, width), col_dim, width)


def lanczos_table():
    fraction = jnp.arange(NFRAC, dtype=jnp.float32) / NFRAC
    offset_grid = jnp.arange(-2, 4, dtype=jnp.float32)
    spread = offset_grid[None, :] - fraction[:, None]
    kernel = jnp.sinc(spread) * jnp.sinc(spread / 3.0)
    return kernel / jnp.sum(kernel, axis=1, keepdims=True)


def blur_table():
    offset_grid = jnp.arange(-PSF_RADIUS, PSF_RADIUS + 1, dtype=jnp.float32)
    widths = 0.7 + 0.2 * jnp.arange(NPSF, dtype=jnp.float32)
    kernel = jnp.exp(-0.5 * (offset_grid[None, :] / widths[:, None]) ** 2)
    return kernel / jnp.sum(kernel, axis=1, keepdims=True)


def lookup(indices, entries, kernel_table):
    chooser = (indices[:, None] == lax.broadcasted_iota(jnp.int32, (1, entries), 1)).astype(
        jnp.float32
    )
    return jnp.dot(chooser, kernel_table, precision=lax.Precision.HIGHEST)


def placed_taps(weights, shifts):
    reach = 2 * HALO + 1
    positions = lax.broadcasted_iota(jnp.int32, (1, 1, reach), 2)
    tap_slot = HALO + shifts[:, None, None] + lax.broadcasted_iota(jnp.int32, (1, 6, 1), 1) - 2
    spread = (tap_slot == positions).astype(jnp.float32)
    return jnp.sum(weights[:, :, None] * spread, axis=1)


def resample_axis(stack, coefficients, out_len, which_axis):
    out_shape = list(stack.shape)
    out_shape[which_axis] = out_len
    total = jnp.zeros(tuple(out_shape), jnp.float32)
    for position in range(2 * HALO + 1):
        window = lax.slice_in_dim(stack, position, position + out_len, 1, which_axis)
        total = total + coefficients[:, position, None, None] * window
    return total


def bisect_lower(valid_count, count_below):

    def one_pass(sweep_no, bounds):
        lower_edge, upper_edge = bounds
        middle = 0.5 * (lower_edge + upper_edge)
        enough = 2.0 * count_below(middle) >= valid_count
        return (jnp.where(enough, lower_edge, middle), jnp.where(enough, middle, upper_edge))

    initial = (
        jnp.full(valid_count.shape, -pivot_span, jnp.float32),
        jnp.full(valid_count.shape, pivot_span, jnp.float32),
    )
    return lax.fori_loop(0, PASSES, one_pass, initial)[0]


def stack_median(pixel_stack):
    valid_count = jnp.sum(pixel_stack < half_sentinel, axis=0, dtype=jnp.float32)

    def count_below(middle):
        return jnp.sum(pixel_stack <= middle[None], axis=0, dtype=jnp.float32)

    lower_edge = bisect_lower(valid_count, count_below)
    return jnp.min(jnp.where(pixel_stack > lower_edge[None], pixel_stack, sentinel), axis=0)


TAPS = 6


def _warp_kernel(
    row_shift, col_shift, row_weight, col_weight, me, padded, bad, warped_out, flagged_out
):
    group_size, row_count, col_count = warped_out.shape
    bands, _, band_rows, _ = flagged_out.shape
    width = padded.shape[2]

    height = padded.shape[1]

    def one_exposure(e, carry):
        block = pltpu.roll(padded[e], height - row_shift[e], 0)
        across = None
        for tap in range(TAPS):
            term = row_weight[e * TAPS + tap] * block[tap : tap + row_count, :]
            across = term if across is None else across + term
        across = pltpu.roll(across, width - col_shift[e], 1)
        total = None
        for tap in range(TAPS):
            term = col_weight[e * TAPS + tap] * across[:, tap : tap + col_count]
            total = term if total is None else total + term
        warped_out[e] = total
        flagged = jnp.where(bad[e] == 1, sentinel, total)
        for band in range(bands):
            slot = lax.rem(band - me[0] + bands, bands)
            flagged_out[slot, e] = flagged[band * band_rows : (band + 1) * band_rows]
        return carry

    lax.fori_loop(0, group_size, one_exposure, 0, unroll=True)


def warp_and_flag(padded, bad_pixels, offsets, warp_index):
    group_size, row_count, col_count = bad_pixels.shape
    kernel_table = lanczos_table()
    row_weight = lookup(warp_index[:, 0], NFRAC, kernel_table).reshape(-1)
    col_weight = lookup(warp_index[:, 1], NFRAC, kernel_table).reshape(-1)
    row_shift = offsets[:, 0] + (HALO - 2)
    col_shift = offsets[:, 1] + (HALO - 2)
    me = lax.axis_index("exp").astype(jnp.int32).reshape(1)
    lanes = -(-padded.shape[2] // 128) * 128
    rows = -(-padded.shape[1] // 8) * 8
    padded = jnp.pad(
        padded, ((0, 0), (0, rows - padded.shape[1]), (0, lanes - padded.shape[2]))
    )
    smem = pl.BlockSpec(memory_space=pltpu.SMEM)
    vmem = pl.BlockSpec(memory_space=pltpu.VMEM)
    shape = jax.ShapeDtypeStruct((group_size, row_count, col_count), jnp.float32)
    bands = lax.axis_size("exp")
    banded = jax.ShapeDtypeStruct(
        (bands, group_size, row_count // bands, col_count), jnp.float32
    )
    return pl.pallas_call(
        _warp_kernel,
        out_shape=(shape, banded),
        in_specs=[smem, smem, smem, smem, smem, vmem, vmem],
        out_specs=(vmem, vmem),
    )(row_shift, col_shift, row_weight, col_weight, me, padded, bad_pixels)


def _slot_kernel(
    step,
    row_shift,
    col_shift,
    row_weight,
    col_weight,
    me,
    padded,
    bad,
    warped_in,
    warped_out,
    flagged_out,
):
    group_size, band_rows, col_count = flagged_out.shape
    bands = warped_out.shape[1] // band_rows
    width = padded.shape[2]
    window = -(-(band_rows + 2 * HALO) // 8) * 8
    band = lax.rem(me[0] + step, bands)
    base = pl.multiple_of(band * band_rows, 8)

    def one_exposure(e, carry):
        block = pltpu.roll(padded[e, pl.ds(base, window), :], window - row_shift[e], 0)
        across = None
        for tap in range(TAPS):
            term = row_weight[e * TAPS + tap] * block[tap : tap + band_rows, :]
            across = term if across is None else across + term
        across = pltpu.roll(across, width - col_shift[e], 1)
        total = None
        for tap in range(TAPS):
            term = col_weight[e * TAPS + tap] * across[:, tap : tap + col_count]
            total = term if total is None else total + term
        warped_out[e, pl.ds(base, band_rows), :] = total
        flagged = jnp.where(bad[e, pl.ds(base, band_rows), :] == 1, sentinel, total)
        flagged_out[e] = flagged
        return carry

    lax.fori_loop(0, group_size, one_exposure, 0, unroll=True)


def warp_by_slot(padded, bad_pixels, offsets, warp_index):
    group_size, row_count, col_count = bad_pixels.shape
    bands = lax.axis_size("exp")
    band_rows = row_count // bands
    height = -(-padded.shape[1] // 8) * 8
    window = -(-(band_rows + 2 * HALO) // 8) * 8
    if band_rows % 8 or row_count - band_rows + window > height:
        return None
    kernel_table = lanczos_table()
    row_weight = lookup(warp_index[:, 0], NFRAC, kernel_table).reshape(-1)
    col_weight = lookup(warp_index[:, 1], NFRAC, kernel_table).reshape(-1)
    row_shift = offsets[:, 0] + (HALO - 2)
    col_shift = offsets[:, 1] + (HALO - 2)
    me = lax.axis_index("exp").astype(jnp.int32).reshape(1)
    lanes = -(-padded.shape[2] // 128) * 128
    padded = jnp.pad(
        padded, ((0, 0), (0, height - padded.shape[1]), (0, lanes - padded.shape[2]))
    )
    smem = pl.BlockSpec(memory_space=pltpu.SMEM)
    vmem = pl.BlockSpec(memory_space=pltpu.VMEM)
    shape = jax.ShapeDtypeStruct((group_size, row_count, col_count), jnp.float32)
    banded = jax.ShapeDtypeStruct((group_size, band_rows, col_count), jnp.float32)
    warped = jnp.zeros((group_size, row_count, col_count), jnp.float32)
    order = [bands // 2] + [s for s in range(1, bands) if s != bands // 2] + [0]
    slots = {}
    for step in order:
        warped, slots[step] = pl.pallas_call(
            functools.partial(_slot_kernel, step),
            out_shape=(shape, banded),
            in_specs=[smem, smem, smem, smem, smem, vmem, vmem, vmem],
            out_specs=(vmem, vmem),
            input_output_aliases={7: 0},
        )(row_shift, col_shift, row_weight, col_weight, me, padded, bad_pixels, warped)
        if step:
            pairs = [(i, (i + step) % bands) for i in range(bands)]
            slots[step] = lax.ppermute(slots[step], "exp", pairs)
    return warped, jnp.concatenate([slots[s] for s in range(bands)], axis=0)


def body(exposures, bad_pixels, offsets, warp_index, blur_index):
    group_size, row_count, col_count = exposures.shape
    padded = extended(exposures, 1, 2, HALO)
    by_slot = warp_by_slot(padded, bad_pixels, offsets, warp_index)
    groups = lax.axis_size("exp")
    if by_slot is not None:
        warped, stack = by_slot
    else:
        warped, flagged = warp_and_flag(padded, bad_pixels, offsets, warp_index)
        arrived = [flagged[0]]
        for step in range(1, groups):
            pairs = [(i, (i + step) % groups) for i in range(groups)]
            arrived.append(lax.ppermute(flagged[step], "exp", pairs))
        stack = jnp.concatenate(arrived, axis=0)
    band = stack_median(stack)
    groups = lax.axis_size("exp")
    sides = lax.axis_size("col")
    band_rows = band.shape[0]
    full = lax.all_to_all(
        jnp.tile(band, (groups * sides, 1)), ("exp", "col"), split_axis=0, concat_axis=0, tiled=True
    )
    full = full.reshape(groups, sides, band_rows, col_count)
    full = full.transpose(0, 2, 1, 3).reshape(row_count, sides * col_count)
    start = lax.axis_index("col") * col_count
    median_sky = lax.dynamic_slice_in_dim(full, start, col_count, axis=1)
    wide = jnp.pad(full, ((0, 0), (PSF_RADIUS, PSF_RADIUS)))
    wide = lax.dynamic_slice_in_dim(wide, start, col_count + 2 * PSF_RADIUS, axis=1)
    bordered = _row_halo(wide, 0, PSF_RADIUS)
    blur = blur_table()
    taps = 2 * PSF_RADIUS + 1
    blurred_rows = jnp.zeros((NPSF, row_count, col_count + 2 * PSF_RADIUS), jnp.float32)
    for tap_no in range(taps):
        blurred_rows = (
            blurred_rows
            + blur[:, tap_no, None, None] * bordered[None, tap_no : tap_no + row_count, :]
        )
    smoothed = jnp.zeros((NPSF, row_count, col_count), jnp.float32)
    for tap_no in range(taps):
        smoothed = (
            smoothed + blur[:, tap_no, None, None] * blurred_rows[:, :, tap_no : tap_no + col_count]
        )
    chooser = (blur_index[:, None] == lax.broadcasted_iota(jnp.int32, (1, NPSF), 1)).astype(
        jnp.float32
    )
    sky_model = jnp.zeros((group_size, row_count, col_count), jnp.float32)
    for kernel_no in range(NPSF):
        sky_model = sky_model + chooser[:, kernel_no, None, None] * smoothed[kernel_no][None]
    residual = jnp.where(bad_pixels == 1, 0.0, warped - sky_model)
    return (residual, median_sky)


def solution(mesh):
    return jax.shard_map(
        body,
        mesh=mesh,
        in_specs=(
            P("exp", "row", "col"),
            P("exp", "row", "col"),
            P("exp", None),
            P("exp", None),
            P("exp"),
        ),
        out_specs=(P("exp", "row", "col"), P("row", "col")),
        check_vma=False,
    )
```

```python
import functools

import jax
import jax.numpy as jnp
from jax import lax
from jax.sharding import PartitionSpec as P
from jax.experimental import pallas as pl
from jax.experimental.pallas import tpu as pltpu


NFRAC = 16
NPSF = 8
PSF_RADIUS = 4
PASSES = 16
HALO = 11


sentinel = 1000000.0
half_sentinel = 500000.0
pivot_span = 16.0


def _row_halo(block, dim, width):
    count = lax.axis_size("row")
    forward = [(i, i + 1) for i in range(count - 1)]
    backward = [(target, source) for source, target in forward]
    size = block.shape[dim]
    low = lax.ppermute(lax.slice_in_dim(block, size - width, None, axis=dim), "row", forward)
    high = lax.ppermute(lax.slice_in_dim(block, 0, width, axis=dim), "row", backward)
    return jnp.concatenate([low, block, high], axis=dim)


def _col_halo(block, dim, width):
    count = lax.axis_size("col")
    size = block.shape[dim]
    right_edge = lax.slice_in_dim(block, size - width, None, axis=dim)
    left_edge = lax.slice_in_dim(block, 0, width, axis=dim)
    if count != 2:
        forward = [(i, i + 1) for i in range(count - 1)]
        backward = [(target, source) for source, target in forward]
        low = lax.ppermute(right_edge, "col", forward)
        high = lax.ppermute(left_edge, "col", backward)
        return jnp.concatenate([low, block, high], axis=dim)
    first = lax.axis_index("col") == 0
    outgoing = jnp.moveaxis(jnp.where(first, right_edge, left_edge), dim, 0)
    packed_shape = outgoing.shape
    packed = outgoing.reshape(width, -1)
    arrived = lax.ppermute(packed, "col", [(0, 1), (1, 0)])
    arrived = jnp.moveaxis(arrived.reshape(packed_shape), 0, dim)
    zeros = jnp.zeros_like(arrived)
    low = jnp.where(first, zeros, arrived)
    high = jnp.where(first, arrived, zeros)
    return jnp.concatenate([low, block, high], axis=dim)


def extended(block, row_dim, col_dim, width):
    return _col_halo(_row_halo(block, row_dim, width), col_dim, width)


def lanczos_table():
    fraction = jnp.arange(NFRAC, dtype=jnp.float32) / NFRAC
    offset_grid = jnp.arange(-2, 4, dtype=jnp.float32)
    spread = offset_grid[None, :] - fraction[:, None]
    kernel = jnp.sinc(spread) * jnp.sinc(spread / 3.0)
    return kernel / jnp.sum(kernel, axis=1, keepdims=True)


def blur_table():
    offset_grid = jnp.arange(-PSF_RADIUS, PSF_RADIUS + 1, dtype=jnp.float32)
    widths = 0.7 + 0.2 * jnp.arange(NPSF, dtype=jnp.float32)
    kernel = jnp.exp(-0.5 * (offset_grid[None, :] / widths[:, None]) ** 2)
    return kernel / jnp.sum(kernel, axis=1, keepdims=True)


def lookup(indices, entries, kernel_table):
    chooser = (indices[:, None] == lax.broadcasted_iota(jnp.int32, (1, entries), 1)).astype(
        jnp.float32
    )
    return jnp.dot(chooser, kernel_table, precision=lax.Precision.HIGHEST)


def bisect_lower(valid_count, count_below):

    def one_pass(sweep_no, bounds):
        lower_edge, upper_edge = bounds
        middle = 0.5 * (lower_edge + upper_edge)
        enough = 2.0 * count_below(middle) >= valid_count
        return (jnp.where(enough, lower_edge, middle), jnp.where(enough, middle, upper_edge))

    initial = (
        jnp.full(valid_count.shape, -pivot_span, jnp.float32),
        jnp.full(valid_count.shape, pivot_span, jnp.float32),
    )
    return lax.fori_loop(0, PASSES, one_pass, initial)[0]


def stack_median(pixel_stack):
    valid_count = jnp.sum(pixel_stack < half_sentinel, axis=0, dtype=jnp.float32)

    def count_below(middle):
        return jnp.sum(pixel_stack <= middle[None], axis=0, dtype=jnp.float32)

    lower_edge = bisect_lower(valid_count, count_below)
    return jnp.min(jnp.where(pixel_stack > lower_edge[None], pixel_stack, sentinel), axis=0)


TAPS = 6


def _warp_kernel(
    row_shift, col_shift, row_weight, col_weight, me, padded, bad, warped_out, flagged_out
):
    group_size, row_count, col_count = warped_out.shape
    bands, _, band_rows, _ = flagged_out.shape
    width = padded.shape[2]

    height = padded.shape[1]

    def one_exposure(e, carry):
        block = pltpu.roll(padded[e], height - row_shift[e], 0)
        across = None
        for tap in range(TAPS):
            term = row_weight[e * TAPS + tap] * block[tap : tap + row_count, :]
            across = term if across is None else across + term
        across = pltpu.roll(across, width - col_shift[e], 1)
        total = None
        for tap in range(TAPS):
            term = col_weight[e * TAPS + tap] * across[:, tap : tap + col_count]
            total = term if total is None else total + term
        warped_out[e] = total
        flagged = jnp.where(bad[e] == 1, sentinel, total)
        for band in range(bands):
            slot = lax.rem(band - me[0] + bands, bands)
            flagged_out[slot, e] = flagged[band * band_rows : (band + 1) * band_rows]
        return carry

    lax.fori_loop(0, group_size, one_exposure, 0, unroll=True)


def warp_and_flag(padded, bad_pixels, offsets, warp_index):
    group_size, row_count, col_count = bad_pixels.shape
    kernel_table = lanczos_table()
    row_weight = lookup(warp_index[:, 0], NFRAC, kernel_table).reshape(-1)
    col_weight = lookup(warp_index[:, 1], NFRAC, kernel_table).reshape(-1)
    row_shift = offsets[:, 0] + (HALO - 2)
    col_shift = offsets[:, 1] + (HALO - 2)
    me = lax.axis_index("exp").astype(jnp.int32).reshape(1)
    lanes = -(-padded.shape[2] // 128) * 128
    rows = -(-padded.shape[1] // 8) * 8
    padded = jnp.pad(
        padded, ((0, 0), (0, rows - padded.shape[1]), (0, lanes - padded.shape[2]))
    )
    smem = pl.BlockSpec(memory_space=pltpu.SMEM)
    vmem = pl.BlockSpec(memory_space=pltpu.VMEM)
    shape = jax.ShapeDtypeStruct((group_size, row_count, col_count), jnp.float32)
    bands = lax.axis_size("exp")
    banded = jax.ShapeDtypeStruct(
        (bands, group_size, row_count // bands, col_count), jnp.float32
    )
    return pl.pallas_call(
        _warp_kernel,
        out_shape=(shape, banded),
        in_specs=[smem, smem, smem, smem, smem, vmem, vmem],
        out_specs=(vmem, vmem),
    )(row_shift, col_shift, row_weight, col_weight, me, padded, bad_pixels)


def _slot_kernel(
    step,
    row_shift,
    col_shift,
    row_weight,
    col_weight,
    me,
    padded,
    bad,
    warped_out,
    flagged_out,
    window_buf,
    bad_buf,
    sems,
):
    group_size, band_rows, col_count = flagged_out.shape
    bands = bad.shape[1] // band_rows
    width = padded.shape[2]
    window = window_buf.shape[1]
    band = lax.rem(me[0] + step, bands)
    base = pl.multiple_of(band * band_rows, 8)
    fetch_rows = pltpu.make_async_copy(padded.at[:, pl.ds(base, window), :], window_buf, sems.at[0])
    fetch_bad = pltpu.make_async_copy(bad.at[:, pl.ds(base, band_rows), :], bad_buf, sems.at[1])
    fetch_rows.start()
    fetch_bad.start()
    fetch_rows.wait()
    fetch_bad.wait()

    def one_exposure(e, carry):
        block = pltpu.roll(window_buf[e], window - row_shift[e], 0)
        across = None
        for tap in range(TAPS):
            term = row_weight[e * TAPS + tap] * block[tap : tap + band_rows, :]
            across = term if across is None else across + term
        across = pltpu.roll(across, width - col_shift[e], 1)
        total = None
        for tap in range(TAPS):
            term = col_weight[e * TAPS + tap] * across[:, tap : tap + col_count]
            total = term if total is None else total + term
        warped_out[e] = total
        flagged_out[e] = jnp.where(bad_buf[e] == 1, sentinel, total)
        return carry

    lax.fori_loop(0, group_size, one_exposure, 0, unroll=True)


def warp_by_slot(padded, bad_pixels, offsets, warp_index):
    group_size, row_count, col_count = bad_pixels.shape
    bands = lax.axis_size("exp")
    band_rows = row_count // bands
    height = -(-padded.shape[1] // 8) * 8
    window = -(-(band_rows + 2 * HALO) // 8) * 8
    if band_rows % 8 or row_count - band_rows + window > height:
        return None
    kernel_table = lanczos_table()
    row_weight = lookup(warp_index[:, 0], NFRAC, kernel_table).reshape(-1)
    col_weight = lookup(warp_index[:, 1], NFRAC, kernel_table).reshape(-1)
    row_shift = offsets[:, 0] + (HALO - 2)
    col_shift = offsets[:, 1] + (HALO - 2)
    me = lax.axis_index("exp").astype(jnp.int32).reshape(1)
    lanes = -(-padded.shape[2] // 128) * 128
    padded = jnp.pad(
        padded, ((0, 0), (0, height - padded.shape[1]), (0, lanes - padded.shape[2]))
    )
    smem = pl.BlockSpec(memory_space=pltpu.SMEM)
    vmem = pl.BlockSpec(memory_space=pltpu.VMEM)
    anywhere = pl.BlockSpec(memory_space=pl.ANY)
    banded = jax.ShapeDtypeStruct((group_size, band_rows, col_count), jnp.float32)
    order = [bands // 2] + [s for s in range(1, bands) if s != bands // 2] + [0]
    slots = {}
    warped_slots = {}
    for step in order:
        warped_slots[step], flagged = pl.pallas_call(
            functools.partial(_slot_kernel, step),
            out_shape=(banded, banded),
            in_specs=[smem, smem, smem, smem, smem, anywhere, anywhere],
            out_specs=(vmem, vmem),
            scratch_shapes=[
                pltpu.VMEM((group_size, window, lanes), jnp.float32),
                pltpu.VMEM((group_size, band_rows, col_count), jnp.int32),
                pltpu.SemaphoreType.DMA((2,)),
            ],
        )(row_shift, col_shift, row_weight, col_weight, me, padded, bad_pixels)
        if step:
            pairs = [(i, (i + step) % bands) for i in range(bands)]
            slots[step] = lax.ppermute(flagged, "exp", pairs)
        else:
            slots[step] = flagged
    stacked = jnp.stack([warped_slots[s] for s in range(bands)])
    natural = jnp.take(stacked, lax.rem(jnp.arange(bands) - me[0] + bands, bands), axis=0)
    warped = natural.transpose(1, 0, 2, 3).reshape(group_size, row_count, col_count)
    return warped, jnp.concatenate([slots[s] for s in range(bands)], axis=0)


def body(exposures, bad_pixels, offsets, warp_index, blur_index):
    group_size, row_count, col_count = exposures.shape
    padded = extended(exposures, 1, 2, HALO)
    by_slot = warp_by_slot(padded, bad_pixels, offsets, warp_index)
    groups = lax.axis_size("exp")
    if by_slot is not None:
        warped, stack = by_slot
    else:
        warped, flagged = warp_and_flag(padded, bad_pixels, offsets, warp_index)
        arrived = [flagged[0]]
        for step in range(1, groups):
            pairs = [(i, (i + step) % groups) for i in range(groups)]
            arrived.append(lax.ppermute(flagged[step], "exp", pairs))
        stack = jnp.concatenate(arrived, axis=0)
    band = stack_median(stack)
    groups = lax.axis_size("exp")
    sides = lax.axis_size("col")
    band_rows = band.shape[0]
    full = lax.all_to_all(
        jnp.tile(band, (groups * sides, 1)), ("exp", "col"), split_axis=0, concat_axis=0, tiled=True
    )
    full = full.reshape(groups, sides, band_rows, col_count)
    full = full.transpose(0, 2, 1, 3).reshape(row_count, sides * col_count)
    start = lax.axis_index("col") * col_count
    median_sky = lax.dynamic_slice_in_dim(full, start, col_count, axis=1)
    wide = jnp.pad(full, ((0, 0), (PSF_RADIUS, PSF_RADIUS)))
    wide = lax.dynamic_slice_in_dim(wide, start, col_count + 2 * PSF_RADIUS, axis=1)
    bordered = _row_halo(wide, 0, PSF_RADIUS)
    blur = blur_table()
    taps = 2 * PSF_RADIUS + 1
    blurred_rows = jnp.zeros((NPSF, row_count, col_count + 2 * PSF_RADIUS), jnp.float32)
    for tap_no in range(taps):
        blurred_rows = (
            blurred_rows
            + blur[:, tap_no, None, None] * bordered[None, tap_no : tap_no + row_count, :]
        )
    smoothed = jnp.zeros((NPSF, row_count, col_count), jnp.float32)
    for tap_no in range(taps):
        smoothed = (
            smoothed + blur[:, tap_no, None, None] * blurred_rows[:, :, tap_no : tap_no + col_count]
        )
    chooser = (blur_index[:, None] == lax.broadcasted_iota(jnp.int32, (1, NPSF), 1)).astype(
        jnp.float32
    )
    sky_model = jnp.zeros((group_size, row_count, col_count), jnp.float32)
    for kernel_no in range(NPSF):
        sky_model = sky_model + chooser[:, kernel_no, None, None] * smoothed[kernel_no][None]
    residual = jnp.where(bad_pixels == 1, 0.0, warped - sky_model)
    return (residual, median_sky)


def solution(mesh):
    return jax.shard_map(
        body,
        mesh=mesh,
        in_specs=(
            P("exp", "row", "col"),
            P("exp", "row", "col"),
            P("exp", None),
            P("exp", None),
            P("exp"),
        ),
        out_specs=(P("exp", "row", "col"), P("row", "col")),
        check_vma=False,
    )
```

```python
import functools

import jax
import jax.numpy as jnp
from jax import lax
from jax.sharding import PartitionSpec as P
from jax.experimental import pallas as pl
from jax.experimental.pallas import tpu as pltpu


NFRAC = 16
NPSF = 8
PSF_RADIUS = 4
PASSES = 16
HALO = 11


sentinel = 1000000.0
half_sentinel = 500000.0
pivot_span = 16.0


def _row_halo(block, dim, width):
    count = lax.axis_size("row")
    forward = [(i, i + 1) for i in range(count - 1)]
    backward = [(target, source) for source, target in forward]
    size = block.shape[dim]
    low = lax.ppermute(lax.slice_in_dim(block, size - width, None, axis=dim), "row", forward)
    high = lax.ppermute(lax.slice_in_dim(block, 0, width, axis=dim), "row", backward)
    return jnp.concatenate([low, block, high], axis=dim)


def _col_halo(block, dim, width):
    count = lax.axis_size("col")
    size = block.shape[dim]
    right_edge = lax.slice_in_dim(block, size - width, None, axis=dim)
    left_edge = lax.slice_in_dim(block, 0, width, axis=dim)
    if count != 2:
        forward = [(i, i + 1) for i in range(count - 1)]
        backward = [(target, source) for source, target in forward]
        low = lax.ppermute(right_edge, "col", forward)
        high = lax.ppermute(left_edge, "col", backward)
        return jnp.concatenate([low, block, high], axis=dim)
    first = lax.axis_index("col") == 0
    outgoing = jnp.moveaxis(jnp.where(first, right_edge, left_edge), dim, 0)
    packed_shape = outgoing.shape
    packed = outgoing.reshape(width, -1)
    arrived = lax.ppermute(packed, "col", [(0, 1), (1, 0)])
    arrived = jnp.moveaxis(arrived.reshape(packed_shape), 0, dim)
    zeros = jnp.zeros_like(arrived)
    low = jnp.where(first, zeros, arrived)
    high = jnp.where(first, arrived, zeros)
    return jnp.concatenate([low, block, high], axis=dim)


def extended(block, row_dim, col_dim, width):
    return _col_halo(_row_halo(block, row_dim, width), col_dim, width)


def lanczos_table():
    fraction = jnp.arange(NFRAC, dtype=jnp.float32) / NFRAC
    offset_grid = jnp.arange(-2, 4, dtype=jnp.float32)
    spread = offset_grid[None, :] - fraction[:, None]
    kernel = jnp.sinc(spread) * jnp.sinc(spread / 3.0)
    return kernel / jnp.sum(kernel, axis=1, keepdims=True)


def blur_table():
    offset_grid = jnp.arange(-PSF_RADIUS, PSF_RADIUS + 1, dtype=jnp.float32)
    widths = 0.7 + 0.2 * jnp.arange(NPSF, dtype=jnp.float32)
    kernel = jnp.exp(-0.5 * (offset_grid[None, :] / widths[:, None]) ** 2)
    return kernel / jnp.sum(kernel, axis=1, keepdims=True)


def lookup(indices, entries, kernel_table):
    chooser = (indices[:, None] == lax.broadcasted_iota(jnp.int32, (1, entries), 1)).astype(
        jnp.float32
    )
    return jnp.dot(chooser, kernel_table, precision=lax.Precision.HIGHEST)


def bisect_lower(valid_count, count_below):

    def one_pass(sweep_no, bounds):
        lower_edge, upper_edge = bounds
        middle = 0.5 * (lower_edge + upper_edge)
        enough = 2.0 * count_below(middle) >= valid_count
        return (jnp.where(enough, lower_edge, middle), jnp.where(enough, middle, upper_edge))

    initial = (
        jnp.full(valid_count.shape, -pivot_span, jnp.float32),
        jnp.full(valid_count.shape, pivot_span, jnp.float32),
    )
    return lax.fori_loop(0, PASSES, one_pass, initial)[0]


def stack_median(pixel_stack):
    valid_count = jnp.sum(pixel_stack < half_sentinel, axis=0, dtype=jnp.float32)

    def count_below(middle):
        return jnp.sum(pixel_stack <= middle[None], axis=0, dtype=jnp.float32)

    lower_edge = bisect_lower(valid_count, count_below)
    return jnp.min(jnp.where(pixel_stack > lower_edge[None], pixel_stack, sentinel), axis=0)


TAPS = 6


def _warp_kernel(
    row_shift, col_shift, row_weight, col_weight, me, padded, bad, warped_out, flagged_out
):
    group_size, row_count, col_count = warped_out.shape
    bands, _, band_rows, _ = flagged_out.shape
    width = padded.shape[2]

    height = padded.shape[1]

    def one_exposure(e, carry):
        block = pltpu.roll(padded[e], height - row_shift[e], 0)
        across = None
        for tap in range(TAPS):
            term = row_weight[e * TAPS + tap] * block[tap : tap + row_count, :]
            across = term if across is None else across + term
        across = pltpu.roll(across, width - col_shift[e], 1)
        total = None
        for tap in range(TAPS):
            term = col_weight[e * TAPS + tap] * across[:, tap : tap + col_count]
            total = term if total is None else total + term
        warped_out[e] = total
        flagged = jnp.where(bad[e] == 1, sentinel, total)
        for band in range(bands):
            slot = lax.rem(band - me[0] + bands, bands)
            flagged_out[slot, e] = flagged[band * band_rows : (band + 1) * band_rows]
        return carry

    lax.fori_loop(0, group_size, one_exposure, 0, unroll=True)


def warp_and_flag(padded, bad_pixels, offsets, warp_index):
    group_size, row_count, col_count = bad_pixels.shape
    kernel_table = lanczos_table()
    row_weight = lookup(warp_index[:, 0], NFRAC, kernel_table).reshape(-1)
    col_weight = lookup(warp_index[:, 1], NFRAC, kernel_table).reshape(-1)
    row_shift = offsets[:, 0] + (HALO - 2)
    col_shift = offsets[:, 1] + (HALO - 2)
    me = lax.axis_index("exp").astype(jnp.int32).reshape(1)
    lanes = -(-padded.shape[2] // 128) * 128
    rows = -(-padded.shape[1] // 8) * 8
    padded = jnp.pad(
        padded, ((0, 0), (0, rows - padded.shape[1]), (0, lanes - padded.shape[2]))
    )
    smem = pl.BlockSpec(memory_space=pltpu.SMEM)
    vmem = pl.BlockSpec(memory_space=pltpu.VMEM)
    shape = jax.ShapeDtypeStruct((group_size, row_count, col_count), jnp.float32)
    bands = lax.axis_size("exp")
    banded = jax.ShapeDtypeStruct(
        (bands, group_size, row_count // bands, col_count), jnp.float32
    )
    return pl.pallas_call(
        _warp_kernel,
        out_shape=(shape, banded),
        in_specs=[smem, smem, smem, smem, smem, vmem, vmem],
        out_specs=(vmem, vmem),
    )(row_shift, col_shift, row_weight, col_weight, me, padded, bad_pixels)


def _slot_kernel(
    step,
    row_shift,
    col_shift,
    row_weight,
    col_weight,
    me,
    padded,
    bad,
    warped_out,
    flagged_out,
    window_buf,
    bad_buf,
    sems,
):
    group_size, band_rows, col_count = flagged_out.shape
    bands = bad.shape[1] // band_rows
    width = padded.shape[2]
    window = window_buf.shape[1]
    band = lax.rem(me[0] + step, bands)
    base = pl.multiple_of(band * band_rows, 8)
    fetch_bad = pltpu.make_async_copy(bad.at[:, pl.ds(base, band_rows), :], bad_buf, sems.at[2])

    def fetch(e):
        return pltpu.make_async_copy(
            padded.at[e, pl.ds(base, window), :], window_buf.at[e % 2], sems.at[e % 2]
        )

    fetch(0).start()
    fetch_bad.start()
    fetch_bad.wait()
    for e in range(group_size):
        if e + 1 < group_size:
            fetch(e + 1).start()
        fetch(e).wait()
        block = pltpu.roll(window_buf[e % 2], window - row_shift[e], 0)
        across = None
        for tap in range(TAPS):
            term = row_weight[e * TAPS + tap] * block[tap : tap + band_rows, :]
            across = term if across is None else across + term
        across = pltpu.roll(across, width - col_shift[e], 1)
        total = None
        for tap in range(TAPS):
            term = col_weight[e * TAPS + tap] * across[:, tap : tap + col_count]
            total = term if total is None else total + term
        warped_out[e] = total
        flagged_out[e] = jnp.where(bad_buf[e] == 1, sentinel, total)


def warp_by_slot(padded, bad_pixels, offsets, warp_index):
    group_size, row_count, col_count = bad_pixels.shape
    bands = lax.axis_size("exp")
    band_rows = row_count // bands
    height = -(-padded.shape[1] // 8) * 8
    window = -(-(band_rows + 2 * HALO) // 8) * 8
    if band_rows % 8 or row_count - band_rows + window > height:
        return None
    kernel_table = lanczos_table()
    row_weight = lookup(warp_index[:, 0], NFRAC, kernel_table).reshape(-1)
    col_weight = lookup(warp_index[:, 1], NFRAC, kernel_table).reshape(-1)
    row_shift = offsets[:, 0] + (HALO - 2)
    col_shift = offsets[:, 1] + (HALO - 2)
    me = lax.axis_index("exp").astype(jnp.int32).reshape(1)
    lanes = -(-padded.shape[2] // 128) * 128
    padded = jnp.pad(
        padded, ((0, 0), (0, height - padded.shape[1]), (0, lanes - padded.shape[2]))
    )
    smem = pl.BlockSpec(memory_space=pltpu.SMEM)
    vmem = pl.BlockSpec(memory_space=pltpu.VMEM)
    anywhere = pl.BlockSpec(memory_space=pl.ANY)
    banded = jax.ShapeDtypeStruct((group_size, band_rows, col_count), jnp.float32)
    order = [bands // 2] + [s for s in range(1, bands) if s != bands // 2] + [0]
    slots = {}
    warped_slots = {}
    for step in order:
        warped_slots[step], flagged = pl.pallas_call(
            functools.partial(_slot_kernel, step),
            out_shape=(banded, banded),
            in_specs=[smem, smem, smem, smem, smem, anywhere, anywhere],
            out_specs=(vmem, vmem),
            scratch_shapes=[
                pltpu.VMEM((2, window, lanes), jnp.float32),
                pltpu.VMEM((group_size, band_rows, col_count), jnp.int32),
                pltpu.SemaphoreType.DMA((3,)),
            ],
        )(row_shift, col_shift, row_weight, col_weight, me, padded, bad_pixels)
        if step:
            pairs = [(i, (i + step) % bands) for i in range(bands)]
            slots[step] = lax.ppermute(flagged, "exp", pairs)
        else:
            slots[step] = flagged
    stacked = jnp.stack([warped_slots[s] for s in range(bands)])
    natural = jnp.take(stacked, lax.rem(jnp.arange(bands) - me[0] + bands, bands), axis=0)
    warped = natural.transpose(1, 0, 2, 3).reshape(group_size, row_count, col_count)
    return warped, jnp.concatenate([slots[s] for s in range(bands)], axis=0)


def body(exposures, bad_pixels, offsets, warp_index, blur_index):
    group_size, row_count, col_count = exposures.shape
    padded = extended(exposures, 1, 2, HALO)
    by_slot = warp_by_slot(padded, bad_pixels, offsets, warp_index)
    groups = lax.axis_size("exp")
    if by_slot is not None:
        warped, stack = by_slot
    else:
        warped, flagged = warp_and_flag(padded, bad_pixels, offsets, warp_index)
        arrived = [flagged[0]]
        for step in range(1, groups):
            pairs = [(i, (i + step) % groups) for i in range(groups)]
            arrived.append(lax.ppermute(flagged[step], "exp", pairs))
        stack = jnp.concatenate(arrived, axis=0)
    band = stack_median(stack)
    groups = lax.axis_size("exp")
    sides = lax.axis_size("col")
    band_rows = band.shape[0]
    full = lax.all_to_all(
        jnp.tile(band, (groups * sides, 1)), ("exp", "col"), split_axis=0, concat_axis=0, tiled=True
    )
    full = full.reshape(groups, sides, band_rows, col_count)
    full = full.transpose(0, 2, 1, 3).reshape(row_count, sides * col_count)
    start = lax.axis_index("col") * col_count
    median_sky = lax.dynamic_slice_in_dim(full, start, col_count, axis=1)
    wide = jnp.pad(full, ((0, 0), (PSF_RADIUS, PSF_RADIUS)))
    wide = lax.dynamic_slice_in_dim(wide, start, col_count + 2 * PSF_RADIUS, axis=1)
    bordered = _row_halo(wide, 0, PSF_RADIUS)
    blur = blur_table()
    taps = 2 * PSF_RADIUS + 1
    blurred_rows = jnp.zeros((NPSF, row_count, col_count + 2 * PSF_RADIUS), jnp.float32)
    for tap_no in range(taps):
        blurred_rows = (
            blurred_rows
            + blur[:, tap_no, None, None] * bordered[None, tap_no : tap_no + row_count, :]
        )
    smoothed = jnp.zeros((NPSF, row_count, col_count), jnp.float32)
    for tap_no in range(taps):
        smoothed = (
            smoothed + blur[:, tap_no, None, None] * blurred_rows[:, :, tap_no : tap_no + col_count]
        )
    chooser = (blur_index[:, None] == lax.broadcasted_iota(jnp.int32, (1, NPSF), 1)).astype(
        jnp.float32
    )
    sky_model = jnp.zeros((group_size, row_count, col_count), jnp.float32)
    for kernel_no in range(NPSF):
        sky_model = sky_model + chooser[:, kernel_no, None, None] * smoothed[kernel_no][None]
    residual = jnp.where(bad_pixels == 1, 0.0, warped - sky_model)
    return (residual, median_sky)


def solution(mesh):
    return jax.shard_map(
        body,
        mesh=mesh,
        in_specs=(
            P("exp", "row", "col"),
            P("exp", "row", "col"),
            P("exp", None),
            P("exp", None),
            P("exp"),
        ),
        out_specs=(P("exp", "row", "col"), P("row", "col")),
        check_vma=False,
    )
```

```python
import functools

import jax
import jax.numpy as jnp
from jax import lax
from jax.sharding import PartitionSpec as P
from jax.experimental import pallas as pl
from jax.experimental.pallas import tpu as pltpu


NFRAC = 16
NPSF = 8
PSF_RADIUS = 4
PASSES = 16
HALO = 11


sentinel = 1000000.0
half_sentinel = 500000.0
pivot_span = 16.0


def _row_halo(block, dim, width):
    count = lax.axis_size("row")
    forward = [(i, i + 1) for i in range(count - 1)]
    backward = [(target, source) for source, target in forward]
    size = block.shape[dim]
    low = lax.ppermute(lax.slice_in_dim(block, size - width, None, axis=dim), "row", forward)
    high = lax.ppermute(lax.slice_in_dim(block, 0, width, axis=dim), "row", backward)
    return jnp.concatenate([low, block, high], axis=dim)


def _col_halo(block, dim, width):
    count = lax.axis_size("col")
    size = block.shape[dim]
    right_edge = lax.slice_in_dim(block, size - width, None, axis=dim)
    left_edge = lax.slice_in_dim(block, 0, width, axis=dim)
    if count != 2:
        forward = [(i, i + 1) for i in range(count - 1)]
        backward = [(target, source) for source, target in forward]
        low = lax.ppermute(right_edge, "col", forward)
        high = lax.ppermute(left_edge, "col", backward)
        return jnp.concatenate([low, block, high], axis=dim)
    first = lax.axis_index("col") == 0
    outgoing = jnp.moveaxis(jnp.where(first, right_edge, left_edge), dim, 0)
    packed_shape = outgoing.shape
    packed = outgoing.reshape(width, -1)
    arrived = lax.ppermute(packed, "col", [(0, 1), (1, 0)])
    arrived = jnp.moveaxis(arrived.reshape(packed_shape), 0, dim)
    zeros = jnp.zeros_like(arrived)
    low = jnp.where(first, zeros, arrived)
    high = jnp.where(first, arrived, zeros)
    return jnp.concatenate([low, block, high], axis=dim)


def extended(block, row_dim, col_dim, width):
    return _col_halo(_row_halo(block, row_dim, width), col_dim, width)


def lanczos_table():
    fraction = jnp.arange(NFRAC, dtype=jnp.float32) / NFRAC
    offset_grid = jnp.arange(-2, 4, dtype=jnp.float32)
    spread = offset_grid[None, :] - fraction[:, None]
    kernel = jnp.sinc(spread) * jnp.sinc(spread / 3.0)
    return kernel / jnp.sum(kernel, axis=1, keepdims=True)


def blur_table():
    offset_grid = jnp.arange(-PSF_RADIUS, PSF_RADIUS + 1, dtype=jnp.float32)
    widths = 0.7 + 0.2 * jnp.arange(NPSF, dtype=jnp.float32)
    kernel = jnp.exp(-0.5 * (offset_grid[None, :] / widths[:, None]) ** 2)
    return kernel / jnp.sum(kernel, axis=1, keepdims=True)


def lookup(indices, entries, kernel_table):
    chooser = (indices[:, None] == lax.broadcasted_iota(jnp.int32, (1, entries), 1)).astype(
        jnp.float32
    )
    return jnp.dot(chooser, kernel_table, precision=lax.Precision.HIGHEST)


def bisect_lower(valid_count, count_below):

    def one_pass(sweep_no, bounds):
        lower_edge, upper_edge = bounds
        middle = 0.5 * (lower_edge + upper_edge)
        enough = 2.0 * count_below(middle) >= valid_count
        return (jnp.where(enough, lower_edge, middle), jnp.where(enough, middle, upper_edge))

    initial = (
        jnp.full(valid_count.shape, -pivot_span, jnp.float32),
        jnp.full(valid_count.shape, pivot_span, jnp.float32),
    )
    return lax.fori_loop(0, PASSES, one_pass, initial)[0]


def stack_median(pixel_stack):
    valid_count = jnp.sum(pixel_stack < half_sentinel, axis=0, dtype=jnp.float32)

    def count_below(middle):
        return jnp.sum(pixel_stack <= middle[None], axis=0, dtype=jnp.float32)

    lower_edge = bisect_lower(valid_count, count_below)
    return jnp.min(jnp.where(pixel_stack > lower_edge[None], pixel_stack, sentinel), axis=0)


TAPS = 6


def _warp_kernel(
    row_shift, col_shift, row_weight, col_weight, me, padded, bad, warped_out, flagged_out
):
    group_size, row_count, col_count = warped_out.shape
    bands, _, band_rows, _ = flagged_out.shape
    width = padded.shape[2]

    height = padded.shape[1]

    def one_exposure(e, carry):
        block = pltpu.roll(padded[e], height - row_shift[e], 0)
        across = None
        for tap in range(TAPS):
            term = row_weight[e * TAPS + tap] * block[tap : tap + row_count, :]
            across = term if across is None else across + term
        across = pltpu.roll(across, width - col_shift[e], 1)
        total = None
        for tap in range(TAPS):
            term = col_weight[e * TAPS + tap] * across[:, tap : tap + col_count]
            total = term if total is None else total + term
        warped_out[e] = total
        flagged = jnp.where(bad[e] == 1, sentinel, total)
        for band in range(bands):
            slot = lax.rem(band - me[0] + bands, bands)
            flagged_out[slot, e] = flagged[band * band_rows : (band + 1) * band_rows]
        return carry

    lax.fori_loop(0, group_size, one_exposure, 0, unroll=True)


def warp_and_flag(padded, bad_pixels, offsets, warp_index):
    group_size, row_count, col_count = bad_pixels.shape
    kernel_table = lanczos_table()
    row_weight = lookup(warp_index[:, 0], NFRAC, kernel_table).reshape(-1)
    col_weight = lookup(warp_index[:, 1], NFRAC, kernel_table).reshape(-1)
    row_shift = offsets[:, 0] + (HALO - 2)
    col_shift = offsets[:, 1] + (HALO - 2)
    me = lax.axis_index("exp").astype(jnp.int32).reshape(1)
    lanes = -(-padded.shape[2] // 128) * 128
    rows = -(-padded.shape[1] // 8) * 8
    padded = jnp.pad(
        padded, ((0, 0), (0, rows - padded.shape[1]), (0, lanes - padded.shape[2]))
    )
    smem = pl.BlockSpec(memory_space=pltpu.SMEM)
    vmem = pl.BlockSpec(memory_space=pltpu.VMEM)
    shape = jax.ShapeDtypeStruct((group_size, row_count, col_count), jnp.float32)
    bands = lax.axis_size("exp")
    banded = jax.ShapeDtypeStruct(
        (bands, group_size, row_count // bands, col_count), jnp.float32
    )
    return pl.pallas_call(
        _warp_kernel,
        out_shape=(shape, banded),
        in_specs=[smem, smem, smem, smem, smem, vmem, vmem],
        out_specs=(vmem, vmem),
    )(row_shift, col_shift, row_weight, col_weight, me, padded, bad_pixels)


def _slot_kernel(
    step,
    row_shift,
    col_shift,
    row_weight,
    col_weight,
    me,
    padded,
    bad,
    warped_out,
    flagged_out,
    window_buf,
    bad_buf,
    sems,
):
    group_size, band_rows, col_count = flagged_out.shape
    bands = bad.shape[1] // band_rows
    width = padded.shape[2]
    window = window_buf.shape[1]
    band = lax.rem(me[0] + step, bands)
    base = pl.multiple_of(band * band_rows, 8)
    fetch_bad = pltpu.make_async_copy(
        bad.at[:, pl.ds(base, band_rows), :], bad_buf, sems.at[group_size]
    )
    fetches = [
        pltpu.make_async_copy(
            padded.at[e, pl.ds(base, window), :], window_buf.at[e], sems.at[e]
        )
        for e in range(group_size)
    ]
    for fetch in fetches:
        fetch.start()
    fetch_bad.start()
    fetch_bad.wait()
    for e in range(group_size):
        fetches[e].wait()
        block = pltpu.roll(window_buf[e], window - row_shift[e], 0)
        across = None
        for tap in range(TAPS):
            term = row_weight[e * TAPS + tap] * block[tap : tap + band_rows, :]
            across = term if across is None else across + term
        across = pltpu.roll(across, width - col_shift[e], 1)
        total = None
        for tap in range(TAPS):
            term = col_weight[e * TAPS + tap] * across[:, tap : tap + col_count]
            total = term if total is None else total + term
        warped_out[e] = total
        flagged_out[e] = jnp.where(bad_buf[e] == 1, sentinel, total)


def warp_by_slot(padded, bad_pixels, offsets, warp_index):
    group_size, row_count, col_count = bad_pixels.shape
    bands = lax.axis_size("exp")
    band_rows = row_count // bands
    height = -(-padded.shape[1] // 8) * 8
    window = -(-(band_rows + 2 * HALO) // 8) * 8
    if band_rows % 8 or row_count - band_rows + window > height:
        return None
    kernel_table = lanczos_table()
    row_weight = lookup(warp_index[:, 0], NFRAC, kernel_table).reshape(-1)
    col_weight = lookup(warp_index[:, 1], NFRAC, kernel_table).reshape(-1)
    row_shift = offsets[:, 0] + (HALO - 2)
    col_shift = offsets[:, 1] + (HALO - 2)
    me = lax.axis_index("exp").astype(jnp.int32).reshape(1)
    lanes = -(-padded.shape[2] // 128) * 128
    padded = jnp.pad(
        padded, ((0, 0), (0, height - padded.shape[1]), (0, lanes - padded.shape[2]))
    )
    smem = pl.BlockSpec(memory_space=pltpu.SMEM)
    vmem = pl.BlockSpec(memory_space=pltpu.VMEM)
    anywhere = pl.BlockSpec(memory_space=pl.ANY)
    banded = jax.ShapeDtypeStruct((group_size, band_rows, col_count), jnp.float32)
    order = [bands // 2] + [s for s in range(1, bands) if s != bands // 2] + [0]
    slots = {}
    warped_slots = {}
    for step in order:
        warped_slots[step], flagged = pl.pallas_call(
            functools.partial(_slot_kernel, step),
            out_shape=(banded, banded),
            in_specs=[smem, smem, smem, smem, smem, anywhere, anywhere],
            out_specs=(vmem, vmem),
            scratch_shapes=[
                pltpu.VMEM((group_size, window, lanes), jnp.float32),
                pltpu.VMEM((group_size, band_rows, col_count), jnp.int32),
                pltpu.SemaphoreType.DMA((group_size + 1,)),
            ],
        )(row_shift, col_shift, row_weight, col_weight, me, padded, bad_pixels)
        if step:
            pairs = [(i, (i + step) % bands) for i in range(bands)]
            slots[step] = lax.ppermute(flagged, "exp", pairs)
        else:
            slots[step] = flagged
    stacked = jnp.stack([warped_slots[s] for s in range(bands)])
    natural = jnp.take(stacked, lax.rem(jnp.arange(bands) - me[0] + bands, bands), axis=0)
    warped = natural.transpose(1, 0, 2, 3).reshape(group_size, row_count, col_count)
    return warped, jnp.concatenate([slots[s] for s in range(bands)], axis=0)


def body(exposures, bad_pixels, offsets, warp_index, blur_index):
    group_size, row_count, col_count = exposures.shape
    padded = extended(exposures, 1, 2, HALO)
    by_slot = warp_by_slot(padded, bad_pixels, offsets, warp_index)
    groups = lax.axis_size("exp")
    if by_slot is not None:
        warped, stack = by_slot
    else:
        warped, flagged = warp_and_flag(padded, bad_pixels, offsets, warp_index)
        arrived = [flagged[0]]
        for step in range(1, groups):
            pairs = [(i, (i + step) % groups) for i in range(groups)]
            arrived.append(lax.ppermute(flagged[step], "exp", pairs))
        stack = jnp.concatenate(arrived, axis=0)
    band = stack_median(stack)
    groups = lax.axis_size("exp")
    sides = lax.axis_size("col")
    band_rows = band.shape[0]
    full = lax.all_to_all(
        jnp.tile(band, (groups * sides, 1)), ("exp", "col"), split_axis=0, concat_axis=0, tiled=True
    )
    full = full.reshape(groups, sides, band_rows, col_count)
    full = full.transpose(0, 2, 1, 3).reshape(row_count, sides * col_count)
    start = lax.axis_index("col") * col_count
    median_sky = lax.dynamic_slice_in_dim(full, start, col_count, axis=1)
    wide = jnp.pad(full, ((0, 0), (PSF_RADIUS, PSF_RADIUS)))
    wide = lax.dynamic_slice_in_dim(wide, start, col_count + 2 * PSF_RADIUS, axis=1)
    bordered = _row_halo(wide, 0, PSF_RADIUS)
    blur = blur_table()
    taps = 2 * PSF_RADIUS + 1
    blurred_rows = jnp.zeros((NPSF, row_count, col_count + 2 * PSF_RADIUS), jnp.float32)
    for tap_no in range(taps):
        blurred_rows = (
            blurred_rows
            + blur[:, tap_no, None, None] * bordered[None, tap_no : tap_no + row_count, :]
        )
    smoothed = jnp.zeros((NPSF, row_count, col_count), jnp.float32)
    for tap_no in range(taps):
        smoothed = (
            smoothed + blur[:, tap_no, None, None] * blurred_rows[:, :, tap_no : tap_no + col_count]
        )
    chooser = (blur_index[:, None] == lax.broadcasted_iota(jnp.int32, (1, NPSF), 1)).astype(
        jnp.float32
    )
    sky_model = jnp.zeros((group_size, row_count, col_count), jnp.float32)
    for kernel_no in range(NPSF):
        sky_model = sky_model + chooser[:, kernel_no, None, None] * smoothed[kernel_no][None]
    residual = jnp.where(bad_pixels == 1, 0.0, warped - sky_model)
    return (residual, median_sky)


def solution(mesh):
    return jax.shard_map(
        body,
        mesh=mesh,
        in_specs=(
            P("exp", "row", "col"),
            P("exp", "row", "col"),
            P("exp", None),
            P("exp", None),
            P("exp"),
        ),
        out_specs=(P("exp", "row", "col"), P("row", "col")),
        check_vma=False,
    )
```

```python
import functools

import jax
import jax.numpy as jnp
from jax import lax
from jax.sharding import PartitionSpec as P
from jax.experimental import pallas as pl
from jax.experimental.pallas import tpu as pltpu


NFRAC = 16
NPSF = 8
PSF_RADIUS = 4
PASSES = 16
HALO = 11


sentinel = 1000000.0
half_sentinel = 500000.0
pivot_span = 16.0


def _row_halo(block, dim, width):
    count = lax.axis_size("row")
    forward = [(i, i + 1) for i in range(count - 1)]
    backward = [(target, source) for source, target in forward]
    size = block.shape[dim]
    low = lax.ppermute(lax.slice_in_dim(block, size - width, None, axis=dim), "row", forward)
    high = lax.ppermute(lax.slice_in_dim(block, 0, width, axis=dim), "row", backward)
    return jnp.concatenate([low, block, high], axis=dim)


def _col_halo(block, dim, width):
    count = lax.axis_size("col")
    size = block.shape[dim]
    right_edge = lax.slice_in_dim(block, size - width, None, axis=dim)
    left_edge = lax.slice_in_dim(block, 0, width, axis=dim)
    if count != 2:
        forward = [(i, i + 1) for i in range(count - 1)]
        backward = [(target, source) for source, target in forward]
        low = lax.ppermute(right_edge, "col", forward)
        high = lax.ppermute(left_edge, "col", backward)
        return jnp.concatenate([low, block, high], axis=dim)
    first = lax.axis_index("col") == 0
    outgoing = jnp.moveaxis(jnp.where(first, right_edge, left_edge), dim, 0)
    packed_shape = outgoing.shape
    packed = outgoing.reshape(width, -1)
    arrived = lax.ppermute(packed, "col", [(0, 1), (1, 0)])
    arrived = jnp.moveaxis(arrived.reshape(packed_shape), 0, dim)
    zeros = jnp.zeros_like(arrived)
    low = jnp.where(first, zeros, arrived)
    high = jnp.where(first, arrived, zeros)
    return jnp.concatenate([low, block, high], axis=dim)


def extended(block, row_dim, col_dim, width):
    return _col_halo(_row_halo(block, row_dim, width), col_dim, width)


def lanczos_table():
    fraction = jnp.arange(NFRAC, dtype=jnp.float32) / NFRAC
    offset_grid = jnp.arange(-2, 4, dtype=jnp.float32)
    spread = offset_grid[None, :] - fraction[:, None]
    kernel = jnp.sinc(spread) * jnp.sinc(spread / 3.0)
    return kernel / jnp.sum(kernel, axis=1, keepdims=True)


def blur_table():
    offset_grid = jnp.arange(-PSF_RADIUS, PSF_RADIUS + 1, dtype=jnp.float32)
    widths = 0.7 + 0.2 * jnp.arange(NPSF, dtype=jnp.float32)
    kernel = jnp.exp(-0.5 * (offset_grid[None, :] / widths[:, None]) ** 2)
    return kernel / jnp.sum(kernel, axis=1, keepdims=True)


def lookup(indices, entries, kernel_table):
    chooser = (indices[:, None] == lax.broadcasted_iota(jnp.int32, (1, entries), 1)).astype(
        jnp.float32
    )
    return jnp.dot(chooser, kernel_table, precision=lax.Precision.HIGHEST)


def bisect_lower(valid_count, count_below):

    def one_pass(sweep_no, bounds):
        lower_edge, upper_edge = bounds
        middle = 0.5 * (lower_edge + upper_edge)
        enough = 2.0 * count_below(middle) >= valid_count
        return (jnp.where(enough, lower_edge, middle), jnp.where(enough, middle, upper_edge))

    initial = (
        jnp.full(valid_count.shape, -pivot_span, jnp.float32),
        jnp.full(valid_count.shape, pivot_span, jnp.float32),
    )
    return lax.fori_loop(0, PASSES, one_pass, initial)[0]


def stack_median(pixel_stack):
    valid_count = jnp.sum(pixel_stack < half_sentinel, axis=0, dtype=jnp.float32)

    def count_below(middle):
        return jnp.sum(pixel_stack <= middle[None], axis=0, dtype=jnp.float32)

    lower_edge = bisect_lower(valid_count, count_below)
    return jnp.min(jnp.where(pixel_stack > lower_edge[None], pixel_stack, sentinel), axis=0)


TAPS = 6


def _warp_kernel(
    row_shift, col_shift, row_weight, col_weight, me, padded, bad, warped_out, flagged_out
):
    group_size, row_count, col_count = warped_out.shape
    bands, _, band_rows, _ = flagged_out.shape
    width = padded.shape[2]

    height = padded.shape[1]

    def one_exposure(e, carry):
        block = pltpu.roll(padded[e], height - row_shift[e], 0)
        across = None
        for tap in range(TAPS):
            term = row_weight[e * TAPS + tap] * block[tap : tap + row_count, :]
            across = term if across is None else across + term
        across = pltpu.roll(across, width - col_shift[e], 1)
        total = None
        for tap in range(TAPS):
            term = col_weight[e * TAPS + tap] * across[:, tap : tap + col_count]
            total = term if total is None else total + term
        warped_out[e] = total
        flagged = jnp.where(bad[e] == 1, sentinel, total)
        for band in range(bands):
            slot = lax.rem(band - me[0] + bands, bands)
            flagged_out[slot, e] = flagged[band * band_rows : (band + 1) * band_rows]
        return carry

    lax.fori_loop(0, group_size, one_exposure, 0, unroll=True)


def warp_and_flag(padded, bad_pixels, offsets, warp_index):
    group_size, row_count, col_count = bad_pixels.shape
    kernel_table = lanczos_table()
    row_weight = lookup(warp_index[:, 0], NFRAC, kernel_table).reshape(-1)
    col_weight = lookup(warp_index[:, 1], NFRAC, kernel_table).reshape(-1)
    row_shift = offsets[:, 0] + (HALO - 2)
    col_shift = offsets[:, 1] + (HALO - 2)
    me = lax.axis_index("exp").astype(jnp.int32).reshape(1)
    lanes = -(-padded.shape[2] // 128) * 128
    rows = -(-padded.shape[1] // 8) * 8
    padded = jnp.pad(
        padded, ((0, 0), (0, rows - padded.shape[1]), (0, lanes - padded.shape[2]))
    )
    smem = pl.BlockSpec(memory_space=pltpu.SMEM)
    vmem = pl.BlockSpec(memory_space=pltpu.VMEM)
    shape = jax.ShapeDtypeStruct((group_size, row_count, col_count), jnp.float32)
    bands = lax.axis_size("exp")
    banded = jax.ShapeDtypeStruct(
        (bands, group_size, row_count // bands, col_count), jnp.float32
    )
    return pl.pallas_call(
        _warp_kernel,
        out_shape=(shape, banded),
        in_specs=[smem, smem, smem, smem, smem, vmem, vmem],
        out_specs=(vmem, vmem),
    )(row_shift, col_shift, row_weight, col_weight, me, padded, bad_pixels)


def _slot_kernel(
    step,
    row_shift,
    col_shift,
    row_weight,
    col_weight,
    me,
    padded,
    bad,
    warped_out,
    flagged_out,
    window_buf,
    bad_buf,
    sems,
):
    group_size, band_rows, col_count = flagged_out.shape
    bands = bad.shape[1] // band_rows
    width = padded.shape[2]
    window = window_buf.shape[1]
    band = lax.rem(me[0] + step, bands)
    base = pl.multiple_of(band * band_rows, 8)
    half = group_size // 2
    spans = [(0, half), (half, group_size - half)]
    fetches = [
        pltpu.make_async_copy(
            padded.at[pl.ds(lo, count), pl.ds(base, window), :],
            window_buf.at[pl.ds(lo, count)],
            sems.at[part],
        )
        for part, (lo, count) in enumerate(spans)
    ]
    fetch_bad = pltpu.make_async_copy(bad.at[:, pl.ds(base, band_rows), :], bad_buf, sems.at[2])
    fetches[0].start()
    fetch_bad.start()
    fetches[1].start()
    fetches[0].wait()
    fetch_bad.wait()

    def one_exposure(e, carry):
        block = pltpu.roll(window_buf[e], window - row_shift[e], 0)
        across = None
        for tap in range(TAPS):
            term = row_weight[e * TAPS + tap] * block[tap : tap + band_rows, :]
            across = term if across is None else across + term
        across = pltpu.roll(across, width - col_shift[e], 1)
        total = None
        for tap in range(TAPS):
            term = col_weight[e * TAPS + tap] * across[:, tap : tap + col_count]
            total = term if total is None else total + term
        warped_out[e] = total
        flagged_out[e] = jnp.where(bad_buf[e] == 1, sentinel, total)
        return carry

    lax.fori_loop(0, half, one_exposure, 0, unroll=True)
    fetches[1].wait()
    lax.fori_loop(half, group_size, one_exposure, 0, unroll=True)


def warp_by_slot(padded, bad_pixels, offsets, warp_index):
    group_size, row_count, col_count = bad_pixels.shape
    bands = lax.axis_size("exp")
    band_rows = row_count // bands
    height = -(-padded.shape[1] // 8) * 8
    window = -(-(band_rows + 2 * HALO) // 8) * 8
    if band_rows % 8 or row_count - band_rows + window > height:
        return None
    kernel_table = lanczos_table()
    row_weight = lookup(warp_index[:, 0], NFRAC, kernel_table).reshape(-1)
    col_weight = lookup(warp_index[:, 1], NFRAC, kernel_table).reshape(-1)
    row_shift = offsets[:, 0] + (HALO - 2)
    col_shift = offsets[:, 1] + (HALO - 2)
    me = lax.axis_index("exp").astype(jnp.int32).reshape(1)
    lanes = -(-padded.shape[2] // 128) * 128
    padded = jnp.pad(
        padded, ((0, 0), (0, height - padded.shape[1]), (0, lanes - padded.shape[2]))
    )
    smem = pl.BlockSpec(memory_space=pltpu.SMEM)
    vmem = pl.BlockSpec(memory_space=pltpu.VMEM)
    anywhere = pl.BlockSpec(memory_space=pl.ANY)
    banded = jax.ShapeDtypeStruct((group_size, band_rows, col_count), jnp.float32)
    order = [bands // 2] + [s for s in range(1, bands) if s != bands // 2] + [0]
    slots = {}
    warped_slots = {}
    for step in order:
        warped_slots[step], flagged = pl.pallas_call(
            functools.partial(_slot_kernel, step),
            out_shape=(banded, banded),
            in_specs=[smem, smem, smem, smem, smem, anywhere, anywhere],
            out_specs=(vmem, vmem),
            scratch_shapes=[
                pltpu.VMEM((group_size, window, lanes), jnp.float32),
                pltpu.VMEM((group_size, band_rows, col_count), jnp.int32),
                pltpu.SemaphoreType.DMA((3,)),
            ],
        )(row_shift, col_shift, row_weight, col_weight, me, padded, bad_pixels)
        if step:
            pairs = [(i, (i + step) % bands) for i in range(bands)]
            slots[step] = lax.ppermute(flagged, "exp", pairs)
        else:
            slots[step] = flagged
    stacked = jnp.stack([warped_slots[s] for s in range(bands)])
    natural = jnp.take(stacked, lax.rem(jnp.arange(bands) - me[0] + bands, bands), axis=0)
    warped = natural.transpose(1, 0, 2, 3).reshape(group_size, row_count, col_count)
    return warped, jnp.concatenate([slots[s] for s in range(bands)], axis=0)


def body(exposures, bad_pixels, offsets, warp_index, blur_index):
    group_size, row_count, col_count = exposures.shape
    padded = extended(exposures, 1, 2, HALO)
    by_slot = warp_by_slot(padded, bad_pixels, offsets, warp_index)
    groups = lax.axis_size("exp")
    if by_slot is not None:
        warped, stack = by_slot
    else:
        warped, flagged = warp_and_flag(padded, bad_pixels, offsets, warp_index)
        arrived = [flagged[0]]
        for step in range(1, groups):
            pairs = [(i, (i + step) % groups) for i in range(groups)]
            arrived.append(lax.ppermute(flagged[step], "exp", pairs))
        stack = jnp.concatenate(arrived, axis=0)
    band = stack_median(stack)
    groups = lax.axis_size("exp")
    sides = lax.axis_size("col")
    band_rows = band.shape[0]
    full = lax.all_to_all(
        jnp.tile(band, (groups * sides, 1)), ("exp", "col"), split_axis=0, concat_axis=0, tiled=True
    )
    full = full.reshape(groups, sides, band_rows, col_count)
    full = full.transpose(0, 2, 1, 3).reshape(row_count, sides * col_count)
    start = lax.axis_index("col") * col_count
    median_sky = lax.dynamic_slice_in_dim(full, start, col_count, axis=1)
    wide = jnp.pad(full, ((0, 0), (PSF_RADIUS, PSF_RADIUS)))
    wide = lax.dynamic_slice_in_dim(wide, start, col_count + 2 * PSF_RADIUS, axis=1)
    bordered = _row_halo(wide, 0, PSF_RADIUS)
    blur = blur_table()
    taps = 2 * PSF_RADIUS + 1
    blurred_rows = jnp.zeros((NPSF, row_count, col_count + 2 * PSF_RADIUS), jnp.float32)
    for tap_no in range(taps):
        blurred_rows = (
            blurred_rows
            + blur[:, tap_no, None, None] * bordered[None, tap_no : tap_no + row_count, :]
        )
    smoothed = jnp.zeros((NPSF, row_count, col_count), jnp.float32)
    for tap_no in range(taps):
        smoothed = (
            smoothed + blur[:, tap_no, None, None] * blurred_rows[:, :, tap_no : tap_no + col_count]
        )
    chooser = (blur_index[:, None] == lax.broadcasted_iota(jnp.int32, (1, NPSF), 1)).astype(
        jnp.float32
    )
    sky_model = jnp.zeros((group_size, row_count, col_count), jnp.float32)
    for kernel_no in range(NPSF):
        sky_model = sky_model + chooser[:, kernel_no, None, None] * smoothed[kernel_no][None]
    residual = jnp.where(bad_pixels == 1, 0.0, warped - sky_model)
    return (residual, median_sky)


def solution(mesh):
    return jax.shard_map(
        body,
        mesh=mesh,
        in_specs=(
            P("exp", "row", "col"),
            P("exp", "row", "col"),
            P("exp", None),
            P("exp", None),
            P("exp"),
        ),
        out_specs=(P("exp", "row", "col"), P("row", "col")),
        check_vma=False,
    )
```

```python
import functools

import jax
import jax.numpy as jnp
from jax import lax
from jax.sharding import PartitionSpec as P
from jax.experimental import pallas as pl
from jax.experimental.pallas import tpu as pltpu


NFRAC = 16
NPSF = 8
PSF_RADIUS = 4
PASSES = 16
HALO = 11


sentinel = 1000000.0
half_sentinel = 500000.0
pivot_span = 16.0


def _row_halo(block, dim, width):
    count = lax.axis_size("row")
    forward = [(i, i + 1) for i in range(count - 1)]
    backward = [(target, source) for source, target in forward]
    size = block.shape[dim]
    low = lax.ppermute(lax.slice_in_dim(block, size - width, None, axis=dim), "row", forward)
    high = lax.ppermute(lax.slice_in_dim(block, 0, width, axis=dim), "row", backward)
    return jnp.concatenate([low, block, high], axis=dim)


def _col_halo(block, dim, width):
    count = lax.axis_size("col")
    size = block.shape[dim]
    right_edge = lax.slice_in_dim(block, size - width, None, axis=dim)
    left_edge = lax.slice_in_dim(block, 0, width, axis=dim)
    if count != 2:
        forward = [(i, i + 1) for i in range(count - 1)]
        backward = [(target, source) for source, target in forward]
        low = lax.ppermute(right_edge, "col", forward)
        high = lax.ppermute(left_edge, "col", backward)
        return jnp.concatenate([low, block, high], axis=dim)
    first = lax.axis_index("col") == 0
    outgoing = jnp.moveaxis(jnp.where(first, right_edge, left_edge), dim, 0)
    packed_shape = outgoing.shape
    packed = outgoing.reshape(width, -1)
    arrived = lax.ppermute(packed, "col", [(0, 1), (1, 0)])
    arrived = jnp.moveaxis(arrived.reshape(packed_shape), 0, dim)
    zeros = jnp.zeros_like(arrived)
    low = jnp.where(first, zeros, arrived)
    high = jnp.where(first, arrived, zeros)
    return jnp.concatenate([low, block, high], axis=dim)


def extended(block, row_dim, col_dim, width):
    return _col_halo(_row_halo(block, row_dim, width), col_dim, width)


def lanczos_table():
    fraction = jnp.arange(NFRAC, dtype=jnp.float32) / NFRAC
    offset_grid = jnp.arange(-2, 4, dtype=jnp.float32)
    spread = offset_grid[None, :] - fraction[:, None]
    kernel = jnp.sinc(spread) * jnp.sinc(spread / 3.0)
    return kernel / jnp.sum(kernel, axis=1, keepdims=True)


def blur_table():
    offset_grid = jnp.arange(-PSF_RADIUS, PSF_RADIUS + 1, dtype=jnp.float32)
    widths = 0.7 + 0.2 * jnp.arange(NPSF, dtype=jnp.float32)
    kernel = jnp.exp(-0.5 * (offset_grid[None, :] / widths[:, None]) ** 2)
    return kernel / jnp.sum(kernel, axis=1, keepdims=True)


def lookup(indices, entries, kernel_table):
    chooser = (indices[:, None] == lax.broadcasted_iota(jnp.int32, (1, entries), 1)).astype(
        jnp.float32
    )
    return jnp.dot(chooser, kernel_table, precision=lax.Precision.HIGHEST)


TAPS = 6


def _warp_kernel(
    row_shift, col_shift, row_weight, col_weight, me, padded, bad, warped_out, flagged_out
):
    group_size, row_count, col_count = warped_out.shape
    bands, _, band_rows, _ = flagged_out.shape
    width = padded.shape[2]

    height = padded.shape[1]

    def one_exposure(e, carry):
        block = pltpu.roll(padded[e], height - row_shift[e], 0)
        across = None
        for tap in range(TAPS):
            term = row_weight[e * TAPS + tap] * block[tap : tap + row_count, :]
            across = term if across is None else across + term
        across = pltpu.roll(across, width - col_shift[e], 1)
        total = None
        for tap in range(TAPS):
            term = col_weight[e * TAPS + tap] * across[:, tap : tap + col_count]
            total = term if total is None else total + term
        warped_out[e] = total
        flagged = jnp.where(bad[e] == 1, sentinel, total)
        for band in range(bands):
            slot = lax.rem(band - me[0] + bands, bands)
            flagged_out[slot, e] = flagged[band * band_rows : (band + 1) * band_rows]
        return carry

    lax.fori_loop(0, group_size, one_exposure, 0, unroll=True)


def warp_and_flag(padded, bad_pixels, offsets, warp_index):
    group_size, row_count, col_count = bad_pixels.shape
    kernel_table = lanczos_table()
    row_weight = lookup(warp_index[:, 0], NFRAC, kernel_table).reshape(-1)
    col_weight = lookup(warp_index[:, 1], NFRAC, kernel_table).reshape(-1)
    row_shift = offsets[:, 0] + (HALO - 2)
    col_shift = offsets[:, 1] + (HALO - 2)
    me = lax.axis_index("exp").astype(jnp.int32).reshape(1)
    lanes = -(-padded.shape[2] // 128) * 128
    rows = -(-padded.shape[1] // 8) * 8
    padded = jnp.pad(
        padded, ((0, 0), (0, rows - padded.shape[1]), (0, lanes - padded.shape[2]))
    )
    smem = pl.BlockSpec(memory_space=pltpu.SMEM)
    vmem = pl.BlockSpec(memory_space=pltpu.VMEM)
    shape = jax.ShapeDtypeStruct((group_size, row_count, col_count), jnp.float32)
    bands = lax.axis_size("exp")
    banded = jax.ShapeDtypeStruct(
        (bands, group_size, row_count // bands, col_count), jnp.float32
    )
    return pl.pallas_call(
        _warp_kernel,
        out_shape=(shape, banded),
        in_specs=[smem, smem, smem, smem, smem, vmem, vmem],
        out_specs=(vmem, vmem),
    )(row_shift, col_shift, row_weight, col_weight, me, padded, bad_pixels)


def _slot_kernel(
    step,
    row_shift,
    col_shift,
    row_weight,
    col_weight,
    me,
    padded,
    bad,
    warped_out,
    flagged_out,
    window_buf,
    bad_buf,
    sems,
):
    group_size, band_rows, col_count = flagged_out.shape
    bands = bad.shape[1] // band_rows
    width = padded.shape[2]
    window = window_buf.shape[1]
    band = lax.rem(me[0] + step, bands)
    base = pl.multiple_of(band * band_rows, 8)
    half = group_size // 2
    spans = [(0, half), (half, group_size - half)]
    fetches = [
        pltpu.make_async_copy(
            padded.at[pl.ds(lo, count), pl.ds(base, window), :],
            window_buf.at[pl.ds(lo, count)],
            sems.at[part],
        )
        for part, (lo, count) in enumerate(spans)
    ]
    fetch_bad = pltpu.make_async_copy(bad.at[:, pl.ds(base, band_rows), :], bad_buf, sems.at[2])
    fetches[0].start()
    fetch_bad.start()
    fetches[1].start()
    fetches[0].wait()
    fetch_bad.wait()

    def one_exposure(e, carry):
        block = pltpu.roll(window_buf[e], window - row_shift[e], 0)
        across = None
        for tap in range(TAPS):
            term = row_weight[e * TAPS + tap] * block[tap : tap + band_rows, :]
            across = term if across is None else across + term
        across = pltpu.roll(across, width - col_shift[e], 1)
        total = None
        for tap in range(TAPS):
            term = col_weight[e * TAPS + tap] * across[:, tap : tap + col_count]
            total = term if total is None else total + term
        warped_out[e] = total
        flagged_out[e] = jnp.where(bad_buf[e] == 1, sentinel, total)
        return carry

    lax.fori_loop(0, half, one_exposure, 0, unroll=True)
    fetches[1].wait()
    lax.fori_loop(half, group_size, one_exposure, 0, unroll=True)


def warp_by_slot(padded, bad_pixels, offsets, warp_index):
    group_size, row_count, col_count = bad_pixels.shape
    bands = lax.axis_size("exp")
    band_rows = row_count // bands
    height = -(-padded.shape[1] // 8) * 8
    window = -(-(band_rows + 2 * HALO) // 8) * 8
    if band_rows % 8 or row_count - band_rows + window > height:
        return None
    kernel_table = lanczos_table()
    row_weight = lookup(warp_index[:, 0], NFRAC, kernel_table).reshape(-1)
    col_weight = lookup(warp_index[:, 1], NFRAC, kernel_table).reshape(-1)
    row_shift = offsets[:, 0] + (HALO - 2)
    col_shift = offsets[:, 1] + (HALO - 2)
    me = lax.axis_index("exp").astype(jnp.int32).reshape(1)
    lanes = -(-padded.shape[2] // 128) * 128
    padded = jnp.pad(
        padded, ((0, 0), (0, height - padded.shape[1]), (0, lanes - padded.shape[2]))
    )
    smem = pl.BlockSpec(memory_space=pltpu.SMEM)
    vmem = pl.BlockSpec(memory_space=pltpu.VMEM)
    anywhere = pl.BlockSpec(memory_space=pl.ANY)
    banded = jax.ShapeDtypeStruct((group_size, band_rows, col_count), jnp.float32)
    order = [bands // 2] + [s for s in range(1, bands) if s != bands // 2] + [0]
    slots = {}
    warped_slots = {}
    for step in order:
        warped_slots[step], flagged = pl.pallas_call(
            functools.partial(_slot_kernel, step),
            out_shape=(banded, banded),
            in_specs=[smem, smem, smem, smem, smem, anywhere, anywhere],
            out_specs=(vmem, vmem),
            scratch_shapes=[
                pltpu.VMEM((group_size, window, lanes), jnp.float32),
                pltpu.VMEM((group_size, band_rows, col_count), jnp.int32),
                pltpu.SemaphoreType.DMA((3,)),
            ],
        )(row_shift, col_shift, row_weight, col_weight, me, padded, bad_pixels)
        if step:
            pairs = [(i, (i + step) % bands) for i in range(bands)]
            slots[step] = lax.ppermute(flagged, "exp", pairs)
        else:
            slots[step] = flagged
    stacked = jnp.stack([warped_slots[s] for s in range(bands)])
    natural = jnp.take(stacked, lax.rem(jnp.arange(bands) - me[0] + bands, bands), axis=0)
    warped = natural.transpose(1, 0, 2, 3).reshape(group_size, row_count, col_count)
    return warped, jnp.concatenate([slots[s] for s in range(bands)], axis=0)


def _median_kernel(stack, out):
    depth = stack.shape[0]
    band_rows = stack.shape[1]
    copies = out.shape[0] // band_rows

    def count_valid(e, total):
        return total + (stack[e] < half_sentinel).astype(jnp.float32)

    valid_count = lax.fori_loop(
        0, depth, count_valid, jnp.zeros(stack.shape[1:], jnp.float32), unroll=8
    )

    def one_pass(sweep_no, bounds):
        lower_edge, upper_edge = bounds
        middle = 0.5 * (lower_edge + upper_edge)

        def count_below(e, total):
            return total + (stack[e] <= middle).astype(jnp.float32)

        counted = lax.fori_loop(
            0, depth, count_below, jnp.zeros(stack.shape[1:], jnp.float32), unroll=8
        )
        enough = 2.0 * counted >= valid_count
        return (jnp.where(enough, lower_edge, middle), jnp.where(enough, middle, upper_edge))

    initial = (
        jnp.full(stack.shape[1:], -pivot_span, jnp.float32),
        jnp.full(stack.shape[1:], pivot_span, jnp.float32),
    )
    lower_edge = lax.fori_loop(0, PASSES, one_pass, initial)[0]

    def smallest_above(e, best):
        value = stack[e]
        return jnp.minimum(best, jnp.where(value > lower_edge, value, sentinel))

    median = lax.fori_loop(
        0, depth, smallest_above, jnp.full(stack.shape[1:], sentinel, jnp.float32), unroll=8
    )
    for copy_no in range(copies):
        out[copy_no * band_rows : (copy_no + 1) * band_rows] = median


def median_copies(stack, copies):
    vmem = pl.BlockSpec(memory_space=pltpu.VMEM)
    shape = jax.ShapeDtypeStruct((copies * stack.shape[1], stack.shape[2]), jnp.float32)
    return pl.pallas_call(
        _median_kernel, out_shape=shape, in_specs=[vmem], out_specs=vmem
    )(stack)


def body(exposures, bad_pixels, offsets, warp_index, blur_index):
    group_size, row_count, col_count = exposures.shape
    padded = extended(exposures, 1, 2, HALO)
    by_slot = warp_by_slot(padded, bad_pixels, offsets, warp_index)
    groups = lax.axis_size("exp")
    if by_slot is not None:
        warped, stack = by_slot
    else:
        warped, flagged = warp_and_flag(padded, bad_pixels, offsets, warp_index)
        arrived = [flagged[0]]
        for step in range(1, groups):
            pairs = [(i, (i + step) % groups) for i in range(groups)]
            arrived.append(lax.ppermute(flagged[step], "exp", pairs))
        stack = jnp.concatenate(arrived, axis=0)
    groups = lax.axis_size("exp")
    sides = lax.axis_size("col")
    band_rows = stack.shape[1]
    full = lax.all_to_all(
        median_copies(stack, groups * sides), ("exp", "col"), split_axis=0, concat_axis=0, tiled=True
    )
    full = full.reshape(groups, sides, band_rows, col_count)
    full = full.transpose(0, 2, 1, 3).reshape(row_count, sides * col_count)
    start = lax.axis_index("col") * col_count
    median_sky = lax.dynamic_slice_in_dim(full, start, col_count, axis=1)
    wide = jnp.pad(full, ((0, 0), (PSF_RADIUS, PSF_RADIUS)))
    wide = lax.dynamic_slice_in_dim(wide, start, col_count + 2 * PSF_RADIUS, axis=1)
    bordered = _row_halo(wide, 0, PSF_RADIUS)
    blur = blur_table()
    taps = 2 * PSF_RADIUS + 1
    blurred_rows = jnp.zeros((NPSF, row_count, col_count + 2 * PSF_RADIUS), jnp.float32)
    for tap_no in range(taps):
        blurred_rows = (
            blurred_rows
            + blur[:, tap_no, None, None] * bordered[None, tap_no : tap_no + row_count, :]
        )
    smoothed = jnp.zeros((NPSF, row_count, col_count), jnp.float32)
    for tap_no in range(taps):
        smoothed = (
            smoothed + blur[:, tap_no, None, None] * blurred_rows[:, :, tap_no : tap_no + col_count]
        )
    chooser = (blur_index[:, None] == lax.broadcasted_iota(jnp.int32, (1, NPSF), 1)).astype(
        jnp.float32
    )
    sky_model = jnp.zeros((group_size, row_count, col_count), jnp.float32)
    for kernel_no in range(NPSF):
        sky_model = sky_model + chooser[:, kernel_no, None, None] * smoothed[kernel_no][None]
    residual = jnp.where(bad_pixels == 1, 0.0, warped - sky_model)
    return (residual, median_sky)


def solution(mesh):
    return jax.shard_map(
        body,
        mesh=mesh,
        in_specs=(
            P("exp", "row", "col"),
            P("exp", "row", "col"),
            P("exp", None),
            P("exp", None),
            P("exp"),
        ),
        out_specs=(P("exp", "row", "col"), P("row", "col")),
        check_vma=False,
    )
```

```python
import functools

import jax
import jax.numpy as jnp
from jax import lax
from jax.sharding import PartitionSpec as P
from jax.experimental import pallas as pl
from jax.experimental.pallas import tpu as pltpu


NFRAC = 16
NPSF = 8
PSF_RADIUS = 4
PASSES = 16
HALO = 11


sentinel = 1000000.0
half_sentinel = 500000.0
pivot_span = 16.0


def _row_halo(block, dim, width):
    count = lax.axis_size("row")
    forward = [(i, i + 1) for i in range(count - 1)]
    backward = [(target, source) for source, target in forward]
    size = block.shape[dim]
    low = lax.ppermute(lax.slice_in_dim(block, size - width, None, axis=dim), "row", forward)
    high = lax.ppermute(lax.slice_in_dim(block, 0, width, axis=dim), "row", backward)
    return jnp.concatenate([low, block, high], axis=dim)


def _col_halo(block, dim, width):
    count = lax.axis_size("col")
    size = block.shape[dim]
    right_edge = lax.slice_in_dim(block, size - width, None, axis=dim)
    left_edge = lax.slice_in_dim(block, 0, width, axis=dim)
    if count != 2:
        forward = [(i, i + 1) for i in range(count - 1)]
        backward = [(target, source) for source, target in forward]
        low = lax.ppermute(right_edge, "col", forward)
        high = lax.ppermute(left_edge, "col", backward)
        return jnp.concatenate([low, block, high], axis=dim)
    first = lax.axis_index("col") == 0
    outgoing = jnp.moveaxis(jnp.where(first, right_edge, left_edge), dim, 0)
    packed_shape = outgoing.shape
    packed = outgoing.reshape(width, -1)
    arrived = lax.ppermute(packed, "col", [(0, 1), (1, 0)])
    arrived = jnp.moveaxis(arrived.reshape(packed_shape), 0, dim)
    zeros = jnp.zeros_like(arrived)
    low = jnp.where(first, zeros, arrived)
    high = jnp.where(first, arrived, zeros)
    return jnp.concatenate([low, block, high], axis=dim)


def extended(block, row_dim, col_dim, width):
    return _col_halo(_row_halo(block, row_dim, width), col_dim, width)


def lanczos_table():
    fraction = jnp.arange(NFRAC, dtype=jnp.float32) / NFRAC
    offset_grid = jnp.arange(-2, 4, dtype=jnp.float32)
    spread = offset_grid[None, :] - fraction[:, None]
    kernel = jnp.sinc(spread) * jnp.sinc(spread / 3.0)
    return kernel / jnp.sum(kernel, axis=1, keepdims=True)


def blur_table():
    offset_grid = jnp.arange(-PSF_RADIUS, PSF_RADIUS + 1, dtype=jnp.float32)
    widths = 0.7 + 0.2 * jnp.arange(NPSF, dtype=jnp.float32)
    kernel = jnp.exp(-0.5 * (offset_grid[None, :] / widths[:, None]) ** 2)
    return kernel / jnp.sum(kernel, axis=1, keepdims=True)


def lookup(indices, entries, kernel_table):
    chooser = (indices[:, None] == lax.broadcasted_iota(jnp.int32, (1, entries), 1)).astype(
        jnp.float32
    )
    return jnp.dot(chooser, kernel_table, precision=lax.Precision.HIGHEST)


def bisect_lower(valid_count, count_below):

    def one_pass(sweep_no, bounds):
        lower_edge, upper_edge = bounds
        middle = 0.5 * (lower_edge + upper_edge)
        enough = 2.0 * count_below(middle) >= valid_count
        return (jnp.where(enough, lower_edge, middle), jnp.where(enough, middle, upper_edge))

    initial = (
        jnp.full(valid_count.shape, -pivot_span, jnp.float32),
        jnp.full(valid_count.shape, pivot_span, jnp.float32),
    )
    return lax.fori_loop(0, PASSES, one_pass, initial)[0]


def stack_median(pixel_stack):
    valid_count = jnp.sum(pixel_stack < half_sentinel, axis=0, dtype=jnp.float32)

    def count_below(middle):
        return jnp.sum(pixel_stack <= middle[None], axis=0, dtype=jnp.float32)

    lower_edge = bisect_lower(valid_count, count_below)
    return jnp.min(jnp.where(pixel_stack > lower_edge[None], pixel_stack, sentinel), axis=0)


TAPS = 6


def _warp_kernel(
    row_shift, col_shift, row_weight, col_weight, me, padded, bad, warped_out, flagged_out
):
    group_size, row_count, col_count = warped_out.shape
    bands, _, band_rows, _ = flagged_out.shape
    width = padded.shape[2]

    height = padded.shape[1]

    def one_exposure(e, carry):
        block = pltpu.roll(padded[e], height - row_shift[e], 0)
        across = None
        for tap in range(TAPS):
            term = row_weight[e * TAPS + tap] * block[tap : tap + row_count, :]
            across = term if across is None else across + term
        across = pltpu.roll(across, width - col_shift[e], 1)
        total = None
        for tap in range(TAPS):
            term = col_weight[e * TAPS + tap] * across[:, tap : tap + col_count]
            total = term if total is None else total + term
        warped_out[e] = total
        flagged = jnp.where(bad[e] == 1, sentinel, total)
        for band in range(bands):
            slot = lax.rem(band - me[0] + bands, bands)
            flagged_out[slot, e] = flagged[band * band_rows : (band + 1) * band_rows]
        return carry

    lax.fori_loop(0, group_size, one_exposure, 0, unroll=True)


def warp_and_flag(padded, bad_pixels, offsets, warp_index):
    group_size, row_count, col_count = bad_pixels.shape
    kernel_table = lanczos_table()
    row_weight = lookup(warp_index[:, 0], NFRAC, kernel_table).reshape(-1)
    col_weight = lookup(warp_index[:, 1], NFRAC, kernel_table).reshape(-1)
    row_shift = offsets[:, 0] + (HALO - 2)
    col_shift = offsets[:, 1] + (HALO - 2)
    me = lax.axis_index("exp").astype(jnp.int32).reshape(1)
    lanes = -(-padded.shape[2] // 128) * 128
    rows = -(-padded.shape[1] // 8) * 8
    padded = jnp.pad(
        padded, ((0, 0), (0, rows - padded.shape[1]), (0, lanes - padded.shape[2]))
    )
    smem = pl.BlockSpec(memory_space=pltpu.SMEM)
    vmem = pl.BlockSpec(memory_space=pltpu.VMEM)
    shape = jax.ShapeDtypeStruct((group_size, row_count, col_count), jnp.float32)
    bands = lax.axis_size("exp")
    banded = jax.ShapeDtypeStruct(
        (bands, group_size, row_count // bands, col_count), jnp.float32
    )
    return pl.pallas_call(
        _warp_kernel,
        out_shape=(shape, banded),
        in_specs=[smem, smem, smem, smem, smem, vmem, vmem],
        out_specs=(vmem, vmem),
    )(row_shift, col_shift, row_weight, col_weight, me, padded, bad_pixels)


def _slot_kernel(
    step,
    row_shift,
    col_shift,
    row_weight,
    col_weight,
    me,
    padded,
    bad,
    warped_out,
    flagged_out,
    window_buf,
    bad_buf,
    sems,
):
    group_size, band_rows, col_count = flagged_out.shape
    bands = bad.shape[1] // band_rows
    width = padded.shape[2]
    window = window_buf.shape[1]
    band = lax.rem(me[0] + step, bands)
    base = pl.multiple_of(band * band_rows, 8)
    parts = 8 if group_size % 8 == 0 else 2
    share = group_size // parts
    spans = [(part * share, share) for part in range(parts - 1)]
    spans.append(((parts - 1) * share, group_size - (parts - 1) * share))
    fetches = [
        pltpu.make_async_copy(
            padded.at[pl.ds(lo, count), pl.ds(base, window), :],
            window_buf.at[pl.ds(lo, count)],
            sems.at[part],
        )
        for part, (lo, count) in enumerate(spans)
    ]
    fetch_bad = pltpu.make_async_copy(
        bad.at[:, pl.ds(base, band_rows), :], bad_buf, sems.at[len(spans)]
    )
    fetches[0].start()
    fetch_bad.start()
    for fetch in fetches[1:]:
        fetch.start()
    fetch_bad.wait()

    def one_exposure(e, carry):
        block = pltpu.roll(window_buf[e], window - row_shift[e], 0)
        across = None
        for tap in range(TAPS):
            term = row_weight[e * TAPS + tap] * block[tap : tap + band_rows, :]
            across = term if across is None else across + term
        across = pltpu.roll(across, width - col_shift[e], 1)
        total = None
        for tap in range(TAPS):
            term = col_weight[e * TAPS + tap] * across[:, tap : tap + col_count]
            total = term if total is None else total + term
        warped_out[e] = total
        flagged_out[e] = jnp.where(bad_buf[e] == 1, sentinel, total)
        return carry

    for fetch, (lo, count) in zip(fetches, spans):
        fetch.wait()
        lax.fori_loop(lo, lo + count, one_exposure, 0, unroll=True)


def warp_by_slot(padded, bad_pixels, offsets, warp_index):
    group_size, row_count, col_count = bad_pixels.shape
    bands = lax.axis_size("exp")
    band_rows = row_count // bands
    height = -(-padded.shape[1] // 8) * 8
    window = -(-(band_rows + 2 * HALO) // 8) * 8
    if band_rows % 8 or row_count - band_rows + window > height:
        return None
    kernel_table = lanczos_table()
    row_weight = lookup(warp_index[:, 0], NFRAC, kernel_table).reshape(-1)
    col_weight = lookup(warp_index[:, 1], NFRAC, kernel_table).reshape(-1)
    row_shift = offsets[:, 0] + (HALO - 2)
    col_shift = offsets[:, 1] + (HALO - 2)
    me = lax.axis_index("exp").astype(jnp.int32).reshape(1)
    lanes = -(-padded.shape[2] // 128) * 128
    padded = jnp.pad(
        padded, ((0, 0), (0, height - padded.shape[1]), (0, lanes - padded.shape[2]))
    )
    smem = pl.BlockSpec(memory_space=pltpu.SMEM)
    vmem = pl.BlockSpec(memory_space=pltpu.VMEM)
    anywhere = pl.BlockSpec(memory_space=pl.ANY)
    banded = jax.ShapeDtypeStruct((group_size, band_rows, col_count), jnp.float32)
    order = [bands // 2] + [s for s in range(1, bands) if s != bands // 2] + [0]
    slots = {}
    warped_slots = {}
    for step in order:
        warped_slots[step], flagged = pl.pallas_call(
            functools.partial(_slot_kernel, step),
            out_shape=(banded, banded),
            in_specs=[smem, smem, smem, smem, smem, anywhere, anywhere],
            out_specs=(vmem, vmem),
            scratch_shapes=[
                pltpu.VMEM((group_size, window, lanes), jnp.float32),
                pltpu.VMEM((group_size, band_rows, col_count), jnp.int32),
                pltpu.SemaphoreType.DMA((9,)),
            ],
        )(row_shift, col_shift, row_weight, col_weight, me, padded, bad_pixels)
        if step:
            pairs = [(i, (i + step) % bands) for i in range(bands)]
            slots[step] = lax.ppermute(flagged, "exp", pairs)
        else:
            slots[step] = flagged
    stacked = jnp.stack([warped_slots[s] for s in range(bands)])
    natural = jnp.take(stacked, lax.rem(jnp.arange(bands) - me[0] + bands, bands), axis=0)
    warped = natural.transpose(1, 0, 2, 3).reshape(group_size, row_count, col_count)
    return warped, jnp.concatenate([slots[s] for s in range(bands)], axis=0)


def body(exposures, bad_pixels, offsets, warp_index, blur_index):
    group_size, row_count, col_count = exposures.shape
    padded = extended(exposures, 1, 2, HALO)
    by_slot = warp_by_slot(padded, bad_pixels, offsets, warp_index)
    groups = lax.axis_size("exp")
    if by_slot is not None:
        warped, stack = by_slot
    else:
        warped, flagged = warp_and_flag(padded, bad_pixels, offsets, warp_index)
        arrived = [flagged[0]]
        for step in range(1, groups):
            pairs = [(i, (i + step) % groups) for i in range(groups)]
            arrived.append(lax.ppermute(flagged[step], "exp", pairs))
        stack = jnp.concatenate(arrived, axis=0)
    band = stack_median(stack)
    groups = lax.axis_size("exp")
    sides = lax.axis_size("col")
    band_rows = band.shape[0]
    full = lax.all_to_all(
        jnp.tile(band, (groups * sides, 1)), ("exp", "col"), split_axis=0, concat_axis=0, tiled=True
    )
    full = full.reshape(groups, sides, band_rows, col_count)
    full = full.transpose(0, 2, 1, 3).reshape(row_count, sides * col_count)
    start = lax.axis_index("col") * col_count
    median_sky = lax.dynamic_slice_in_dim(full, start, col_count, axis=1)
    wide = jnp.pad(full, ((0, 0), (PSF_RADIUS, PSF_RADIUS)))
    wide = lax.dynamic_slice_in_dim(wide, start, col_count + 2 * PSF_RADIUS, axis=1)
    bordered = _row_halo(wide, 0, PSF_RADIUS)
    blur = blur_table()
    taps = 2 * PSF_RADIUS + 1
    blurred_rows = jnp.zeros((NPSF, row_count, col_count + 2 * PSF_RADIUS), jnp.float32)
    for tap_no in range(taps):
        blurred_rows = (
            blurred_rows
            + blur[:, tap_no, None, None] * bordered[None, tap_no : tap_no + row_count, :]
        )
    smoothed = jnp.zeros((NPSF, row_count, col_count), jnp.float32)
    for tap_no in range(taps):
        smoothed = (
            smoothed + blur[:, tap_no, None, None] * blurred_rows[:, :, tap_no : tap_no + col_count]
        )
    chooser = (blur_index[:, None] == lax.broadcasted_iota(jnp.int32, (1, NPSF), 1)).astype(
        jnp.float32
    )
    sky_model = jnp.zeros((group_size, row_count, col_count), jnp.float32)
    for kernel_no in range(NPSF):
        sky_model = sky_model + chooser[:, kernel_no, None, None] * smoothed[kernel_no][None]
    residual = jnp.where(bad_pixels == 1, 0.0, warped - sky_model)
    return (residual, median_sky)


def solution(mesh):
    return jax.shard_map(
        body,
        mesh=mesh,
        in_specs=(
            P("exp", "row", "col"),
            P("exp", "row", "col"),
            P("exp", None),
            P("exp", None),
            P("exp"),
        ),
        out_specs=(P("exp", "row", "col"), P("row", "col")),
        check_vma=False,
    )
```

```python
import functools

import jax
import jax.numpy as jnp
from jax import lax
from jax.sharding import PartitionSpec as P
from jax.experimental import pallas as pl
from jax.experimental.pallas import tpu as pltpu


NFRAC = 16
NPSF = 8
PSF_RADIUS = 4
PASSES = 16
HALO = 11


sentinel = 1000000.0
half_sentinel = 500000.0
pivot_span = 16.0


def _row_halo(block, dim, width):
    count = lax.axis_size("row")
    forward = [(i, i + 1) for i in range(count - 1)]
    backward = [(target, source) for source, target in forward]
    size = block.shape[dim]
    low = lax.ppermute(lax.slice_in_dim(block, size - width, None, axis=dim), "row", forward)
    high = lax.ppermute(lax.slice_in_dim(block, 0, width, axis=dim), "row", backward)
    return jnp.concatenate([low, block, high], axis=dim)


def _col_halo(block, dim, width):
    count = lax.axis_size("col")
    size = block.shape[dim]
    right_edge = lax.slice_in_dim(block, size - width, None, axis=dim)
    left_edge = lax.slice_in_dim(block, 0, width, axis=dim)
    if count != 2:
        forward = [(i, i + 1) for i in range(count - 1)]
        backward = [(target, source) for source, target in forward]
        low = lax.ppermute(right_edge, "col", forward)
        high = lax.ppermute(left_edge, "col", backward)
        return jnp.concatenate([low, block, high], axis=dim)
    first = lax.axis_index("col") == 0
    outgoing = jnp.moveaxis(jnp.where(first, right_edge, left_edge), dim, 0)
    packed_shape = outgoing.shape
    packed = outgoing.reshape(width, -1)
    arrived = lax.ppermute(packed, "col", [(0, 1), (1, 0)])
    arrived = jnp.moveaxis(arrived.reshape(packed_shape), 0, dim)
    zeros = jnp.zeros_like(arrived)
    low = jnp.where(first, zeros, arrived)
    high = jnp.where(first, arrived, zeros)
    return jnp.concatenate([low, block, high], axis=dim)


def extended(block, row_dim, col_dim, width):
    return _col_halo(_row_halo(block, row_dim, width), col_dim, width)


def lanczos_table():
    fraction = jnp.arange(NFRAC, dtype=jnp.float32) / NFRAC
    offset_grid = jnp.arange(-2, 4, dtype=jnp.float32)
    spread = offset_grid[None, :] - fraction[:, None]
    kernel = jnp.sinc(spread) * jnp.sinc(spread / 3.0)
    return kernel / jnp.sum(kernel, axis=1, keepdims=True)


def blur_table():
    offset_grid = jnp.arange(-PSF_RADIUS, PSF_RADIUS + 1, dtype=jnp.float32)
    widths = 0.7 + 0.2 * jnp.arange(NPSF, dtype=jnp.float32)
    kernel = jnp.exp(-0.5 * (offset_grid[None, :] / widths[:, None]) ** 2)
    return kernel / jnp.sum(kernel, axis=1, keepdims=True)


def lookup(indices, entries, kernel_table):
    chooser = (indices[:, None] == lax.broadcasted_iota(jnp.int32, (1, entries), 1)).astype(
        jnp.float32
    )
    return jnp.dot(chooser, kernel_table, precision=lax.Precision.HIGHEST)


def bisect_lower(valid_count, count_below):

    def one_pass(bounds):
        lower_edge, upper_edge = bounds
        middle = 0.5 * (lower_edge + upper_edge)
        enough = 2.0 * count_below(middle) >= valid_count
        return (jnp.where(enough, lower_edge, middle), jnp.where(enough, middle, upper_edge))

    initial = (
        jnp.full(valid_count.shape, -pivot_span, jnp.float32),
        jnp.full(valid_count.shape, pivot_span, jnp.float32),
    )
    bounds = initial
    for _ in range(PASSES):
        bounds = one_pass(bounds)
    return bounds[0]


def stack_median(pixel_stack):
    valid_count = jnp.sum(pixel_stack < half_sentinel, axis=0, dtype=jnp.float32)

    def count_below(middle):
        return jnp.sum(pixel_stack <= middle[None], axis=0, dtype=jnp.float32)

    lower_edge = bisect_lower(valid_count, count_below)
    return jnp.min(jnp.where(pixel_stack > lower_edge[None], pixel_stack, sentinel), axis=0)


TAPS = 6


def _warp_kernel(
    row_shift, col_shift, row_weight, col_weight, me, padded, bad, warped_out, flagged_out
):
    group_size, row_count, col_count = warped_out.shape
    bands, _, band_rows, _ = flagged_out.shape
    width = padded.shape[2]

    height = padded.shape[1]

    def one_exposure(e, carry):
        block = pltpu.roll(padded[e], height - row_shift[e], 0)
        across = None
        for tap in range(TAPS):
            term = row_weight[e * TAPS + tap] * block[tap : tap + row_count, :]
            across = term if across is None else across + term
        across = pltpu.roll(across, width - col_shift[e], 1)
        total = None
        for tap in range(TAPS):
            term = col_weight[e * TAPS + tap] * across[:, tap : tap + col_count]
            total = term if total is None else total + term
        warped_out[e] = total
        flagged = jnp.where(bad[e] == 1, sentinel, total)
        for band in range(bands):
            slot = lax.rem(band - me[0] + bands, bands)
            flagged_out[slot, e] = flagged[band * band_rows : (band + 1) * band_rows]
        return carry

    lax.fori_loop(0, group_size, one_exposure, 0, unroll=True)


def warp_and_flag(padded, bad_pixels, offsets, warp_index):
    group_size, row_count, col_count = bad_pixels.shape
    kernel_table = lanczos_table()
    row_weight = lookup(warp_index[:, 0], NFRAC, kernel_table).reshape(-1)
    col_weight = lookup(warp_index[:, 1], NFRAC, kernel_table).reshape(-1)
    row_shift = offsets[:, 0] + (HALO - 2)
    col_shift = offsets[:, 1] + (HALO - 2)
    me = lax.axis_index("exp").astype(jnp.int32).reshape(1)
    lanes = -(-padded.shape[2] // 128) * 128
    rows = -(-padded.shape[1] // 8) * 8
    padded = jnp.pad(
        padded, ((0, 0), (0, rows - padded.shape[1]), (0, lanes - padded.shape[2]))
    )
    smem = pl.BlockSpec(memory_space=pltpu.SMEM)
    vmem = pl.BlockSpec(memory_space=pltpu.VMEM)
    shape = jax.ShapeDtypeStruct((group_size, row_count, col_count), jnp.float32)
    bands = lax.axis_size("exp")
    banded = jax.ShapeDtypeStruct(
        (bands, group_size, row_count // bands, col_count), jnp.float32
    )
    return pl.pallas_call(
        _warp_kernel,
        out_shape=(shape, banded),
        in_specs=[smem, smem, smem, smem, smem, vmem, vmem],
        out_specs=(vmem, vmem),
    )(row_shift, col_shift, row_weight, col_weight, me, padded, bad_pixels)


def _slot_kernel(
    step,
    row_shift,
    col_shift,
    row_weight,
    col_weight,
    me,
    padded,
    bad,
    warped_out,
    flagged_out,
    window_buf,
    bad_buf,
    sems,
):
    group_size, band_rows, col_count = flagged_out.shape
    bands = bad.shape[1] // band_rows
    width = padded.shape[2]
    window = window_buf.shape[1]
    band = lax.rem(me[0] + step, bands)
    base = pl.multiple_of(band * band_rows, 8)
    parts = 4 if group_size % 4 == 0 else 2
    share = group_size // parts
    spans = [(part * share, share) for part in range(parts - 1)]
    spans.append(((parts - 1) * share, group_size - (parts - 1) * share))
    fetches = [
        pltpu.make_async_copy(
            padded.at[pl.ds(lo, count), pl.ds(base, window), :],
            window_buf.at[pl.ds(lo, count)],
            sems.at[part],
        )
        for part, (lo, count) in enumerate(spans)
    ]
    fetch_bad = pltpu.make_async_copy(
        bad.at[:, pl.ds(base, band_rows), :], bad_buf, sems.at[len(spans)]
    )
    fetches[0].start()
    fetch_bad.start()
    for fetch in fetches[1:]:
        fetch.start()
    fetch_bad.wait()

    def one_exposure(e, carry):
        block = pltpu.roll(window_buf[e], window - row_shift[e], 0)
        across = None
        for tap in range(TAPS):
            term = row_weight[e * TAPS + tap] * block[tap : tap + band_rows, :]
            across = term if across is None else across + term
        across = pltpu.roll(across, width - col_shift[e], 1)
        total = None
        for tap in range(TAPS):
            term = col_weight[e * TAPS + tap] * across[:, tap : tap + col_count]
            total = term if total is None else total + term
        warped_out[e] = total
        flagged_out[e] = jnp.where(bad_buf[e] == 1, sentinel, total)
        return carry

    for fetch, (lo, count) in zip(fetches, spans):
        fetch.wait()
        lax.fori_loop(lo, lo + count, one_exposure, 0, unroll=True)


def warp_by_slot(padded, bad_pixels, offsets, warp_index):
    group_size, row_count, col_count = bad_pixels.shape
    bands = lax.axis_size("exp")
    band_rows = row_count // bands
    height = -(-padded.shape[1] // 8) * 8
    window = -(-(band_rows + 2 * HALO) // 8) * 8
    if band_rows % 8 or row_count - band_rows + window > height:
        return None
    kernel_table = lanczos_table()
    row_weight = lookup(warp_index[:, 0], NFRAC, kernel_table).reshape(-1)
    col_weight = lookup(warp_index[:, 1], NFRAC, kernel_table).reshape(-1)
    row_shift = offsets[:, 0] + (HALO - 2)
    col_shift = offsets[:, 1] + (HALO - 2)
    me = lax.axis_index("exp").astype(jnp.int32).reshape(1)
    lanes = -(-padded.shape[2] // 128) * 128
    padded = jnp.pad(
        padded, ((0, 0), (0, height - padded.shape[1]), (0, lanes - padded.shape[2]))
    )
    smem = pl.BlockSpec(memory_space=pltpu.SMEM)
    vmem = pl.BlockSpec(memory_space=pltpu.VMEM)
    anywhere = pl.BlockSpec(memory_space=pl.ANY)
    banded = jax.ShapeDtypeStruct((group_size, band_rows, col_count), jnp.float32)
    order = [bands // 2] + [s for s in range(1, bands) if s != bands // 2] + [0]
    slots = {}
    warped_slots = {}
    for step in order:
        warped_slots[step], flagged = pl.pallas_call(
            functools.partial(_slot_kernel, step),
            out_shape=(banded, banded),
            in_specs=[smem, smem, smem, smem, smem, anywhere, anywhere],
            out_specs=(vmem, vmem),
            scratch_shapes=[
                pltpu.VMEM((group_size, window, lanes), jnp.float32),
                pltpu.VMEM((group_size, band_rows, col_count), jnp.int32),
                pltpu.SemaphoreType.DMA((5,)),
            ],
        )(row_shift, col_shift, row_weight, col_weight, me, padded, bad_pixels)
        if step:
            pairs = [(i, (i + step) % bands) for i in range(bands)]
            slots[step] = lax.ppermute(flagged, "exp", pairs)
        else:
            slots[step] = flagged
    stacked = jnp.stack([warped_slots[s] for s in range(bands)])
    natural = jnp.take(stacked, lax.rem(jnp.arange(bands) - me[0] + bands, bands), axis=0)
    warped = natural.transpose(1, 0, 2, 3).reshape(group_size, row_count, col_count)
    return warped, jnp.concatenate([slots[s] for s in range(bands)], axis=0)


def body(exposures, bad_pixels, offsets, warp_index, blur_index):
    group_size, row_count, col_count = exposures.shape
    padded = extended(exposures, 1, 2, HALO)
    by_slot = warp_by_slot(padded, bad_pixels, offsets, warp_index)
    groups = lax.axis_size("exp")
    if by_slot is not None:
        warped, stack = by_slot
    else:
        warped, flagged = warp_and_flag(padded, bad_pixels, offsets, warp_index)
        arrived = [flagged[0]]
        for step in range(1, groups):
            pairs = [(i, (i + step) % groups) for i in range(groups)]
            arrived.append(lax.ppermute(flagged[step], "exp", pairs))
        stack = jnp.concatenate(arrived, axis=0)
    band = stack_median(stack)
    groups = lax.axis_size("exp")
    sides = lax.axis_size("col")
    band_rows = band.shape[0]
    full = lax.all_to_all(
        jnp.tile(band, (groups * sides, 1)), ("exp", "col"), split_axis=0, concat_axis=0, tiled=True
    )
    full = full.reshape(groups, sides, band_rows, col_count)
    full = full.transpose(0, 2, 1, 3).reshape(row_count, sides * col_count)
    start = lax.axis_index("col") * col_count
    median_sky = lax.dynamic_slice_in_dim(full, start, col_count, axis=1)
    wide = jnp.pad(full, ((0, 0), (PSF_RADIUS, PSF_RADIUS)))
    wide = lax.dynamic_slice_in_dim(wide, start, col_count + 2 * PSF_RADIUS, axis=1)
    bordered = _row_halo(wide, 0, PSF_RADIUS)
    blur = blur_table()
    taps = 2 * PSF_RADIUS + 1
    blurred_rows = jnp.zeros((NPSF, row_count, col_count + 2 * PSF_RADIUS), jnp.float32)
    for tap_no in range(taps):
        blurred_rows = (
            blurred_rows
            + blur[:, tap_no, None, None] * bordered[None, tap_no : tap_no + row_count, :]
        )
    smoothed = jnp.zeros((NPSF, row_count, col_count), jnp.float32)
    for tap_no in range(taps):
        smoothed = (
            smoothed + blur[:, tap_no, None, None] * blurred_rows[:, :, tap_no : tap_no + col_count]
        )
    chooser = (blur_index[:, None] == lax.broadcasted_iota(jnp.int32, (1, NPSF), 1)).astype(
        jnp.float32
    )
    sky_model = jnp.zeros((group_size, row_count, col_count), jnp.float32)
    for kernel_no in range(NPSF):
        sky_model = sky_model + chooser[:, kernel_no, None, None] * smoothed[kernel_no][None]
    residual = jnp.where(bad_pixels == 1, 0.0, warped - sky_model)
    return (residual, median_sky)


def solution(mesh):
    return jax.shard_map(
        body,
        mesh=mesh,
        in_specs=(
            P("exp", "row", "col"),
            P("exp", "row", "col"),
            P("exp", None),
            P("exp", None),
            P("exp"),
        ),
        out_specs=(P("exp", "row", "col"), P("row", "col")),
        check_vma=False,
    )
```
